32 devices in a mesh: grp: 4 (over y, x), patch: 8 (over z, core).
Axes of the slice: x: 2, y: 2, z: 4, core: 2. Of those that a mesh axis runs over, the one named last changes fastest.
Arguments:
- state: float32 [9, 60, 65536], P(None, 'grp', 'patch'), may hold values from -6 to 6
- courant_x: float32 [60, 65536], P('grp', 'patch'), may hold values from -0.45 to 0.45
- courant_y: float32 [60, 65536], P('grp', 'patch'), may hold values from -0.45 to 0.45
- surface: bfloat16 [16, 65536], P('grp', 'patch'), may hold values from -6 to 6
- w_in: bfloat16 [556, 256], replicated, may hold values from -0.25 to 0.25
- b_hidden: float32 [4, 256], replicated, may hold values from -3 to 3
- w_mid: bfloat16 [3, 256, 256], replicated, may hold values from -0.375 to 0.375
- w_out: bfloat16 [256, 540], replicated, may hold values from -0.375 to 0.375
- owner_map: int32 [512, 1], replicated, may hold values from 0 to 7; in each aligned block of 16 rows (0 to 15, 16 to 31, ...) at most 4 rows name the same one
- neighbours: int32 [8, 4], replicated, may hold values from 0 to 7, as said below
Outputs:
- new_state: float32 [9, 60, 65536], P(None, 'grp', 'patch')
- owner_heating: float32 [128, 1024], P('grp', 'patch')
The draws below stay inside these ranges and needn't reach their ends.
Inputs may be any that keep to these rules, and one draw needn't show every extreme that they name: owner_map[b, 0] is the owner of block b (row b % 64 of patch b // 64); within each aligned run of 16 blocks no owner is named more than 4 times, and in some run one owner exactly 4 times. The patches tile a periodic arrangement of 2 by 4: neighbours[p, 0] and neighbours[p, 1] precede and follow p along the first direction, neighbours[p, 2] and neighbours[p, 3] along the second; neighbours[neighbours[p, 0], 1] = p, neighbours[neighbours[p, 2], 3] = p, and neighbours[neighbours[p, 0], 2] = neighbours[neighbours[p, 2], 0].
All inputs are finite; a program needn't handle non-finite values.
Results may differ from the reference program's by a relative error of at most 0.0059.
The reference program's roundings to bfloat16 on the way (of `features`, `hidden` and `tendency`) count: a program that leaves them out, or rounds other values in their place, can miss the bound.
Values may be sent and summed in bfloat16 or wider, within the bound.
No kernel may reach another device: no remote copies, remote signals or barrier semaphores. Data moves between devices by JAX's collectives and lax.ppermute only.
A program may use at most 640 MiB of HBM per device.

```python
import math
import jax
import jax.numpy as jnp
import numpy as np
from jax import lax

VARS = 9
LEV = 60
SURF = 16
HID = 256
MIDS = 3
SUBSTEPS = 3
PY = 128
PX = 64
FEAT = 556
OUTF = 540
QB = 16
CAPQ = 4
COLS = 65536
BLOCKS = 512
RSLOT = 128
PATCH_ROWS = 2
PATCH_COLS = 4
N_GRP = 4
N_PATCH = 8


def draw_state(key, part):
    value_key = jax.random.fold_in(key, 11)
    values = jax.random.normal(value_key, (VARS, LEV, COLS), jnp.float32)
    return jnp.clip(values, -6.0, 6.0).astype(jnp.float32)


def draw_neighbours(key, part):
    total = PATCH_ROWS * PATCH_COLS
    placed = jax.random.permutation(key, total).astype(jnp.int32)
    patch_at = jnp.argsort(placed, stable=True).astype(jnp.int32)
    row_pos = placed // PATCH_COLS
    col_pos = placed % PATCH_COLS
    north_id = patch_at[(row_pos - 1) % PATCH_ROWS * PATCH_COLS + col_pos]
    south_id = patch_at[(row_pos + 1) % PATCH_ROWS * PATCH_COLS + col_pos]
    west_id = patch_at[row_pos * PATCH_COLS + (col_pos - 1) % PATCH_COLS]
    east_id = patch_at[row_pos * PATCH_COLS + (col_pos + 1) % PATCH_COLS]
    return jnp.stack([north_id, south_id, west_id, east_id], axis=1).astype(jnp.int32)


def steps_of(rng, dims, shards, least, high):
    gain, own = 1.0, jax.random.fold_in(rng, 6)
    for position, blocks in shards:
        draws = jnp.exp(jax.random.uniform(jax.random.fold_in(own, position), (blocks,), jnp.float32, least / len(shards), high / len(shards)))
        gain = gain * jnp.repeat(draws, dims[position] // blocks).reshape([-1 if axis == position else 1 for axis in range(len(dims))])
    return gain


def deal_out(own_key, own, number, rows, number_of, top, reach, skew):
    order = jax.random.permutation(own_key, number_of)
    crowded, usual = portions_of(number_of, rows * top, reach, skew, True), portions_of(number_of, rows * top, reach, skew, False)
    places = jnp.arange(number_of)

    def named(tallies, turn):
        used = int((tallies > 0).sum())
        fixed = max(1, used // 4)
        shifted = fixed + (places - fixed + turn * (used - fixed)) % max(1, number_of - fixed)
        return jnp.zeros((number_of,), jnp.int32).at[order[jnp.where(places < fixed, places, shifted)]].set(jnp.asarray(tallies, jnp.int32))

    tallies = jnp.where(number % 4 == 0, named(crowded, number // 4), named(usual, number - number // 4 - 1))
    mixed = jax.random.permutation(jax.random.fold_in(own, 3), number_of)
    giver, sink = mixed[0:number_of // 2 * 2:2], mixed[1:number_of // 2 * 2:2]
    slack = jnp.minimum(tallies[giver] - 1, reach - tallies[sink]) // 2
    slack = jnp.where((giver == order[0]) | (sink == order[0]) | (tallies[sink] == 0), 0, jnp.maximum(slack, 0))
    shifted = jax.random.randint(jax.random.fold_in(own, 4), (number_of // 2,), 0, 1 << 20) % (slack + 1)
    tallies = tallies.at[giver].add(-shifted).at[sink].add(shifted)
    items = jnp.searchsorted(jnp.cumsum(tallies), jnp.arange(rows * top), side="right").astype(jnp.int32)
    grid = items.reshape(top, rows).T
    grid = grid[jax.random.permutation(jax.random.fold_in(own, 1), rows)]
    turn = jax.random.randint(jax.random.fold_in(own, 2), (rows, 1), 0, top)
    return jnp.take_along_axis(grid, (jnp.arange(top)[None, :] + turn) % top, axis=1)


def portions_of(count, total, limit, slope, full):
    weights = [(1 << 20) // math.isqrt(standing ** slope) + 1 for standing in range(1, count + 1)]
    largest = limit if full else min(limit, max(-(-total // count), total * weights[0] // sum(weights)))
    least = 1 if total - largest >= count - 1 else 0
    holding, spare = [largest] + [least] * (count - 1), total - largest - least * (count - 1)
    while spare > 0:
        movable = [i for i in range(1, count) if holding[i] < largest] or [i for i in range(1, count) if holding[i] < limit]
        whole, left = sum([weights[i] for i in movable]), spare
        for i in movable:
            more = min(limit - holding[i], max(1, left * weights[i] // whole), spare)
            holding[i] = holding[i] + more
            spare = spare - more
    return np.array(holding)


def centred(stream_key, shape, scale, limit, pieces=(), kind=jnp.bfloat16):
    factor_of = steps_of(stream_key, shape, pieces, -0.22, 0.18) if pieces else 1.0
    array = jax.random.normal(stream_key, shape, jnp.float32) * scale * factor_of
    return jnp.minimum(jnp.maximum(array, -limit), limit).astype(kind)


def setup_inputs(seed: int = 0) -> dict:
    key_of = jax.random.split(jax.random.key(seed), 11)
    state = draw_state(jax.random.fold_in(key_of[10], 71), 0)
    courant_x = jnp.clip(jax.random.uniform(key_of[1], (LEV, COLS), jnp.float32, -0.45, 0.45) * steps_of(key_of[1], (LEV, COLS), ((0, 4), (1, 8)), -0.4, 0.0), -0.45, 0.45)
    courant_y = jnp.clip(jax.random.uniform(key_of[2], (LEV, COLS), jnp.float32, -0.45, 0.45) * steps_of(key_of[2], (LEV, COLS), ((0, 4), (1, 8)), -0.4, 0.0), -0.45, 0.45)
    surface = centred(key_of[3], (SURF, COLS), 1.0, 6.0, ((0, 4), (1, 8)))
    w_in = centred(key_of[4], (FEAT, HID), FEAT ** -0.5, 0.25)
    b_hidden = centred(key_of[5], (MIDS + 1, HID), 0.5, 3.0, (), jnp.float32)
    w_mid = centred(key_of[6], (MIDS, HID, HID), HID ** -0.5, 0.375)
    w_out = centred(key_of[7], (HID, OUTF), HID ** -0.5, 0.375)
    owner_map_keys = jax.random.split(jax.random.fold_in(key_of[8], 1), BLOCKS // QB)
    owner_map_turns = jax.random.permutation(jax.random.fold_in(key_of[8], 3), BLOCKS // QB)
    owner_map = jax.vmap(lambda own, number: deal_out(jax.random.fold_in(key_of[8], 2), own, number, QB, N_PATCH, 1, CAPQ, 2))(owner_map_keys, owner_map_turns).reshape((BLOCKS, 1))
    neighbours = draw_neighbours(jax.random.fold_in(key_of[10], 71), 0)
    return dict(state=state, courant_x=courant_x, courant_y=courant_y, surface=surface, w_in=w_in, b_hidden=b_hidden, w_mid=w_mid, w_out=w_out, owner_map=owner_map, neighbours=neighbours)


KAPPA = 0.24
PHYS_DT = 0.05
HEAT_WEIGHT = 0.125


def advance_grid(tracer, along_x, along_y, neighbours):
    northern = jnp.concatenate([tracer[:, neighbours[:, 0], -1:, :], tracer[:, :, :-1, :]], axis=2)
    southern = jnp.concatenate([tracer[:, :, 1:, :], tracer[:, neighbours[:, 1], :1, :]], axis=2)
    western = jnp.concatenate([tracer[:, neighbours[:, 2], :, -1:], tracer[:, :, :, :-1]], axis=3)
    eastern = jnp.concatenate([tracer[:, :, :, 1:], tracer[:, neighbours[:, 3], :, :1]], axis=3)
    return tracer - 0.5 * along_x * (southern - northern) - 0.5 * along_y * (eastern - western) + KAPPA * (northern + southern + western + eastern - 4.0 * tracer)


def activate(pre_act):
    return lax.optimization_barrier(jax.nn.silu(pre_act).astype(jnp.bfloat16)).astype(jnp.float32)


def reference(state, courant_x, courant_y, surface, w_in, b_hidden, w_mid, w_out, owner_map, neighbours):
    grid_x = courant_x.reshape(LEV, N_PATCH, PX, PY)
    grid_y = courant_y.reshape(LEV, N_PATCH, PX, PY)

    def dynamics(tracer):
        tracer = tracer.reshape(LEV, N_PATCH, PX, PY)
        for substep_index in range(SUBSTEPS):
            tracer = advance_grid(tracer, grid_x, grid_y, neighbours)
        return tracer.reshape(LEV, COLS)

    advected = lax.map(dynamics, state)
    weights_in = w_in.astype(jnp.float32)
    weights_mid = w_mid.astype(jnp.float32)
    weights_out = w_out.astype(jnp.float32)
    highest = lax.Precision.HIGHEST

    def physics(patch_index):
        start = patch_index * PX * PY
        columns = lax.dynamic_slice_in_dim(state, start, PX * PY, 2).reshape(VARS * LEV, PX * PY)
        surf_cols = lax.dynamic_slice_in_dim(surface, start, PX * PY, 1).astype(jnp.float32)
        features = jnp.concatenate([columns, surf_cols], axis=0).astype(jnp.bfloat16)
        features = lax.optimization_barrier(features).astype(jnp.float32)
        hidden = activate(jnp.dot(features.T, weights_in, precision=highest) + b_hidden[0])
        for layer_index in range(MIDS):
            hidden = activate(jnp.dot(hidden, weights_mid[layer_index], precision=highest) + b_hidden[layer_index + 1])
        tendency = jnp.dot(hidden, weights_out, precision=highest).astype(jnp.bfloat16)
        return tendency.T

    tendencies = lax.map(physics, jnp.arange(N_PATCH, dtype=jnp.int32))
    tendency_grid = tendencies.reshape(N_PATCH, VARS, LEV, PX * PY).transpose(1, 2, 0, 3).reshape(VARS, LEV, COLS)
    new_state = advected + PHYS_DT * tendency_grid.astype(jnp.float32)
    heating = HEAT_WEIGHT * jnp.sum(tendencies[:, :LEV].astype(jnp.float32), axis=1)
    heating = heating.reshape(N_PATCH, N_GRP, QB, PY)
    owners = owner_map.reshape(N_PATCH, N_GRP, QB).astype(jnp.int32)
    matches = (owners[..., None] == jnp.arange(N_PATCH, dtype=jnp.int32)).astype(jnp.int32)
    before = jnp.cumsum(matches, axis=2) - matches
    slot_rank = jnp.sum(before * matches, axis=3).astype(jnp.int32)
    patch_ids = jnp.arange(N_PATCH, dtype=jnp.int32)[:, None, None]
    group_ids = jnp.arange(N_GRP, dtype=jnp.int32)[None, :, None]
    slot_rows = ((group_ids * N_PATCH + patch_ids) * CAPQ + slot_rank).astype(jnp.int32)
    slot_table = jnp.zeros((RSLOT, N_PATCH, PY), jnp.float32).at[slot_rows, owners].set(heating)
    return new_state, slot_table.reshape(RSLOT, N_PATCH * PY)
```

```python
import jax
import jax.numpy as jnp
from jax import lax
from jax.sharding import PartitionSpec as P

VARS = 9
LEV = 60
SURF = 16
SUBSTEPS = 3
PY = 128
PX = 64


KAPPA = 0.24
PHYS_DT = 0.05
HEAT_WEIGHT = 0.125


def strips(tracer, depth_cells):
    row_strips = jnp.stack([tracer[..., :depth_cells, :], tracer[..., -depth_cells:, :]])
    col_strips = jnp.stack(
        [
            jnp.swapaxes(tracer[..., :depth_cells], -1, -2),
            jnp.swapaxes(tracer[..., -depth_cells:], -1, -2),
        ]
    )
    return (row_strips[None], col_strips[None])


def exchange(row_edges, col_edges, patches):
    row_flat = row_edges.astype(jnp.bfloat16).reshape(-1)
    col_flat = col_edges.astype(jnp.bfloat16).reshape(-1)
    payload = jnp.concatenate([row_flat, col_flat])
    sent = jnp.broadcast_to(payload[None], (patches,) + payload.shape)
    got = lax.all_to_all(sent, "patch", split_axis=0, concat_axis=0, tiled=True)
    row_all = got[:, : row_flat.size].reshape((patches,) + row_edges.shape[1:])
    col_all = got[:, row_flat.size :].reshape((patches,) + col_edges.shape[1:])
    return row_all.astype(row_edges.dtype), col_all.astype(col_edges.dtype)


def take_patch(gathered, index):
    return jnp.take(gathered, index, axis=0)


def assemble(tracer, row_all, col_all, neighbours, beside_all, depth_cells):
    north_id, south_id, west_id, east_id = (
        beside_all[0],
        beside_all[1],
        beside_all[2],
        beside_all[3],
    )
    top_band = take_patch(row_all, north_id)[1]
    bottom_band = take_patch(row_all, south_id)[0]
    left_band = jnp.swapaxes(take_patch(col_all, west_id)[1], -1, -2)
    right_band = jnp.swapaxes(take_patch(col_all, east_id)[0], -1, -2)
    corner_nw = take_patch(row_all, neighbours[north_id, 2])[1][..., -depth_cells:]
    corner_ne = take_patch(row_all, neighbours[north_id, 3])[1][..., :depth_cells]
    corner_sw = take_patch(row_all, neighbours[south_id, 2])[0][..., -depth_cells:]
    corner_se = take_patch(row_all, neighbours[south_id, 3])[0][..., :depth_cells]
    upper_band = jnp.concatenate([corner_nw, top_band, corner_ne], axis=-1)
    middle = jnp.concatenate([left_band, tracer, right_band], axis=-1)
    lower_band = jnp.concatenate([corner_sw, bottom_band, corner_se], axis=-1)
    return jnp.concatenate([upper_band, middle, lower_band], axis=-2)


def advance(padded, along_x, along_y):
    centre = padded[..., 1:-1, 1:-1]
    northern = padded[..., :-2, 1:-1]
    southern = padded[..., 2:, 1:-1]
    western = padded[..., 1:-1, :-2]
    eastern = padded[..., 1:-1, 2:]
    return (
        centre
        - 0.5 * along_x * (southern - northern)
        - 0.5 * along_y * (eastern - western)
        + KAPPA * (northern + southern + western + eastern - 4.0 * centre)
    )


def activate(pre_act):
    return jax.nn.silu(pre_act).astype(jnp.bfloat16)


def hidden_layers(hidden, b_hidden, w_mid):
    for layer_index in range(w_mid.shape[0]):
        pre_act = (
            jnp.einsum(
                "...h,hj->...j", hidden, w_mid[layer_index], preferred_element_type=jnp.float32
            )
            + b_hidden[layer_index + 1]
        )
        hidden = activate(pre_act)
    return hidden


def on_device(
    state, courant_x, courant_y, surface, w_in, b_hidden, w_mid, w_out, owner_map, neighbours
):
    groups = lax.axis_size("grp")
    patches = lax.axis_size("patch")
    group_here = lax.axis_index("grp")
    patch_here = lax.axis_index("patch")
    level_share = LEV // groups
    surf_share = SURF // groups
    feat_share = VARS * level_share + surf_share
    quarter_rows = PX // groups
    capacity = max(2, 2 * quarter_rows // patches)
    slot_count = patches * capacity
    tracer = state.reshape(VARS, level_share, PX, PY)
    courants = jnp.concatenate(
        [courant_x.reshape(1, level_share, PX, PY), courant_y.reshape(1, level_share, PX, PY)],
        axis=0,
    )
    beside_all = jnp.take(neighbours, patch_here, axis=0)
    features = jnp.concatenate(
        [
            tracer.astype(jnp.bfloat16).reshape(VARS * level_share, PX, PY),
            surface.reshape(surf_share, PX, PY),
        ],
        axis=0,
    )
    by_quarter = features.reshape(feat_share, groups, quarter_rows, PY).transpose(1, 2, 0, 3)
    owners_all = owner_map.reshape(patches, groups, quarter_rows)
    owners_here = jnp.take(owners_all, patch_here, axis=0)
    matches = (owners_here[..., None] == jnp.arange(patches, dtype=jnp.int32)).astype(jnp.int32)
    slot_rank = jnp.sum((jnp.cumsum(matches, axis=1) - matches) * matches, axis=2)
    slot_index = owners_here * capacity + slot_rank
    selector = (
        slot_index[:, None, :] == jnp.arange(slot_count, dtype=jnp.int32)[None, :, None]
    ).astype(jnp.bfloat16)
    selector_here = jnp.take(selector, group_here, axis=0)
    state_part = (
        w_in[: VARS * LEV]
        .reshape(VARS, groups, level_share, -1)
        .transpose(1, 0, 2, 3)
        .reshape(groups, VARS * level_share, -1)
    )
    w_local = jnp.concatenate(
        [state_part, w_in[VARS * LEV :].reshape(groups, surf_share, -1)], axis=1
    )
    w_split = w_out.reshape(-1, VARS, groups, level_share)
    regrouped = lax.all_to_all(by_quarter, "grp", split_axis=0, concat_axis=0, tiled=True)
    pre_act = (
        jnp.einsum("gbfc,gfh->bch", regrouped, w_local, preferred_element_type=jnp.float32)
        + b_hidden[0]
    )
    hidden = hidden_layers(activate(pre_act), b_hidden, w_mid)
    tendency = jnp.einsum(
        "bch,hvgl->bvglc", hidden, w_split, preferred_element_type=jnp.float32
    ).astype(jnp.bfloat16)
    heating = HEAT_WEIGHT * jnp.sum(tendency[:, 0].astype(jnp.float32), axis=(1, 2))
    packed = jnp.dot(
        selector_here.astype(jnp.float32), heating, precision=lax.Precision.HIGHEST
    ).reshape(patches, capacity, PY)
    owner_heating = lax.all_to_all(
        packed, "patch", split_axis=0, concat_axis=0, tiled=True
    ).reshape(slot_count, PY)
    arrived = lax.all_to_all(tendency, "grp", split_axis=2, concat_axis=0, tiled=True)
    tendency_here = arrived.reshape(PX, VARS, level_share, PY).transpose(1, 2, 0, 3)
    advected = tracer
    for section_index in range(SUBSTEPS):
        row_edges, col_edges = strips(advected, 1)
        row_edges, col_edges = exchange(row_edges, col_edges, patches)
        padded = assemble(advected, row_edges, col_edges, neighbours, beside_all, 1)
        advected = advance(padded, courants[0:1], courants[1:2])
    new_state = advected + PHYS_DT * tendency_here.astype(jnp.float32)
    return (new_state.reshape(VARS, level_share, PX * PY), owner_heating)


def solution(mesh):
    placed = (
        P(None, "grp", "patch"),
        P("grp", "patch"),
        P("grp", "patch"),
        P("grp", "patch"),
        P(),
        P(),
        P(),
        P(),
        P(),
        P(),
    )
    return jax.shard_map(
        on_device,
        mesh=mesh,
        in_specs=placed,
        out_specs=(P(None, "grp", "patch"), P("grp", "patch")),
        check_vma=False,
    )
```

```python
import functools

import jax
import jax.numpy as jnp
from jax import lax
from jax.experimental import pallas as pl
from jax.experimental.pallas import tpu as pltpu
from jax.sharding import PartitionSpec as P

VARS = 9
LEV = 60
SURF = 16
SUBSTEPS = 3
PY = 128
PX = 64


KAPPA = 0.24
PHYS_DT = 0.05
HEAT_WEIGHT = 0.125


def stencil_kernel(*refs, with_tend):
    if with_tend:
        st_ref, cx_ref, cy_ref, halo_ref, tend_ref, out_ref, edge_ref = refs
    else:
        st_ref, cx_ref, cy_ref, halo_ref, out_ref, edge_ref = refs
    rows = st_ref.shape[2] // PY
    halo = halo_ref[0].astype(jnp.float32)
    north = halo[:, 0:PY]
    south = halo[:, PY : 2 * PY]
    sides = halo[:, 2 * PY : 3 * PY]
    lane = lax.broadcasted_iota(jnp.int32, north.shape, 1)
    cols = jnp.zeros_like(north)
    for x in range(rows):
        here = slice(x * PY, (x + 1) * PY)
        cur = st_ref[0, :, here]
        up = north if x == 0 else st_ref[0, :, (x - 1) * PY : x * PY]
        down = south if x == rows - 1 else st_ref[0, :, (x + 1) * PY : (x + 2) * PY]
        west = jnp.where(lane == 0, pltpu.roll(sides, (PY - x) % PY, 1), pltpu.roll(cur, 1, 1))
        east = jnp.where(
            lane == PY - 1, pltpu.roll(sides, (PY - 1 - rows - x) % PY, 1), pltpu.roll(cur, PY - 1, 1)
        )
        along_x = cx_ref[:, here]
        along_y = cy_ref[:, here]
        val = (
            cur
            - 0.5 * along_x * (down - up)
            - 0.5 * along_y * (east - west)
            + KAPPA * (up + down + west + east - 4.0 * cur)
        )
        if with_tend:
            val = val + PHYS_DT * tend_ref[x, 0].astype(jnp.float32)
        out_ref[0, :, here] = val
        if x == 0:
            edge_ref[0, :, 0:PY] = val
        if x == rows - 1:
            edge_ref[0, :, PY : 2 * PY] = val
        cols = jnp.where(lane == x, pltpu.roll(val, x % PY, 1), cols)
        cols = jnp.where(lane == rows + x, pltpu.roll(val, (rows + x - PY + 1) % PY, 1), cols)
    edge_ref[0, :, 2 * PY : 3 * PY] = cols


def stencil(tracer, along_x, along_y, halo, tend):
    n_vars, levels, width = tracer.shape
    with_tend = tend is not None
    in_specs = [
        pl.BlockSpec((1, levels, width), lambda v: (v, 0, 0)),
        pl.BlockSpec((levels, width), lambda v: (0, 0)),
        pl.BlockSpec((levels, width), lambda v: (0, 0)),
        pl.BlockSpec((1, levels, 3 * PY), lambda v: (v, 0, 0)),
    ]
    args = [tracer, along_x, along_y, halo]
    if with_tend:
        in_specs.append(pl.BlockSpec((tend.shape[0], 1, levels, PY), lambda v: (0, v, 0, 0)))
        args.append(tend)
    return pl.pallas_call(
        functools.partial(stencil_kernel, with_tend=with_tend),
        grid=(n_vars,),
        in_specs=in_specs,
        out_specs=[
            pl.BlockSpec((1, levels, width), lambda v: (v, 0, 0)),
            pl.BlockSpec((1, levels, 3 * PY), lambda v: (v, 0, 0)),
        ],
        out_shape=[
            jax.ShapeDtypeStruct(tracer.shape, jnp.float32),
            jax.ShapeDtypeStruct((n_vars, levels, 3 * PY), jnp.float32),
        ],
        cost_estimate=pl.CostEstimate(
            flops=20 * tracer.size, transcendentals=0, bytes_accessed=4 * (2 * tracer.size + 2 * along_x.size)
        ),
    )(*args)


def first_edges(tracer):
    width = tracer.shape[-1]
    return jnp.concatenate(
        [tracer[..., 0:PY], tracer[..., width - PY :], tracer[..., 0::PY], tracer[..., PY - 1 :: PY]],
        axis=-1,
    )


def exchange_halo(edges, beside_all, patches):
    payload = edges.astype(jnp.bfloat16)
    sent = jnp.broadcast_to(payload[None], (patches,) + payload.shape)
    got = lax.all_to_all(sent, "patch", split_axis=0, concat_axis=0, tiled=True)
    rows = PX
    north = jnp.take(got, beside_all[0], axis=0)[..., PY : 2 * PY]
    south = jnp.take(got, beside_all[1], axis=0)[..., 0:PY]
    west = jnp.take(got, beside_all[2], axis=0)[..., 2 * PY + rows : 3 * PY]
    east = jnp.take(got, beside_all[3], axis=0)[..., 2 * PY : 2 * PY + rows]
    return jnp.concatenate([north, south, west, east], axis=-1)


def activate(pre_act):
    return jax.nn.silu(pre_act).astype(jnp.bfloat16)


def hidden_layers(hidden, b_hidden, w_mid):
    for layer_index in range(w_mid.shape[0]):
        pre_act = (
            jnp.einsum(
                "...h,hj->...j", hidden, w_mid[layer_index], preferred_element_type=jnp.float32
            )
            + b_hidden[layer_index + 1]
        )
        hidden = activate(pre_act)
    return hidden


def on_device(
    state, courant_x, courant_y, surface, w_in, b_hidden, w_mid, w_out, owner_map, neighbours
):
    groups = lax.axis_size("grp")
    patches = lax.axis_size("patch")
    group_here = lax.axis_index("grp")
    patch_here = lax.axis_index("patch")
    level_share = LEV // groups
    surf_share = SURF // groups
    feat_share = VARS * level_share + surf_share
    quarter_rows = PX // groups
    capacity = max(2, 2 * quarter_rows // patches)
    slot_count = patches * capacity
    tracer = state.reshape(VARS, level_share, PX, PY)
    beside_all = jnp.take(neighbours, patch_here, axis=0)
    features = jnp.concatenate(
        [
            tracer.astype(jnp.bfloat16).reshape(VARS * level_share, PX, PY),
            surface.reshape(surf_share, PX, PY),
        ],
        axis=0,
    )
    by_quarter = features.reshape(feat_share, groups, quarter_rows, PY).transpose(1, 2, 0, 3)
    owners_all = owner_map.reshape(patches, groups, quarter_rows)
    owners_here = jnp.take(owners_all, patch_here, axis=0)
    matches = (owners_here[..., None] == jnp.arange(patches, dtype=jnp.int32)).astype(jnp.int32)
    slot_rank = jnp.sum((jnp.cumsum(matches, axis=1) - matches) * matches, axis=2)
    slot_index = owners_here * capacity + slot_rank
    selector = (
        slot_index[:, None, :] == jnp.arange(slot_count, dtype=jnp.int32)[None, :, None]
    ).astype(jnp.bfloat16)
    selector_here = jnp.take(selector, group_here, axis=0)
    state_part = (
        w_in[: VARS * LEV]
        .reshape(VARS, groups, level_share, -1)
        .transpose(1, 0, 2, 3)
        .reshape(groups, VARS * level_share, -1)
    )
    w_local = jnp.concatenate(
        [state_part, w_in[VARS * LEV :].reshape(groups, surf_share, -1)], axis=1
    )
    w_split = w_out.reshape(-1, VARS, groups, level_share)
    regrouped = lax.all_to_all(by_quarter, "grp", split_axis=0, concat_axis=0, tiled=True)
    pre_act = (
        jnp.einsum("gbfc,gfh->bch", regrouped, w_local, preferred_element_type=jnp.float32)
        + b_hidden[0]
    )
    hidden = hidden_layers(activate(pre_act), b_hidden, w_mid)
    tendency = jnp.einsum(
        "bch,hvgl->bvglc", hidden, w_split, preferred_element_type=jnp.float32
    ).astype(jnp.bfloat16)
    heating = HEAT_WEIGHT * jnp.sum(tendency[:, 0].astype(jnp.float32), axis=(1, 2))
    packed = jnp.dot(
        selector_here.astype(jnp.float32), heating, precision=lax.Precision.HIGHEST
    ).reshape(patches, capacity, PY)
    owner_heating = lax.all_to_all(
        packed, "patch", split_axis=0, concat_axis=0, tiled=True
    ).reshape(slot_count, PY)
    arrived = lax.all_to_all(tendency, "grp", split_axis=2, concat_axis=0, tiled=True)
    tendency_here = arrived.reshape(PX, VARS, level_share, PY)
    advected = state
    edges = first_edges(state)
    for section_index in range(SUBSTEPS):
        halo = exchange_halo(edges, beside_all, patches)
        last = section_index == SUBSTEPS - 1
        advected, edges = stencil(
            advected, courant_x, courant_y, halo, tendency_here if last else None
        )
    new_state = advected
    return (new_state, owner_heating)


def solution(mesh):
    placed = (
        P(None, "grp", "patch"),
        P("grp", "patch"),
        P("grp", "patch"),
        P("grp", "patch"),
        P(),
        P(),
        P(),
        P(),
        P(),
        P(),
    )
    return jax.shard_map(
        on_device,
        mesh=mesh,
        in_specs=placed,
        out_specs=(P(None, "grp", "patch"), P("grp", "patch")),
        check_vma=False,
    )
```

```python
import functools

import jax
import jax.numpy as jnp
from jax import lax
from jax.experimental import pallas as pl
from jax.experimental.pallas import tpu as pltpu
from jax.sharding import PartitionSpec as P

VARS = 9
LEV = 60
SURF = 16
SUBSTEPS = 3
PY = 128
PX = 64


KAPPA = 0.24
PHYS_DT = 0.05
HEAT_WEIGHT = 0.125


def stencil_kernel(*refs, with_tend):
    if with_tend:
        st_ref, cx_ref, cy_ref, rows_ref, sides_ref, tend_ref, out_ref = refs
    else:
        st_ref, cx_ref, cy_ref, rows_ref, sides_ref, out_ref = refs
    rows = st_ref.shape[2] // PY
    north = rows_ref[0, :, 0:PY]
    south = rows_ref[0, :, PY : 2 * PY]
    lane = lax.broadcasted_iota(jnp.int32, north.shape, 1)
    for x in range(rows):
        here = slice(x * PY, (x + 1) * PY)
        cur = st_ref[0, :, here]
        up = north if x == 0 else st_ref[0, :, (x - 1) * PY : x * PY]
        down = south if x == rows - 1 else st_ref[0, :, (x + 1) * PY : (x + 2) * PY]
        side = sides_ref[0, :, here]
        west = jnp.where(lane == 0, side, pltpu.roll(cur, 1, 1))
        east = jnp.where(lane == PY - 1, side, pltpu.roll(cur, PY - 1, 1))
        along_x = cx_ref[:, here]
        along_y = cy_ref[:, here]
        val = (
            cur
            - 0.5 * along_x * (down - up)
            - 0.5 * along_y * (east - west)
            + KAPPA * (up + down + west + east - 4.0 * cur)
        )
        if with_tend:
            val = val + PHYS_DT * tend_ref[x, 0].astype(jnp.float32)
        out_ref[0, :, here] = val


def stencil(tracer, along_x, along_y, halo_rows, halo_sides, tend):
    n_vars, levels, width = tracer.shape
    with_tend = tend is not None
    in_specs = [
        pl.BlockSpec((1, levels, width), lambda v: (v, 0, 0)),
        pl.BlockSpec((levels, width), lambda v: (0, 0)),
        pl.BlockSpec((levels, width), lambda v: (0, 0)),
        pl.BlockSpec((1, levels, 2 * PY), lambda v: (v, 0, 0)),
        pl.BlockSpec((1, levels, width), lambda v: (v, 0, 0)),
    ]
    args = [tracer, along_x, along_y, halo_rows, halo_sides]
    if with_tend:
        in_specs.append(pl.BlockSpec((tend.shape[0], 1, levels, PY), lambda v: (0, v, 0, 0)))
        args.append(tend)
    return pl.pallas_call(
        functools.partial(stencil_kernel, with_tend=with_tend),
        grid=(n_vars,),
        in_specs=in_specs,
        out_specs=pl.BlockSpec((1, levels, width), lambda v: (v, 0, 0)),
        out_shape=jax.ShapeDtypeStruct(tracer.shape, jnp.float32),
        cost_estimate=pl.CostEstimate(
            flops=20 * tracer.size, transcendentals=0, bytes_accessed=4 * (3 * tracer.size + 2 * along_x.size)
        ),
    )(*args)


def edges_of(tracer):
    width = tracer.shape[-1]
    return jnp.concatenate(
        [tracer[..., 0:PY], tracer[..., width - PY :], tracer[..., 0::PY], tracer[..., PY - 1 :: PY]],
        axis=-1,
    ).astype(jnp.bfloat16)


def exchange_halo(tracer, beside_all, patches):
    payload = edges_of(tracer)
    sent = jnp.broadcast_to(payload[None], (patches,) + payload.shape)
    got = lax.all_to_all(sent, "patch", split_axis=0, concat_axis=0, tiled=True).astype(jnp.float32)
    rows = PX
    north = jnp.take(got, beside_all[0], axis=0)[..., PY : 2 * PY]
    south = jnp.take(got, beside_all[1], axis=0)[..., 0:PY]
    west = jnp.take(got, beside_all[2], axis=0)[..., 2 * PY + rows : 2 * PY + 2 * rows]
    east = jnp.take(got, beside_all[3], axis=0)[..., 2 * PY : 2 * PY + rows]
    width = tracer.shape[-1]
    lane = lax.broadcasted_iota(jnp.int32, tracer.shape, 2) % PY
    spread_w = jnp.broadcast_to(west[..., None], west.shape + (PY,)).reshape(tracer.shape)
    spread_e = jnp.broadcast_to(east[..., None], east.shape + (PY,)).reshape(tracer.shape)
    sides = jnp.where(lane == 0, spread_w, jnp.where(lane == PY - 1, spread_e, 0.0))
    return jnp.concatenate([north, south], axis=-1), sides


def activate(pre_act):
    return jax.nn.silu(pre_act).astype(jnp.bfloat16)


def hidden_layers(hidden, b_hidden, w_mid):
    for layer_index in range(w_mid.shape[0]):
        pre_act = (
            jnp.einsum(
                "...h,hj->...j", hidden, w_mid[layer_index], preferred_element_type=jnp.float32
            )
            + b_hidden[layer_index + 1]
        )
        hidden = activate(pre_act)
    return hidden


def on_device(
    state, courant_x, courant_y, surface, w_in, b_hidden, w_mid, w_out, owner_map, neighbours
):
    groups = lax.axis_size("grp")
    patches = lax.axis_size("patch")
    group_here = lax.axis_index("grp")
    patch_here = lax.axis_index("patch")
    level_share = LEV // groups
    surf_share = SURF // groups
    feat_share = VARS * level_share + surf_share
    quarter_rows = PX // groups
    capacity = max(2, 2 * quarter_rows // patches)
    slot_count = patches * capacity
    tracer = state.reshape(VARS, level_share, PX, PY)
    beside_all = jnp.take(neighbours, patch_here, axis=0)
    features = jnp.concatenate(
        [
            tracer.astype(jnp.bfloat16).reshape(VARS * level_share, PX, PY),
            surface.reshape(surf_share, PX, PY),
        ],
        axis=0,
    )
    by_quarter = features.reshape(feat_share, groups, quarter_rows, PY).transpose(1, 2, 0, 3)
    owners_all = owner_map.reshape(patches, groups, quarter_rows)
    owners_here = jnp.take(owners_all, patch_here, axis=0)
    matches = (owners_here[..., None] == jnp.arange(patches, dtype=jnp.int32)).astype(jnp.int32)
    slot_rank = jnp.sum((jnp.cumsum(matches, axis=1) - matches) * matches, axis=2)
    slot_index = owners_here * capacity + slot_rank
    selector = (
        slot_index[:, None, :] == jnp.arange(slot_count, dtype=jnp.int32)[None, :, None]
    ).astype(jnp.bfloat16)
    selector_here = jnp.take(selector, group_here, axis=0)
    state_part = (
        w_in[: VARS * LEV]
        .reshape(VARS, groups, level_share, -1)
        .transpose(1, 0, 2, 3)
        .reshape(groups, VARS * level_share, -1)
    )
    w_local = jnp.concatenate(
        [state_part, w_in[VARS * LEV :].reshape(groups, surf_share, -1)], axis=1
    )
    w_split = w_out.reshape(-1, VARS, groups, level_share)
    regrouped = lax.all_to_all(by_quarter, "grp", split_axis=0, concat_axis=0, tiled=True)
    pre_act = (
        jnp.einsum("gbfc,gfh->bch", regrouped, w_local, preferred_element_type=jnp.float32)
        + b_hidden[0]
    )
    hidden = hidden_layers(activate(pre_act), b_hidden, w_mid)
    tendency = jnp.einsum(
        "bch,hvgl->bvglc", hidden, w_split, preferred_element_type=jnp.float32
    ).astype(jnp.bfloat16)
    heating = HEAT_WEIGHT * jnp.sum(tendency[:, 0].astype(jnp.float32), axis=(1, 2))
    packed = jnp.dot(
        selector_here.astype(jnp.float32), heating, precision=lax.Precision.HIGHEST
    ).reshape(patches, capacity, PY)
    owner_heating = lax.all_to_all(
        packed, "patch", split_axis=0, concat_axis=0, tiled=True
    ).reshape(slot_count, PY)
    arrived = lax.all_to_all(tendency, "grp", split_axis=2, concat_axis=0, tiled=True)
    tendency_here = arrived.reshape(PX, VARS, level_share, PY)
    advected = state
    for section_index in range(SUBSTEPS):
        halo_rows, halo_sides = exchange_halo(advected, beside_all, patches)
        last = section_index == SUBSTEPS - 1
        advected = stencil(
            advected, courant_x, courant_y, halo_rows, halo_sides, tendency_here if last else None
        )
    new_state = advected
    return (new_state, owner_heating)


def solution(mesh):
    placed = (
        P(None, "grp", "patch"),
        P("grp", "patch"),
        P("grp", "patch"),
        P("grp", "patch"),
        P(),
        P(),
        P(),
        P(),
        P(),
        P(),
    )
    return jax.shard_map(
        on_device,
        mesh=mesh,
        in_specs=placed,
        out_specs=(P(None, "grp", "patch"), P("grp", "patch")),
        check_vma=False,
    )
```

```python
import functools

import jax
import jax.numpy as jnp
from jax import lax
from jax.experimental import pallas as pl
from jax.experimental.pallas import tpu as pltpu
from jax.sharding import PartitionSpec as P

VARS = 9
LEV = 60
SURF = 16
SUBSTEPS = 3
PY = 128
PX = 64


KAPPA = 0.24
PHYS_DT = 0.05
HEAT_WEIGHT = 0.125


def stencil_kernel(*refs, with_tend):
    if with_tend:
        st_ref, cx_ref, cy_ref, rows_ref, tend_ref, out_ref = refs
    else:
        st_ref, cx_ref, cy_ref, rows_ref, out_ref = refs
    rows = st_ref.shape[2] // PY
    north = rows_ref[0, :, 0:PY]
    south = rows_ref[0, :, PY : 2 * PY]
    sides = rows_ref[0, :, 2 * PY : 3 * PY]
    lane = lax.broadcasted_iota(jnp.int32, north.shape, 1)
    for x in range(rows):
        here = slice(x * PY, (x + 1) * PY)
        cur = st_ref[0, :, here]
        up = north if x == 0 else st_ref[0, :, (x - 1) * PY : x * PY]
        down = south if x == rows - 1 else st_ref[0, :, (x + 1) * PY : (x + 2) * PY]
        side = pltpu.roll(sides, (PY - 2 * x) % PY, 1)
        west = jnp.where(lane == 0, side, pltpu.roll(cur, 1, 1))
        east = jnp.where(lane == PY - 1, side, pltpu.roll(cur, PY - 1, 1))
        along_x = cx_ref[:, here]
        along_y = cy_ref[:, here]
        val = (
            cur
            - 0.5 * along_x * (down - up)
            - 0.5 * along_y * (east - west)
            + KAPPA * (up + down + west + east - 4.0 * cur)
        )
        if with_tend:
            val = val + PHYS_DT * tend_ref[x, 0].astype(jnp.float32)
        out_ref[0, :, here] = val


def stencil(tracer, along_x, along_y, halo, tend):
    n_vars, levels, width = tracer.shape
    with_tend = tend is not None
    in_specs = [
        pl.BlockSpec((1, levels, width), lambda v: (v, 0, 0)),
        pl.BlockSpec((levels, width), lambda v: (0, 0)),
        pl.BlockSpec((levels, width), lambda v: (0, 0)),
        pl.BlockSpec((1, levels, 3 * PY), lambda v: (v, 0, 0)),
    ]
    args = [tracer, along_x, along_y, halo]
    if with_tend:
        in_specs.append(pl.BlockSpec((tend.shape[0], 1, levels, PY), lambda v: (0, v, 0, 0)))
        args.append(tend)
    return pl.pallas_call(
        functools.partial(stencil_kernel, with_tend=with_tend),
        grid=(n_vars,),
        in_specs=in_specs,
        out_specs=pl.BlockSpec((1, levels, width), lambda v: (v, 0, 0)),
        out_shape=jax.ShapeDtypeStruct(tracer.shape, jnp.float32),
        cost_estimate=pl.CostEstimate(
            flops=20 * tracer.size, transcendentals=0, bytes_accessed=4 * (2 * tracer.size + 2 * along_x.size)
        ),
    )(*args)


def edges_of(tracer):
    width = tracer.shape[-1]
    return jnp.concatenate(
        [tracer[..., 0:PY], tracer[..., width - PY :], tracer[..., 0::PY], tracer[..., PY - 1 :: PY]],
        axis=-1,
    ).astype(jnp.bfloat16)


def exchange_halo(tracer, beside_all, patches):
    payload = edges_of(tracer)
    sent = jnp.broadcast_to(payload[None], (patches,) + payload.shape)
    got = lax.all_to_all(sent, "patch", split_axis=0, concat_axis=0, tiled=True)
    rows = PX
    north = jnp.take(got, beside_all[0], axis=0)[..., PY : 2 * PY]
    south = jnp.take(got, beside_all[1], axis=0)[..., 0:PY]
    west = jnp.take(got, beside_all[2], axis=0)[..., 2 * PY + rows : 2 * PY + 2 * rows]
    east = jnp.take(got, beside_all[3], axis=0)[..., 2 * PY : 2 * PY + rows]
    sides = jnp.stack([west, jnp.roll(east, -1, axis=-1)], axis=-1).reshape(west.shape[:-1] + (2 * rows,))
    return jnp.concatenate([north, south, sides], axis=-1).astype(jnp.float32)


def activate(pre_act):
    return jax.nn.silu(pre_act).astype(jnp.bfloat16)


def hidden_layers(hidden, b_hidden, w_mid):
    for layer_index in range(w_mid.shape[0]):
        pre_act = (
            jnp.einsum(
                "...h,hj->...j", hidden, w_mid[layer_index], preferred_element_type=jnp.float32
            )
            + b_hidden[layer_index + 1]
        )
        hidden = activate(pre_act)
    return hidden


def on_device(
    state, courant_x, courant_y, surface, w_in, b_hidden, w_mid, w_out, owner_map, neighbours
):
    groups = lax.axis_size("grp")
    patches = lax.axis_size("patch")
    group_here = lax.axis_index("grp")
    patch_here = lax.axis_index("patch")
    level_share = LEV // groups
    surf_share = SURF // groups
    feat_share = VARS * level_share + surf_share
    quarter_rows = PX // groups
    capacity = max(2, 2 * quarter_rows // patches)
    slot_count = patches * capacity
    tracer = state.reshape(VARS, level_share, PX, PY)
    beside_all = jnp.take(neighbours, patch_here, axis=0)
    features = jnp.concatenate(
        [
            tracer.astype(jnp.bfloat16).reshape(VARS * level_share, PX, PY),
            surface.reshape(surf_share, PX, PY),
        ],
        axis=0,
    )
    by_quarter = features.reshape(feat_share, groups, quarter_rows, PY).transpose(1, 2, 0, 3)
    owners_all = owner_map.reshape(patches, groups, quarter_rows)
    owners_here = jnp.take(owners_all, patch_here, axis=0)
    matches = (owners_here[..., None] == jnp.arange(patches, dtype=jnp.int32)).astype(jnp.int32)
    slot_rank = jnp.sum((jnp.cumsum(matches, axis=1) - matches) * matches, axis=2)
    slot_index = owners_here * capacity + slot_rank
    selector = (
        slot_index[:, None, :] == jnp.arange(slot_count, dtype=jnp.int32)[None, :, None]
    ).astype(jnp.bfloat16)
    selector_here = jnp.take(selector, group_here, axis=0)
    state_part = (
        w_in[: VARS * LEV]
        .reshape(VARS, groups, level_share, -1)
        .transpose(1, 0, 2, 3)
        .reshape(groups, VARS * level_share, -1)
    )
    w_local = jnp.concatenate(
        [state_part, w_in[VARS * LEV :].reshape(groups, surf_share, -1)], axis=1
    )
    w_split = w_out.reshape(-1, VARS, groups, level_share)
    regrouped = lax.all_to_all(by_quarter, "grp", split_axis=0, concat_axis=0, tiled=True)
    pre_act = (
        jnp.einsum("gbfc,gfh->bch", regrouped, w_local, preferred_element_type=jnp.float32)
        + b_hidden[0]
    )
    hidden = hidden_layers(activate(pre_act), b_hidden, w_mid)
    tendency = jnp.einsum(
        "bch,hvgl->bvglc", hidden, w_split, preferred_element_type=jnp.float32
    ).astype(jnp.bfloat16)
    heating = HEAT_WEIGHT * jnp.sum(tendency[:, 0].astype(jnp.float32), axis=(1, 2))
    packed = jnp.dot(
        selector_here.astype(jnp.float32), heating, precision=lax.Precision.HIGHEST
    ).reshape(patches, capacity, PY)
    owner_heating = lax.all_to_all(
        packed, "patch", split_axis=0, concat_axis=0, tiled=True
    ).reshape(slot_count, PY)
    arrived = lax.all_to_all(tendency, "grp", split_axis=2, concat_axis=0, tiled=True)
    tendency_here = arrived.reshape(PX, VARS, level_share, PY)
    advected = state
    for section_index in range(SUBSTEPS):
        halo = exchange_halo(advected, beside_all, patches)
        last = section_index == SUBSTEPS - 1
        advected = stencil(
            advected, courant_x, courant_y, halo, tendency_here if last else None
        )
    new_state = advected
    return (new_state, owner_heating)


def solution(mesh):
    placed = (
        P(None, "grp", "patch"),
        P("grp", "patch"),
        P("grp", "patch"),
        P("grp", "patch"),
        P(),
        P(),
        P(),
        P(),
        P(),
        P(),
    )
    return jax.shard_map(
        on_device,
        mesh=mesh,
        in_specs=placed,
        out_specs=(P(None, "grp", "patch"), P("grp", "patch")),
        check_vma=False,
    )
```

```python
import functools

import jax
import jax.numpy as jnp
from jax import lax
from jax.experimental import pallas as pl
from jax.experimental.pallas import tpu as pltpu
from jax.sharding import PartitionSpec as P

VARS = 9
LEV = 60
SURF = 16
SUBSTEPS = 3
PY = 128
PX = 64


KAPPA = 0.24
PHYS_DT = 0.05
HEAT_WEIGHT = 0.125


def stencil_kernel(*refs, with_tend):
    if with_tend:
        st_ref, cx_ref, cy_ref, rows_ref, tend_ref, out_ref = refs
    else:
        st_ref, cx_ref, cy_ref, rows_ref, out_ref = refs
    rows = st_ref.shape[2] // PY
    north = rows_ref[0, :, 0:PY]
    south = rows_ref[0, :, PY : 2 * PY]
    sides = rows_ref[0, :, 2 * PY : 3 * PY]
    lane = lax.broadcasted_iota(jnp.int32, north.shape, 1)
    for x in range(rows):
        here = slice(x * PY, (x + 1) * PY)
        cur = st_ref[0, :, here]
        up = north if x == 0 else st_ref[0, :, (x - 1) * PY : x * PY]
        down = south if x == rows - 1 else st_ref[0, :, (x + 1) * PY : (x + 2) * PY]
        side = pltpu.roll(sides, (PY - 2 * x) % PY, 1)
        west = jnp.where(lane == 0, side, pltpu.roll(cur, 1, 1))
        east = jnp.where(lane == PY - 1, side, pltpu.roll(cur, PY - 1, 1))
        along_x = cx_ref[:, here]
        along_y = cy_ref[:, here]
        val = (
            cur
            - 0.5 * along_x * (down - up)
            - 0.5 * along_y * (east - west)
            + KAPPA * (up + down + west + east - 4.0 * cur)
        )
        if with_tend:
            val = val + PHYS_DT * tend_ref[x, 0].astype(jnp.float32)
        out_ref[0, :, here] = val


def stencil(tracer, along_x, along_y, halo, tend):
    n_vars, levels, width = tracer.shape
    with_tend = tend is not None
    in_specs = [
        pl.BlockSpec((1, levels, width), lambda v: (v, 0, 0)),
        pl.BlockSpec((levels, width), lambda v: (0, 0)),
        pl.BlockSpec((levels, width), lambda v: (0, 0)),
        pl.BlockSpec((1, levels, 3 * PY), lambda v: (v, 0, 0)),
    ]
    args = [tracer, along_x, along_y, halo]
    if with_tend:
        in_specs.append(pl.BlockSpec((tend.shape[0], 1, levels, PY), lambda v: (0, v, 0, 0)))
        args.append(tend)
    return pl.pallas_call(
        functools.partial(stencil_kernel, with_tend=with_tend),
        grid=(n_vars,),
        in_specs=in_specs,
        out_specs=pl.BlockSpec((1, levels, width), lambda v: (v, 0, 0)),
        out_shape=jax.ShapeDtypeStruct(tracer.shape, jnp.float32),
        cost_estimate=pl.CostEstimate(
            flops=20 * tracer.size, transcendentals=0, bytes_accessed=4 * (2 * tracer.size + 2 * along_x.size)
        ),
    )(*args)


def edges_of(tracer):
    width = tracer.shape[-1]
    return jnp.concatenate(
        [tracer[..., 0:PY], tracer[..., width - PY :], tracer[..., 0::PY], tracer[..., PY - 1 :: PY]],
        axis=-1,
    ).astype(jnp.bfloat16)


def exchange_halo(tracer, beside_all, patches):
    payload = edges_of(tracer)
    got = lax.all_gather(payload, "patch", axis=0, tiled=False)
    rows = PX
    north = jnp.take(got, beside_all[0], axis=0)[..., PY : 2 * PY]
    south = jnp.take(got, beside_all[1], axis=0)[..., 0:PY]
    west = jnp.take(got, beside_all[2], axis=0)[..., 2 * PY + rows : 2 * PY + 2 * rows]
    east = jnp.take(got, beside_all[3], axis=0)[..., 2 * PY : 2 * PY + rows]
    sides = jnp.stack([west, jnp.roll(east, -1, axis=-1)], axis=-1).reshape(west.shape[:-1] + (2 * rows,))
    return jnp.concatenate([north, south, sides], axis=-1).astype(jnp.float32)


def activate(pre_act):
    return jax.nn.silu(pre_act).astype(jnp.bfloat16)


def hidden_layers(hidden, b_hidden, w_mid):
    for layer_index in range(w_mid.shape[0]):
        pre_act = (
            jnp.einsum(
                "...h,hj->...j", hidden, w_mid[layer_index], preferred_element_type=jnp.float32
            )
            + b_hidden[layer_index + 1]
        )
        hidden = activate(pre_act)
    return hidden


def on_device(
    state, courant_x, courant_y, surface, w_in, b_hidden, w_mid, w_out, owner_map, neighbours
):
    groups = lax.axis_size("grp")
    patches = lax.axis_size("patch")
    group_here = lax.axis_index("grp")
    patch_here = lax.axis_index("patch")
    level_share = LEV // groups
    surf_share = SURF // groups
    feat_share = VARS * level_share + surf_share
    quarter_rows = PX // groups
    capacity = max(2, 2 * quarter_rows // patches)
    slot_count = patches * capacity
    tracer = state.reshape(VARS, level_share, PX, PY)
    beside_all = jnp.take(neighbours, patch_here, axis=0)
    features = jnp.concatenate(
        [
            tracer.astype(jnp.bfloat16).reshape(VARS * level_share, PX, PY),
            surface.reshape(surf_share, PX, PY),
        ],
        axis=0,
    )
    by_quarter = features.reshape(feat_share, groups, quarter_rows, PY).transpose(1, 2, 0, 3)
    owners_all = owner_map.reshape(patches, groups, quarter_rows)
    owners_here = jnp.take(owners_all, patch_here, axis=0)
    matches = (owners_here[..., None] == jnp.arange(patches, dtype=jnp.int32)).astype(jnp.int32)
    slot_rank = jnp.sum((jnp.cumsum(matches, axis=1) - matches) * matches, axis=2)
    slot_index = owners_here * capacity + slot_rank
    selector = (
        slot_index[:, None, :] == jnp.arange(slot_count, dtype=jnp.int32)[None, :, None]
    ).astype(jnp.bfloat16)
    selector_here = jnp.take(selector, group_here, axis=0)
    state_part = (
        w_in[: VARS * LEV]
        .reshape(VARS, groups, level_share, -1)
        .transpose(1, 0, 2, 3)
        .reshape(groups, VARS * level_share, -1)
    )
    w_local = jnp.concatenate(
        [state_part, w_in[VARS * LEV :].reshape(groups, surf_share, -1)], axis=1
    )
    w_split = w_out.reshape(-1, VARS, groups, level_share)
    regrouped = lax.all_to_all(by_quarter, "grp", split_axis=0, concat_axis=0, tiled=True)
    pre_act = (
        jnp.einsum("gbfc,gfh->bch", regrouped, w_local, preferred_element_type=jnp.float32)
        + b_hidden[0]
    )
    hidden = hidden_layers(activate(pre_act), b_hidden, w_mid)
    tendency = jnp.einsum(
        "bch,hvgl->bvglc", hidden, w_split, preferred_element_type=jnp.float32
    ).astype(jnp.bfloat16)
    heating = HEAT_WEIGHT * jnp.sum(tendency[:, 0].astype(jnp.float32), axis=(1, 2))
    packed = jnp.dot(
        selector_here.astype(jnp.float32), heating, precision=lax.Precision.HIGHEST
    ).reshape(patches, capacity, PY)
    owner_heating = lax.all_to_all(
        packed, "patch", split_axis=0, concat_axis=0, tiled=True
    ).reshape(slot_count, PY)
    arrived = lax.all_to_all(tendency, "grp", split_axis=2, concat_axis=0, tiled=True)
    tendency_here = arrived.reshape(PX, VARS, level_share, PY)
    advected = state
    for section_index in range(SUBSTEPS):
        halo = exchange_halo(advected, beside_all, patches)
        last = section_index == SUBSTEPS - 1
        advected = stencil(
            advected, courant_x, courant_y, halo, tendency_here if last else None
        )
    new_state = advected
    return (new_state, owner_heating)


def solution(mesh):
    placed = (
        P(None, "grp", "patch"),
        P("grp", "patch"),
        P("grp", "patch"),
        P("grp", "patch"),
        P(),
        P(),
        P(),
        P(),
        P(),
        P(),
    )
    return jax.shard_map(
        on_device,
        mesh=mesh,
        in_specs=placed,
        out_specs=(P(None, "grp", "patch"), P("grp", "patch")),
        check_vma=False,
    )
```

```python
import functools

import jax
import jax.numpy as jnp
from jax import lax
from jax.experimental import pallas as pl
from jax.experimental.pallas import tpu as pltpu
from jax.sharding import PartitionSpec as P

VARS = 9
LEV = 60
SURF = 16
SUBSTEPS = 3
PY = 128
PX = 64


KAPPA = 0.24
PHYS_DT = 0.05
HEAT_WEIGHT = 0.125


def stencil_kernel(*refs, with_tend):
    if with_tend:
        st_ref, cx_ref, cy_ref, rows_ref, tend_ref, out_ref, erow_ref, ecol_ref, stack_ref = refs
    else:
        st_ref, cx_ref, cy_ref, rows_ref, out_ref, erow_ref, ecol_ref, stack_ref = refs
    rows = st_ref.shape[2] // PY
    slot = stack_ref.shape[0] // rows
    levels = st_ref.shape[1]
    north = rows_ref[0, :, 0:PY]
    south = rows_ref[0, :, PY : 2 * PY]
    sides = rows_ref[0, :, 2 * PY : 3 * PY]
    lane = lax.broadcasted_iota(jnp.int32, north.shape, 1)
    stack_ref[...] = jnp.zeros(stack_ref.shape, stack_ref.dtype)
    for x in range(rows):
        here = slice(x * PY, (x + 1) * PY)
        cur = st_ref[0, :, here]
        up = north if x == 0 else st_ref[0, :, (x - 1) * PY : x * PY]
        down = south if x == rows - 1 else st_ref[0, :, (x + 1) * PY : (x + 2) * PY]
        side = pltpu.roll(sides, (PY - 2 * x) % PY, 1)
        west = jnp.where(lane == 0, side, pltpu.roll(cur, 1, 1))
        east = jnp.where(lane == PY - 1, side, pltpu.roll(cur, PY - 1, 1))
        along_x = cx_ref[:, here]
        along_y = cy_ref[:, here]
        val = (
            cur
            - 0.5 * along_x * (down - up)
            - 0.5 * along_y * (east - west)
            + KAPPA * (up + down + west + east - 4.0 * cur)
        )
        if with_tend:
            val = val + PHYS_DT * tend_ref[x, 0].astype(jnp.float32)
        out_ref[0, :, here] = val
        packed = val.astype(jnp.bfloat16)
        stack_ref[x * slot : x * slot + levels, :] = packed
        if x == 0:
            erow_ref[0, :, 0:PY] = packed
        if x == rows - 1:
            erow_ref[0, :, PY : 2 * PY] = packed
    pick_row = lax.broadcasted_iota(jnp.int32, (8, PY), 0)
    pick_lane = lax.broadcasted_iota(jnp.int32, (8, PY), 1)
    picker = (
        ((pick_row == 0) & (pick_lane == 0)) | ((pick_row == 1) & (pick_lane == PY - 1))
    ).astype(jnp.bfloat16)
    ecol_ref[0] = lax.dot_general(
        picker, stack_ref[...], (((1,), (1,)), ((), ())), preferred_element_type=jnp.float32
    )


def stencil(tracer, along_x, along_y, halo, tend):
    n_vars, levels, width = tracer.shape
    rows = width // PY
    slot = 16
    with_tend = tend is not None
    in_specs = [
        pl.BlockSpec((1, levels, width), lambda v: (v, 0, 0)),
        pl.BlockSpec((levels, width), lambda v: (0, 0)),
        pl.BlockSpec((levels, width), lambda v: (0, 0)),
        pl.BlockSpec((1, levels, 3 * PY), lambda v: (v, 0, 0)),
    ]
    args = [tracer, along_x, along_y, halo]
    if with_tend:
        in_specs.append(pl.BlockSpec((tend.shape[0], 1, levels, PY), lambda v: (0, v, 0, 0)))
        args.append(tend)
    return pl.pallas_call(
        functools.partial(stencil_kernel, with_tend=with_tend),
        grid=(n_vars,),
        in_specs=in_specs,
        out_specs=[
            pl.BlockSpec((1, levels, width), lambda v: (v, 0, 0)),
            pl.BlockSpec((1, levels, 2 * PY), lambda v: (v, 0, 0)),
            pl.BlockSpec((1, 8, rows * slot), lambda v: (v, 0, 0)),
        ],
        out_shape=[
            jax.ShapeDtypeStruct(tracer.shape, jnp.float32),
            jax.ShapeDtypeStruct((n_vars, levels, 2 * PY), jnp.bfloat16),
            jax.ShapeDtypeStruct((n_vars, 8, rows * slot), jnp.float32),
        ],
        scratch_shapes=[pltpu.VMEM((rows * slot, PY), jnp.bfloat16)],
        cost_estimate=pl.CostEstimate(
            flops=20 * tracer.size, transcendentals=0, bytes_accessed=4 * (2 * tracer.size + 2 * along_x.size)
        ),
    )(*args)


def first_edges(tracer):
    n_vars, levels, width = tracer.shape
    rows = width // PY
    edge_rows = jnp.concatenate([tracer[..., 0:PY], tracer[..., width - PY :]], axis=-1)
    edge_cols = jnp.stack([tracer[..., 0::PY], tracer[..., PY - 1 :: PY]], axis=1)
    edge_cols = jnp.swapaxes(edge_cols, 2, 3)
    edge_cols = jnp.pad(edge_cols, ((0, 0), (0, 0), (0, 0), (0, 16 - levels)))
    return edge_rows.astype(jnp.bfloat16), edge_cols.reshape(n_vars, 2, rows * 16)


def exchange_halo(edge_rows, edge_cols, beside_all, patches):
    n_vars, levels, _ = edge_rows.shape
    rows = PX
    row_flat = edge_rows.astype(jnp.bfloat16).reshape(-1)
    col_flat = edge_cols[:, 0:2].astype(jnp.bfloat16).reshape(-1)
    payload = jnp.concatenate([row_flat, col_flat])
    got = lax.all_gather(payload, "patch", axis=0, tiled=False)
    rows_all = got[:, : row_flat.size].reshape((patches,) + edge_rows.shape)
    cols_all = got[:, row_flat.size :].reshape(patches, n_vars, 2, rows, 16)
    north = jnp.take(rows_all, beside_all[0], axis=0)[..., PY : 2 * PY]
    south = jnp.take(rows_all, beside_all[1], axis=0)[..., 0:PY]
    west = jnp.swapaxes(jnp.take(cols_all, beside_all[2], axis=0)[:, 1, :, 0:levels], 1, 2)
    east = jnp.swapaxes(jnp.take(cols_all, beside_all[3], axis=0)[:, 0, :, 0:levels], 1, 2)
    sides = jnp.stack([west, jnp.roll(east, -1, axis=-1)], axis=-1).reshape(west.shape[:-1] + (2 * rows,))
    return jnp.concatenate([north, south, sides], axis=-1).astype(jnp.float32)


def activate(pre_act):
    return jax.nn.silu(pre_act).astype(jnp.bfloat16)


def hidden_layers(hidden, b_hidden, w_mid):
    for layer_index in range(w_mid.shape[0]):
        pre_act = (
            jnp.einsum(
                "...h,hj->...j", hidden, w_mid[layer_index], preferred_element_type=jnp.float32
            )
            + b_hidden[layer_index + 1]
        )
        hidden = activate(pre_act)
    return hidden


def on_device(
    state, courant_x, courant_y, surface, w_in, b_hidden, w_mid, w_out, owner_map, neighbours
):
    groups = lax.axis_size("grp")
    patches = lax.axis_size("patch")
    group_here = lax.axis_index("grp")
    patch_here = lax.axis_index("patch")
    level_share = LEV // groups
    surf_share = SURF // groups
    feat_share = VARS * level_share + surf_share
    quarter_rows = PX // groups
    capacity = max(2, 2 * quarter_rows // patches)
    slot_count = patches * capacity
    tracer = state.reshape(VARS, level_share, PX, PY)
    beside_all = jnp.take(neighbours, patch_here, axis=0)
    features = jnp.concatenate(
        [
            tracer.astype(jnp.bfloat16).reshape(VARS * level_share, PX, PY),
            surface.reshape(surf_share, PX, PY),
        ],
        axis=0,
    )
    by_quarter = features.reshape(feat_share, groups, quarter_rows, PY).transpose(1, 2, 0, 3)
    owners_all = owner_map.reshape(patches, groups, quarter_rows)
    owners_here = jnp.take(owners_all, patch_here, axis=0)
    matches = (owners_here[..., None] == jnp.arange(patches, dtype=jnp.int32)).astype(jnp.int32)
    slot_rank = jnp.sum((jnp.cumsum(matches, axis=1) - matches) * matches, axis=2)
    slot_index = owners_here * capacity + slot_rank
    selector = (
        slot_index[:, None, :] == jnp.arange(slot_count, dtype=jnp.int32)[None, :, None]
    ).astype(jnp.bfloat16)
    selector_here = jnp.take(selector, group_here, axis=0)
    state_part = (
        w_in[: VARS * LEV]
        .reshape(VARS, groups, level_share, -1)
        .transpose(1, 0, 2, 3)
        .reshape(groups, VARS * level_share, -1)
    )
    w_local = jnp.concatenate(
        [state_part, w_in[VARS * LEV :].reshape(groups, surf_share, -1)], axis=1
    )
    w_split = w_out.reshape(-1, VARS, groups, level_share)
    regrouped = lax.all_to_all(by_quarter, "grp", split_axis=0, concat_axis=0, tiled=True)
    pre_act = (
        jnp.einsum("gbfc,gfh->bch", regrouped, w_local, preferred_element_type=jnp.float32)
        + b_hidden[0]
    )
    hidden = hidden_layers(activate(pre_act), b_hidden, w_mid)
    tendency = jnp.einsum(
        "bch,hvgl->bvglc", hidden, w_split, preferred_element_type=jnp.float32
    ).astype(jnp.bfloat16)
    heating = HEAT_WEIGHT * jnp.sum(tendency[:, 0].astype(jnp.float32), axis=(1, 2))
    packed = jnp.dot(
        selector_here.astype(jnp.float32), heating, precision=lax.Precision.HIGHEST
    ).reshape(patches, capacity, PY)
    owner_heating = lax.all_to_all(
        packed, "patch", split_axis=0, concat_axis=0, tiled=True
    ).reshape(slot_count, PY)
    arrived = lax.all_to_all(tendency, "grp", split_axis=2, concat_axis=0, tiled=True)
    tendency_here = arrived.reshape(PX, VARS, level_share, PY)
    advected = state
    edge_rows, edge_cols = first_edges(state)
    for section_index in range(SUBSTEPS):
        halo = exchange_halo(edge_rows, edge_cols, beside_all, patches)
        last = section_index == SUBSTEPS - 1
        advected, edge_rows, edge_cols = stencil(
            advected, courant_x, courant_y, halo, tendency_here if last else None
        )
    new_state = advected
    return (new_state, owner_heating)


def solution(mesh):
    placed = (
        P(None, "grp", "patch"),
        P("grp", "patch"),
        P("grp", "patch"),
        P("grp", "patch"),
        P(),
        P(),
        P(),
        P(),
        P(),
        P(),
    )
    return jax.shard_map(
        on_device,
        mesh=mesh,
        in_specs=placed,
        out_specs=(P(None, "grp", "patch"), P("grp", "patch")),
        check_vma=False,
    )
```

```python
import functools

import jax
import jax.numpy as jnp
from jax import lax
from jax.experimental import pallas as pl
from jax.experimental.pallas import tpu as pltpu
from jax.sharding import PartitionSpec as P

VARS = 9
LEV = 60
SURF = 16
SUBSTEPS = 3
PY = 128
PX = 64


KAPPA = 0.24
PHYS_DT = 0.05
HEAT_WEIGHT = 0.125


def stencil_kernel(*refs, with_tend):
    if with_tend:
        st_ref, cx_ref, cy_ref, rows_ref, tend_ref, out_ref, pay_ref, stack_ref = refs
    else:
        st_ref, cx_ref, cy_ref, rows_ref, out_ref, pay_ref, stack_ref = refs
    rows = st_ref.shape[2] // PY
    slot = stack_ref.shape[0] // rows
    levels = st_ref.shape[1]
    north = rows_ref[0, :, 0:PY]
    south = rows_ref[0, :, PY : 2 * PY]
    sides = rows_ref[0, :, 2 * PY : 3 * PY]
    lane = lax.broadcasted_iota(jnp.int32, north.shape, 1)
    stack_ref[...] = jnp.zeros(stack_ref.shape, stack_ref.dtype)
    for x in range(rows):
        here = slice(x * PY, (x + 1) * PY)
        cur = st_ref[0, :, here]
        up = north if x == 0 else st_ref[0, :, (x - 1) * PY : x * PY]
        down = south if x == rows - 1 else st_ref[0, :, (x + 1) * PY : (x + 2) * PY]
        side = pltpu.roll(sides, (PY - 2 * x) % PY, 1)
        west = jnp.where(lane == 0, side, pltpu.roll(cur, 1, 1))
        east = jnp.where(lane == PY - 1, side, pltpu.roll(cur, PY - 1, 1))
        along_x = cx_ref[:, here]
        along_y = cy_ref[:, here]
        val = (
            cur
            - 0.5 * along_x * (down - up)
            - 0.5 * along_y * (east - west)
            + KAPPA * (up + down + west + east - 4.0 * cur)
        )
        if with_tend:
            val = val + PHYS_DT * tend_ref[x, 0].astype(jnp.float32)
        out_ref[0, :, here] = val
        packed = val.astype(jnp.bfloat16)
        stack_ref[x * slot : x * slot + levels, :] = packed
        if x == 0:
            pay_ref[0, 0:levels, 0:PY] = packed
        if x == rows - 1:
            pay_ref[0, 0:levels, PY : 2 * PY] = packed
    pad_rows = pay_ref.shape[1] - levels
    if pad_rows:
        pay_ref[0, levels:, 0 : 2 * PY] = jnp.zeros((pad_rows, 2 * PY), pay_ref.dtype)
    chunks = stack_ref.shape[0] // PY
    pick_row = lax.broadcasted_iota(jnp.int32, (2 * chunks, PY), 0)
    pick_lane = lax.broadcasted_iota(jnp.int32, (2 * chunks, PY), 1)
    cols = jnp.zeros((2 * chunks, PY), jnp.float32)
    for j in range(chunks):
        picker = (
            ((pick_row == 2 * j) & (pick_lane == 0)) | ((pick_row == 2 * j + 1) & (pick_lane == PY - 1))
        ).astype(jnp.bfloat16)
        cols = cols + lax.dot_general(
            picker,
            stack_ref[j * PY : (j + 1) * PY, :],
            (((1,), (1,)), ((), ())),
            preferred_element_type=jnp.float32,
        )
    pay_ref[0, :, 2 * PY : 3 * PY] = cols.astype(pay_ref.dtype)


def stencil(tracer, along_x, along_y, halo, tend):
    n_vars, levels, width = tracer.shape
    rows = width // PY
    slot = 16
    with_tend = tend is not None
    in_specs = [
        pl.BlockSpec((1, levels, width), lambda v: (v, 0, 0)),
        pl.BlockSpec((levels, width), lambda v: (0, 0)),
        pl.BlockSpec((levels, width), lambda v: (0, 0)),
        pl.BlockSpec((1, levels, 3 * PY), lambda v: (v, 0, 0)),
    ]
    args = [tracer, along_x, along_y, halo]
    if with_tend:
        in_specs.append(pl.BlockSpec((tend.shape[0], 1, levels, PY), lambda v: (0, v, 0, 0)))
        args.append(tend)
    return pl.pallas_call(
        functools.partial(stencil_kernel, with_tend=with_tend),
        grid=(n_vars,),
        in_specs=in_specs,
        out_specs=[
            pl.BlockSpec((1, levels, width), lambda v: (v, 0, 0)),
            pl.BlockSpec((1, slot, 3 * PY), lambda v: (v, 0, 0)),
        ],
        out_shape=[
            jax.ShapeDtypeStruct(tracer.shape, jnp.float32),
            jax.ShapeDtypeStruct((n_vars, slot, 3 * PY), jnp.bfloat16),
        ],
        scratch_shapes=[pltpu.VMEM((rows * slot, PY), jnp.bfloat16)],
        cost_estimate=pl.CostEstimate(
            flops=20 * tracer.size, transcendentals=0, bytes_accessed=4 * (2 * tracer.size + 2 * along_x.size)
        ),
    )(*args)


def first_edges(tracer):
    n_vars, levels, width = tracer.shape
    rows = width // PY
    slot = 16
    chunk_rows = PY // slot
    edge_rows = jnp.concatenate([tracer[..., 0:PY], tracer[..., width - PY :]], axis=-1)
    edge_rows = jnp.pad(edge_rows, ((0, 0), (0, slot - levels), (0, 0)))
    edge_cols = jnp.stack([tracer[..., 0::PY], tracer[..., PY - 1 :: PY]], axis=1)
    edge_cols = jnp.pad(edge_cols, ((0, 0), (0, 0), (0, slot - levels), (0, 0)))
    edge_cols = edge_cols.reshape(n_vars, 2, slot, rows // chunk_rows, chunk_rows)
    edge_cols = edge_cols.transpose(0, 3, 1, 4, 2).reshape(n_vars, 2 * rows // chunk_rows, PY)
    return jnp.concatenate([edge_rows, edge_cols], axis=-1).astype(jnp.bfloat16)


def exchange_halo(payload, beside_all, patches, levels):
    n_vars, slot, _ = payload.shape
    rows = PX
    chunk_rows = PY // slot
    got = lax.all_gather(payload, "patch", axis=0, tiled=False)
    north = jnp.take(got, beside_all[0], axis=0)[:, 0:levels, PY : 2 * PY]
    south = jnp.take(got, beside_all[1], axis=0)[:, 0:levels, 0:PY]

    def column(patch, which):
        cols = jnp.take(got, patch, axis=0)[..., 2 * PY : 3 * PY]
        cols = cols.reshape(n_vars, rows // chunk_rows, 2, chunk_rows, slot)[:, :, which]
        return cols.transpose(0, 3, 1, 2).reshape(n_vars, slot, rows)[:, 0:levels]

    west = column(beside_all[2], 1)
    east = column(beside_all[3], 0)
    sides = jnp.stack([west, jnp.roll(east, -1, axis=-1)], axis=-1).reshape(west.shape[:-1] + (2 * rows,))
    return jnp.concatenate([north, south, sides], axis=-1).astype(jnp.float32)


def activate(pre_act):
    return jax.nn.silu(pre_act).astype(jnp.bfloat16)


def hidden_layers(hidden, b_hidden, w_mid):
    for layer_index in range(w_mid.shape[0]):
        pre_act = (
            jnp.einsum(
                "...h,hj->...j", hidden, w_mid[layer_index], preferred_element_type=jnp.float32
            )
            + b_hidden[layer_index + 1]
        )
        hidden = activate(pre_act)
    return hidden


def on_device(
    state, courant_x, courant_y, surface, w_in, b_hidden, w_mid, w_out, owner_map, neighbours
):
    groups = lax.axis_size("grp")
    patches = lax.axis_size("patch")
    group_here = lax.axis_index("grp")
    patch_here = lax.axis_index("patch")
    level_share = LEV // groups
    surf_share = SURF // groups
    feat_share = VARS * level_share + surf_share
    quarter_rows = PX // groups
    capacity = max(2, 2 * quarter_rows // patches)
    slot_count = patches * capacity
    tracer = state.reshape(VARS, level_share, PX, PY)
    beside_all = jnp.take(neighbours, patch_here, axis=0)
    features = jnp.concatenate(
        [
            tracer.astype(jnp.bfloat16).reshape(VARS * level_share, PX, PY),
            surface.reshape(surf_share, PX, PY),
        ],
        axis=0,
    )
    by_quarter = features.reshape(feat_share, groups, quarter_rows, PY).transpose(1, 2, 0, 3)
    owners_all = owner_map.reshape(patches, groups, quarter_rows)
    owners_here = jnp.take(owners_all, patch_here, axis=0)
    matches = (owners_here[..., None] == jnp.arange(patches, dtype=jnp.int32)).astype(jnp.int32)
    slot_rank = jnp.sum((jnp.cumsum(matches, axis=1) - matches) * matches, axis=2)
    slot_index = owners_here * capacity + slot_rank
    selector = (
        slot_index[:, None, :] == jnp.arange(slot_count, dtype=jnp.int32)[None, :, None]
    ).astype(jnp.bfloat16)
    selector_here = jnp.take(selector, group_here, axis=0)
    state_part = (
        w_in[: VARS * LEV]
        .reshape(VARS, groups, level_share, -1)
        .transpose(1, 0, 2, 3)
        .reshape(groups, VARS * level_share, -1)
    )
    w_local = jnp.concatenate(
        [state_part, w_in[VARS * LEV :].reshape(groups, surf_share, -1)], axis=1
    )
    w_split = w_out.reshape(-1, VARS, groups, level_share)
    regrouped = lax.all_to_all(by_quarter, "grp", split_axis=0, concat_axis=0, tiled=True)
    pre_act = (
        jnp.einsum("gbfc,gfh->bch", regrouped, w_local, preferred_element_type=jnp.float32)
        + b_hidden[0]
    )
    hidden = hidden_layers(activate(pre_act), b_hidden, w_mid)
    tendency = jnp.einsum(
        "bch,hvgl->bvglc", hidden, w_split, preferred_element_type=jnp.float32
    ).astype(jnp.bfloat16)
    heating = HEAT_WEIGHT * jnp.sum(tendency[:, 0].astype(jnp.float32), axis=(1, 2))
    packed = jnp.dot(
        selector_here.astype(jnp.float32), heating, precision=lax.Precision.HIGHEST
    ).reshape(patches, capacity, PY)
    owner_heating = lax.all_to_all(
        packed, "patch", split_axis=0, concat_axis=0, tiled=True
    ).reshape(slot_count, PY)
    arrived = lax.all_to_all(tendency, "grp", split_axis=2, concat_axis=0, tiled=True)
    tendency_here = arrived.reshape(PX, VARS, level_share, PY)
    advected = state
    payload = first_edges(state)
    for section_index in range(SUBSTEPS):
        halo = exchange_halo(payload, beside_all, patches, level_share)
        last = section_index == SUBSTEPS - 1
        advected, payload = stencil(
            advected, courant_x, courant_y, halo, tendency_here if last else None
        )
    new_state = advected
    return (new_state, owner_heating)


def solution(mesh):
    placed = (
        P(None, "grp", "patch"),
        P("grp", "patch"),
        P("grp", "patch"),
        P("grp", "patch"),
        P(),
        P(),
        P(),
        P(),
        P(),
        P(),
    )
    return jax.shard_map(
        on_device,
        mesh=mesh,
        in_specs=placed,
        out_specs=(P(None, "grp", "patch"), P("grp", "patch")),
        check_vma=False,
    )
```

```python
import functools

import jax
import jax.numpy as jnp
from jax import lax
from jax.experimental import pallas as pl
from jax.experimental.pallas import tpu as pltpu
from jax.sharding import PartitionSpec as P

VARS = 9
LEV = 60
SURF = 16
SUBSTEPS = 3
PY = 128
PX = 64


KAPPA = 0.24
PHYS_DT = 0.05
HEAT_WEIGHT = 0.125


def stencil_kernel(*refs, with_tend):
    if with_tend:
        st_ref, cx_ref, cy_ref, rows_ref, tend_ref, out_ref, pay_ref, stack_ref = refs
    else:
        st_ref, cx_ref, cy_ref, rows_ref, out_ref, pay_ref, stack_ref = refs
    rows = st_ref.shape[2] // PY
    slot = stack_ref.shape[0] // rows
    levels = st_ref.shape[1]
    north = rows_ref[0, :, 0:PY]
    south = rows_ref[0, :, PY : 2 * PY]
    sides = rows_ref[0, :, 2 * PY : 3 * PY]
    lane = lax.broadcasted_iota(jnp.int32, north.shape, 1)
    stack_ref[...] = jnp.zeros(stack_ref.shape, stack_ref.dtype)
    for x in range(rows):
        here = slice(x * PY, (x + 1) * PY)
        cur = st_ref[0, :, here]
        up = north if x == 0 else st_ref[0, :, (x - 1) * PY : x * PY]
        down = south if x == rows - 1 else st_ref[0, :, (x + 1) * PY : (x + 2) * PY]
        side = pltpu.roll(sides, (PY - 2 * x) % PY, 1)
        west = jnp.where(lane == 0, side, pltpu.roll(cur, 1, 1))
        east = jnp.where(lane == PY - 1, side, pltpu.roll(cur, PY - 1, 1))
        along_x = cx_ref[:, here]
        along_y = cy_ref[:, here]
        val = (
            cur
            - 0.5 * along_x * (down - up)
            - 0.5 * along_y * (east - west)
            + KAPPA * (up + down + west + east - 4.0 * cur)
        )
        if with_tend:
            val = val + PHYS_DT * tend_ref[x, 0].astype(jnp.float32)
        out_ref[0, :, here] = val
        packed = val.astype(jnp.bfloat16)
        stack_ref[x * slot : x * slot + levels, :] = packed
        if x == 0:
            pay_ref[0, 0:levels, 0:PY] = packed
        if x == rows - 1:
            pay_ref[0, 0:levels, PY : 2 * PY] = packed
    finish_payload(pay_ref, stack_ref, levels)


def finish_payload(pay_ref, stack_ref, levels):
    pad_rows = pay_ref.shape[1] - levels
    if pad_rows:
        pay_ref[0, levels:, 0 : 2 * PY] = jnp.zeros((pad_rows, 2 * PY), pay_ref.dtype)
    chunks = stack_ref.shape[0] // PY
    pick_row = lax.broadcasted_iota(jnp.int32, (2 * chunks, PY), 0)
    pick_lane = lax.broadcasted_iota(jnp.int32, (2 * chunks, PY), 1)
    cols = jnp.zeros((2 * chunks, PY), jnp.float32)
    for j in range(chunks):
        picker = (
            ((pick_row == 2 * j) & (pick_lane == 0)) | ((pick_row == 2 * j + 1) & (pick_lane == PY - 1))
        ).astype(jnp.bfloat16)
        cols = cols + lax.dot_general(
            picker,
            stack_ref[j * PY : (j + 1) * PY, :],
            (((1,), (1,)), ((), ())),
            preferred_element_type=jnp.float32,
        )
    pay_ref[0, :, 2 * PY : 3 * PY] = cols.astype(pay_ref.dtype)


def stencil(tracer, along_x, along_y, halo, tend):
    n_vars, levels, width = tracer.shape
    rows = width // PY
    slot = 16
    with_tend = tend is not None
    in_specs = [
        pl.BlockSpec((1, levels, width), lambda v: (v, 0, 0)),
        pl.BlockSpec((levels, width), lambda v: (0, 0)),
        pl.BlockSpec((levels, width), lambda v: (0, 0)),
        pl.BlockSpec((1, levels, 3 * PY), lambda v: (v, 0, 0)),
    ]
    args = [tracer, along_x, along_y, halo]
    if with_tend:
        in_specs.append(pl.BlockSpec((tend.shape[0], 1, levels, PY), lambda v: (0, v, 0, 0)))
        args.append(tend)
    return pl.pallas_call(
        functools.partial(stencil_kernel, with_tend=with_tend),
        grid=(n_vars,),
        in_specs=in_specs,
        out_specs=[
            pl.BlockSpec((1, levels, width), lambda v: (v, 0, 0)),
            pl.BlockSpec((1, slot, 3 * PY), lambda v: (v, 0, 0)),
        ],
        out_shape=[
            jax.ShapeDtypeStruct(tracer.shape, jnp.float32),
            jax.ShapeDtypeStruct((n_vars, slot, 3 * PY), jnp.bfloat16),
        ],
        scratch_shapes=[pltpu.VMEM((rows * slot, PY), jnp.bfloat16)],
        cost_estimate=pl.CostEstimate(
            flops=20 * tracer.size, transcendentals=0, bytes_accessed=4 * (2 * tracer.size + 2 * along_x.size)
        ),
    )(*args)


def pack_kernel(st_ref, pay_ref, stack_ref):
    rows = st_ref.shape[2] // PY
    slot = stack_ref.shape[0] // rows
    levels = st_ref.shape[1]
    stack_ref[...] = jnp.zeros(stack_ref.shape, stack_ref.dtype)
    for x in range(rows):
        packed = st_ref[0, :, x * PY : (x + 1) * PY].astype(jnp.bfloat16)
        stack_ref[x * slot : x * slot + levels, :] = packed
        if x == 0:
            pay_ref[0, 0:levels, 0:PY] = packed
        if x == rows - 1:
            pay_ref[0, 0:levels, PY : 2 * PY] = packed
    finish_payload(pay_ref, stack_ref, levels)


def first_edges(tracer):
    n_vars, levels, width = tracer.shape
    rows = width // PY
    slot = 16
    return pl.pallas_call(
        pack_kernel,
        grid=(n_vars,),
        in_specs=[pl.BlockSpec((1, levels, width), lambda v: (v, 0, 0))],
        out_specs=pl.BlockSpec((1, slot, 3 * PY), lambda v: (v, 0, 0)),
        out_shape=jax.ShapeDtypeStruct((n_vars, slot, 3 * PY), jnp.bfloat16),
        scratch_shapes=[pltpu.VMEM((rows * slot, PY), jnp.bfloat16)],
        cost_estimate=pl.CostEstimate(flops=0, transcendentals=0, bytes_accessed=4 * tracer.size),
    )(tracer)


def exchange_halo(payload, beside_all, patches, levels):
    n_vars, slot, _ = payload.shape
    rows = PX
    chunk_rows = PY // slot
    got = lax.all_gather(payload, "patch", axis=0, tiled=False)
    north = jnp.take(got, beside_all[0], axis=0)[:, 0:levels, PY : 2 * PY]
    south = jnp.take(got, beside_all[1], axis=0)[:, 0:levels, 0:PY]

    def column(patch, which):
        cols = jnp.take(got, patch, axis=0)[..., 2 * PY : 3 * PY]
        cols = cols.reshape(n_vars, rows // chunk_rows, 2, chunk_rows, slot)[:, :, which]
        return cols.transpose(0, 3, 1, 2).reshape(n_vars, slot, rows)[:, 0:levels]

    west = column(beside_all[2], 1)
    east = column(beside_all[3], 0)
    sides = jnp.stack([west, jnp.roll(east, -1, axis=-1)], axis=-1).reshape(west.shape[:-1] + (2 * rows,))
    return jnp.concatenate([north, south, sides], axis=-1).astype(jnp.float32)


def activate(pre_act):
    return jax.nn.silu(pre_act).astype(jnp.bfloat16)


def hidden_layers(hidden, b_hidden, w_mid):
    for layer_index in range(w_mid.shape[0]):
        pre_act = (
            jnp.einsum(
                "...h,hj->...j", hidden, w_mid[layer_index], preferred_element_type=jnp.float32
            )
            + b_hidden[layer_index + 1]
        )
        hidden = activate(pre_act)
    return hidden


def on_device(
    state, courant_x, courant_y, surface, w_in, b_hidden, w_mid, w_out, owner_map, neighbours
):
    groups = lax.axis_size("grp")
    patches = lax.axis_size("patch")
    group_here = lax.axis_index("grp")
    patch_here = lax.axis_index("patch")
    level_share = LEV // groups
    surf_share = SURF // groups
    feat_share = VARS * level_share + surf_share
    quarter_rows = PX // groups
    capacity = max(2, 2 * quarter_rows // patches)
    slot_count = patches * capacity
    tracer = state.reshape(VARS, level_share, PX, PY)
    beside_all = jnp.take(neighbours, patch_here, axis=0)
    features = jnp.concatenate(
        [
            tracer.astype(jnp.bfloat16).reshape(VARS * level_share, PX, PY),
            surface.reshape(surf_share, PX, PY),
        ],
        axis=0,
    )
    by_quarter = features.reshape(feat_share, groups, quarter_rows, PY).transpose(1, 2, 0, 3)
    owners_all = owner_map.reshape(patches, groups, quarter_rows)
    owners_here = jnp.take(owners_all, patch_here, axis=0)
    matches = (owners_here[..., None] == jnp.arange(patches, dtype=jnp.int32)).astype(jnp.int32)
    slot_rank = jnp.sum((jnp.cumsum(matches, axis=1) - matches) * matches, axis=2)
    slot_index = owners_here * capacity + slot_rank
    selector = (
        slot_index[:, None, :] == jnp.arange(slot_count, dtype=jnp.int32)[None, :, None]
    ).astype(jnp.bfloat16)
    selector_here = jnp.take(selector, group_here, axis=0)
    state_part = (
        w_in[: VARS * LEV]
        .reshape(VARS, groups, level_share, -1)
        .transpose(1, 0, 2, 3)
        .reshape(groups, VARS * level_share, -1)
    )
    w_local = jnp.concatenate(
        [state_part, w_in[VARS * LEV :].reshape(groups, surf_share, -1)], axis=1
    )
    w_split = w_out.reshape(-1, VARS, groups, level_share)
    regrouped = lax.all_to_all(by_quarter, "grp", split_axis=0, concat_axis=0, tiled=True)
    pre_act = (
        jnp.einsum("gbfc,gfh->bch", regrouped, w_local, preferred_element_type=jnp.float32)
        + b_hidden[0]
    )
    hidden = hidden_layers(activate(pre_act), b_hidden, w_mid)
    tendency = jnp.einsum(
        "bch,hvgl->bvglc", hidden, w_split, preferred_element_type=jnp.float32
    ).astype(jnp.bfloat16)
    heating = HEAT_WEIGHT * jnp.sum(tendency[:, 0].astype(jnp.float32), axis=(1, 2))
    packed = jnp.dot(
        selector_here.astype(jnp.float32), heating, precision=lax.Precision.HIGHEST
    ).reshape(patches, capacity, PY)
    owner_heating = lax.all_to_all(
        packed, "patch", split_axis=0, concat_axis=0, tiled=True
    ).reshape(slot_count, PY)
    arrived = lax.all_to_all(tendency, "grp", split_axis=2, concat_axis=0, tiled=True)
    tendency_here = arrived.reshape(PX, VARS, level_share, PY)
    advected = state
    payload = first_edges(state)
    for section_index in range(SUBSTEPS):
        halo = exchange_halo(payload, beside_all, patches, level_share)
        last = section_index == SUBSTEPS - 1
        advected, payload = stencil(
            advected, courant_x, courant_y, halo, tendency_here if last else None
        )
    new_state = advected
    return (new_state, owner_heating)


def solution(mesh):
    placed = (
        P(None, "grp", "patch"),
        P("grp", "patch"),
        P("grp", "patch"),
        P("grp", "patch"),
        P(),
        P(),
        P(),
        P(),
        P(),
        P(),
    )
    return jax.shard_map(
        on_device,
        mesh=mesh,
        in_specs=placed,
        out_specs=(P(None, "grp", "patch"), P("grp", "patch")),
        check_vma=False,
    )
```

```python
import functools

import jax
import jax.numpy as jnp
from jax import lax
from jax.experimental import pallas as pl
from jax.experimental.pallas import tpu as pltpu
from jax.sharding import PartitionSpec as P

VARS = 9
LEV = 60
SURF = 16
SUBSTEPS = 3
PY = 128
PX = 64


KAPPA = 0.24
PHYS_DT = 0.05
HEAT_WEIGHT = 0.125


def stencil_kernel(*refs, with_tend):
    if with_tend:
        st_ref, cx_ref, cy_ref, rows_ref, tend_ref, out_ref, pay_ref, stack_ref = refs
    else:
        st_ref, cx_ref, cy_ref, rows_ref, out_ref, pay_ref, stack_ref = refs
    rows = st_ref.shape[2] // PY
    slot = stack_ref.shape[0] // rows
    levels = st_ref.shape[1]
    north = rows_ref[0, :, 0:PY]
    south = rows_ref[0, :, PY : 2 * PY]
    sides = rows_ref[0, :, 2 * PY : 3 * PY]
    lane = lax.broadcasted_iota(jnp.int32, north.shape, 1)
    stack_ref[...] = jnp.zeros(stack_ref.shape, stack_ref.dtype)
    for x in range(rows):
        here = slice(x * PY, (x + 1) * PY)
        cur = st_ref[0, :, here]
        up = north if x == 0 else st_ref[0, :, (x - 1) * PY : x * PY]
        down = south if x == rows - 1 else st_ref[0, :, (x + 1) * PY : (x + 2) * PY]
        side = pltpu.roll(sides, (PY - 2 * x) % PY, 1)
        west = jnp.where(lane == 0, side, pltpu.roll(cur, 1, 1))
        east = jnp.where(lane == PY - 1, side, pltpu.roll(cur, PY - 1, 1))
        along_x = cx_ref[:, here]
        along_y = cy_ref[:, here]
        val = (
            cur
            - 0.5 * along_x * (down - up)
            - 0.5 * along_y * (east - west)
            + KAPPA * (up + down + west + east - 4.0 * cur)
        )
        if with_tend:
            val = val + PHYS_DT * tend_ref[x, 0].astype(jnp.float32)
        out_ref[0, :, here] = val
        packed = val.astype(jnp.bfloat16)
        stack_ref[x * slot : x * slot + levels, :] = packed
        if x == 0:
            pay_ref[0, 0:levels, 0:PY] = packed
        if x == rows - 1:
            pay_ref[0, 0:levels, PY : 2 * PY] = packed
    finish_payload(pay_ref, stack_ref, levels)


def finish_payload(pay_ref, stack_ref, levels):
    pad_rows = pay_ref.shape[1] - levels
    if pad_rows:
        pay_ref[0, levels:, 0 : 2 * PY] = jnp.zeros((pad_rows, 2 * PY), pay_ref.dtype)
    chunks = stack_ref.shape[0] // PY
    pick_row = lax.broadcasted_iota(jnp.int32, (2 * chunks, PY), 0)
    pick_lane = lax.broadcasted_iota(jnp.int32, (2 * chunks, PY), 1)
    cols = jnp.zeros((2 * chunks, PY), jnp.float32)
    for j in range(chunks):
        picker = (
            ((pick_row == 2 * j) & (pick_lane == 0)) | ((pick_row == 2 * j + 1) & (pick_lane == PY - 1))
        ).astype(jnp.bfloat16)
        cols = cols + lax.dot_general(
            picker,
            stack_ref[j * PY : (j + 1) * PY, :],
            (((1,), (1,)), ((), ())),
            preferred_element_type=jnp.float32,
        )
    pay_ref[0, :, 2 * PY : 3 * PY] = cols.astype(pay_ref.dtype)


def stencil(tracer, along_x, along_y, halo, tend):
    n_vars, levels, width = tracer.shape
    rows = width // PY
    slot = 16
    with_tend = tend is not None
    in_specs = [
        pl.BlockSpec((1, levels, width), lambda v: (v, 0, 0)),
        pl.BlockSpec((levels, width), lambda v: (0, 0)),
        pl.BlockSpec((levels, width), lambda v: (0, 0)),
        pl.BlockSpec((1, levels, 3 * PY), lambda v: (v, 0, 0)),
    ]
    args = [tracer, along_x, along_y, halo]
    if with_tend:
        in_specs.append(pl.BlockSpec((tend.shape[0], 1, levels, PY), lambda v: (0, v, 0, 0)))
        args.append(tend)
    return pl.pallas_call(
        functools.partial(stencil_kernel, with_tend=with_tend),
        grid=(n_vars,),
        in_specs=in_specs,
        out_specs=[
            pl.BlockSpec((1, levels, width), lambda v: (v, 0, 0)),
            pl.BlockSpec((1, slot, 3 * PY), lambda v: (v, 0, 0)),
        ],
        out_shape=[
            jax.ShapeDtypeStruct(tracer.shape, jnp.float32),
            jax.ShapeDtypeStruct((n_vars, slot, 3 * PY), jnp.bfloat16),
        ],
        scratch_shapes=[pltpu.VMEM((rows * slot, PY), jnp.bfloat16)],
        cost_estimate=pl.CostEstimate(
            flops=20 * tracer.size, transcendentals=0, bytes_accessed=4 * (2 * tracer.size + 2 * along_x.size)
        ),
    )(*args)


def pack_kernel(st_ref, surf_ref, pay_ref, feat_ref, stack_ref, *, n_surf):
    rows = st_ref.shape[2] // PY
    slot = stack_ref.shape[0] // rows
    levels = st_ref.shape[1]
    keep_surface = pl.program_id(0) < n_surf
    stack_ref[...] = jnp.zeros(stack_ref.shape, stack_ref.dtype)
    for x in range(rows):
        here = slice(x * PY, (x + 1) * PY)
        packed = st_ref[0, :, here].astype(jnp.bfloat16)
        stack_ref[x * slot : x * slot + levels, :] = packed
        feat_ref[x, 0, 0:levels, :] = packed
        surf_row = surf_ref[0, :, here]
        feat_ref[x, 0, levels : levels + 1, :] = jnp.where(keep_surface, surf_row, jnp.zeros_like(surf_row))
        if x == 0:
            pay_ref[0, 0:levels, 0:PY] = packed
        if x == rows - 1:
            pay_ref[0, 0:levels, PY : 2 * PY] = packed
    finish_payload(pay_ref, stack_ref, levels)


def first_edges(tracer, surface):
    n_vars, levels, width = tracer.shape
    n_surf = surface.shape[0]
    rows = width // PY
    slot = 16
    surf_rows = surface.reshape(n_surf, 1, width)
    return pl.pallas_call(
        functools.partial(pack_kernel, n_surf=n_surf),
        grid=(n_vars,),
        in_specs=[
            pl.BlockSpec((1, levels, width), lambda v: (v, 0, 0)),
            pl.BlockSpec((1, 1, width), lambda v: (jnp.minimum(v, n_surf - 1), 0, 0)),
        ],
        out_specs=[
            pl.BlockSpec((1, slot, 3 * PY), lambda v: (v, 0, 0)),
            pl.BlockSpec((rows, 1, slot, PY), lambda v: (0, v, 0, 0)),
        ],
        out_shape=[
            jax.ShapeDtypeStruct((n_vars, slot, 3 * PY), jnp.bfloat16),
            jax.ShapeDtypeStruct((rows, n_vars, slot, PY), jnp.bfloat16),
        ],
        scratch_shapes=[pltpu.VMEM((rows * slot, PY), jnp.bfloat16)],
        cost_estimate=pl.CostEstimate(flops=0, transcendentals=0, bytes_accessed=5 * tracer.size),
    )(tracer, surf_rows)


def exchange_halo(payload, beside_all, patches, levels):
    n_vars, slot, _ = payload.shape
    rows = PX
    chunk_rows = PY // slot
    got = lax.all_gather(payload, "patch", axis=0, tiled=False)
    north = jnp.take(got, beside_all[0], axis=0)[:, 0:levels, PY : 2 * PY]
    south = jnp.take(got, beside_all[1], axis=0)[:, 0:levels, 0:PY]

    def column(patch, which):
        cols = jnp.take(got, patch, axis=0)[..., 2 * PY : 3 * PY]
        cols = cols.reshape(n_vars, rows // chunk_rows, 2, chunk_rows, slot)[:, :, which]
        return cols.transpose(0, 3, 1, 2).reshape(n_vars, slot, rows)[:, 0:levels]

    west = column(beside_all[2], 1)
    east = column(beside_all[3], 0)
    sides = jnp.stack([west, jnp.roll(east, -1, axis=-1)], axis=-1).reshape(west.shape[:-1] + (2 * rows,))
    return jnp.concatenate([north, south, sides], axis=-1).astype(jnp.float32)


def activate(pre_act):
    return jax.nn.silu(pre_act).astype(jnp.bfloat16)


def hidden_layers(hidden, b_hidden, w_mid):
    for layer_index in range(w_mid.shape[0]):
        pre_act = (
            jnp.einsum(
                "...h,hj->...j", hidden, w_mid[layer_index], preferred_element_type=jnp.float32
            )
            + b_hidden[layer_index + 1]
        )
        hidden = activate(pre_act)
    return hidden


def on_device(
    state, courant_x, courant_y, surface, w_in, b_hidden, w_mid, w_out, owner_map, neighbours
):
    groups = lax.axis_size("grp")
    patches = lax.axis_size("patch")
    group_here = lax.axis_index("grp")
    patch_here = lax.axis_index("patch")
    level_share = LEV // groups
    surf_share = SURF // groups
    feat_share = VARS * level_share + surf_share
    quarter_rows = PX // groups
    capacity = max(2, 2 * quarter_rows // patches)
    slot_count = patches * capacity
    slot = 16
    beside_all = jnp.take(neighbours, patch_here, axis=0)
    payload, feat = first_edges(state, surface)
    by_quarter = feat.reshape(groups, quarter_rows, VARS * slot, PY)
    owners_all = owner_map.reshape(patches, groups, quarter_rows)
    owners_here = jnp.take(owners_all, patch_here, axis=0)
    matches = (owners_here[..., None] == jnp.arange(patches, dtype=jnp.int32)).astype(jnp.int32)
    slot_rank = jnp.sum((jnp.cumsum(matches, axis=1) - matches) * matches, axis=2)
    slot_index = owners_here * capacity + slot_rank
    selector = (
        slot_index[:, None, :] == jnp.arange(slot_count, dtype=jnp.int32)[None, :, None]
    ).astype(jnp.bfloat16)
    selector_here = jnp.take(selector, group_here, axis=0)
    state_part = w_in[: VARS * LEV].reshape(VARS, groups, level_share, -1).transpose(1, 0, 2, 3)
    state_part = jnp.pad(state_part, ((0, 0), (0, 0), (0, slot - level_share), (0, 0)))
    surf_part = w_in[VARS * LEV :].reshape(groups, surf_share, -1)
    w_local = state_part.at[:, :surf_share, level_share, :].set(surf_part).reshape(groups, VARS * slot, -1)
    w_split = w_out.reshape(-1, VARS, groups, level_share)
    regrouped = lax.all_to_all(by_quarter, "grp", split_axis=0, concat_axis=0, tiled=True)
    pre_act = (
        jnp.einsum("gbfc,gfh->bch", regrouped, w_local, preferred_element_type=jnp.float32)
        + b_hidden[0]
    )
    hidden = hidden_layers(activate(pre_act), b_hidden, w_mid)
    tendency = jnp.einsum(
        "bch,hvgl->gbvlc", hidden, w_split, preferred_element_type=jnp.float32
    ).astype(jnp.bfloat16)
    heating = HEAT_WEIGHT * jnp.sum(tendency[:, :, 0].astype(jnp.float32), axis=(0, 2))
    packed = jnp.dot(
        selector_here.astype(jnp.float32), heating, precision=lax.Precision.HIGHEST
    ).reshape(patches, capacity, PY)
    owner_heating = lax.all_to_all(
        packed, "patch", split_axis=0, concat_axis=0, tiled=True
    ).reshape(slot_count, PY)
    arrived = lax.all_to_all(tendency, "grp", split_axis=0, concat_axis=0, tiled=True)
    tendency_here = arrived.reshape(PX, VARS, level_share, PY)
    advected = state
    for section_index in range(SUBSTEPS):
        halo = exchange_halo(payload, beside_all, patches, level_share)
        last = section_index == SUBSTEPS - 1
        advected, payload = stencil(
            advected, courant_x, courant_y, halo, tendency_here if last else None
        )
    new_state = advected
    return (new_state, owner_heating)


def solution(mesh):
    placed = (
        P(None, "grp", "patch"),
        P("grp", "patch"),
        P("grp", "patch"),
        P("grp", "patch"),
        P(),
        P(),
        P(),
        P(),
        P(),
        P(),
    )
    return jax.shard_map(
        on_device,
        mesh=mesh,
        in_specs=placed,
        out_specs=(P(None, "grp", "patch"), P("grp", "patch")),
        check_vma=False,
    )
```

```python
import functools

import jax
import jax.numpy as jnp
from jax import lax
from jax.experimental import pallas as pl
from jax.experimental.pallas import tpu as pltpu
from jax.sharding import PartitionSpec as P

VARS = 9
LEV = 60
SURF = 16
SUBSTEPS = 3
PY = 128
PX = 64


KAPPA = 0.24
PHYS_DT = 0.05
HEAT_WEIGHT = 0.125


def stencil_kernel(*refs, with_tend):
    if with_tend:
        st_ref, cx_ref, cy_ref, rows_ref, tend_ref, out_ref, pay_ref, stack_ref = refs
    else:
        st_ref, cx_ref, cy_ref, rows_ref, out_ref, pay_ref, stack_ref = refs
    rows = st_ref.shape[2] // PY
    slot = stack_ref.shape[0] // rows
    levels = st_ref.shape[1]
    north = rows_ref[0, :, 0:PY]
    south = rows_ref[0, :, PY : 2 * PY]
    sides = rows_ref[0, :, 2 * PY : 3 * PY]
    lane = lax.broadcasted_iota(jnp.int32, north.shape, 1)
    stack_ref[...] = jnp.zeros(stack_ref.shape, stack_ref.dtype)
    for x in range(rows):
        here = slice(x * PY, (x + 1) * PY)
        cur = st_ref[0, :, here]
        up = north if x == 0 else st_ref[0, :, (x - 1) * PY : x * PY]
        down = south if x == rows - 1 else st_ref[0, :, (x + 1) * PY : (x + 2) * PY]
        side = pltpu.roll(sides, (PY - 2 * x) % PY, 1)
        west = jnp.where(lane == 0, side, pltpu.roll(cur, 1, 1))
        east = jnp.where(lane == PY - 1, side, pltpu.roll(cur, PY - 1, 1))
        along_x = cx_ref[:, here]
        along_y = cy_ref[:, here]
        val = (
            cur
            - 0.5 * along_x * (down - up)
            - 0.5 * along_y * (east - west)
            + KAPPA * (up + down + west + east - 4.0 * cur)
        )
        if with_tend:
            quarter = rows // tend_ref.shape[0]
            block = tend_ref[x // quarter, 0, 0:levels, (x % quarter) * PY : (x % quarter + 1) * PY]
            val = val + PHYS_DT * block.astype(jnp.float32)
        out_ref[0, :, here] = val
        packed = val.astype(jnp.bfloat16)
        stack_ref[x * slot : x * slot + levels, :] = packed
        if x == 0:
            pay_ref[0, 0:levels, 0:PY] = packed
        if x == rows - 1:
            pay_ref[0, 0:levels, PY : 2 * PY] = packed
    finish_payload(pay_ref, stack_ref, levels)


def finish_payload(pay_ref, stack_ref, levels):
    pad_rows = pay_ref.shape[1] - levels
    if pad_rows:
        pay_ref[0, levels:, 0 : 2 * PY] = jnp.zeros((pad_rows, 2 * PY), pay_ref.dtype)
    chunks = stack_ref.shape[0] // PY
    pick_row = lax.broadcasted_iota(jnp.int32, (2 * chunks, PY), 0)
    pick_lane = lax.broadcasted_iota(jnp.int32, (2 * chunks, PY), 1)
    cols = jnp.zeros((2 * chunks, PY), jnp.float32)
    for j in range(chunks):
        picker = (
            ((pick_row == 2 * j) & (pick_lane == 0)) | ((pick_row == 2 * j + 1) & (pick_lane == PY - 1))
        ).astype(jnp.bfloat16)
        cols = cols + lax.dot_general(
            picker,
            stack_ref[j * PY : (j + 1) * PY, :],
            (((1,), (1,)), ((), ())),
            preferred_element_type=jnp.float32,
        )
    pay_ref[0, :, 2 * PY : 3 * PY] = cols.astype(pay_ref.dtype)


def stencil(tracer, along_x, along_y, halo, tend):
    n_vars, levels, width = tracer.shape
    rows = width // PY
    slot = 16
    with_tend = tend is not None
    in_specs = [
        pl.BlockSpec((1, levels, width), lambda v: (v, 0, 0)),
        pl.BlockSpec((levels, width), lambda v: (0, 0)),
        pl.BlockSpec((levels, width), lambda v: (0, 0)),
        pl.BlockSpec((1, levels, 3 * PY), lambda v: (v, 0, 0)),
    ]
    args = [tracer, along_x, along_y, halo]
    if with_tend:
        in_specs.append(pl.BlockSpec((tend.shape[0], 1) + tend.shape[2:], lambda v: (0, v, 0, 0)))
        args.append(tend)
    return pl.pallas_call(
        functools.partial(stencil_kernel, with_tend=with_tend),
        grid=(n_vars,),
        in_specs=in_specs,
        out_specs=[
            pl.BlockSpec((1, levels, width), lambda v: (v, 0, 0)),
            pl.BlockSpec((1, slot, 3 * PY), lambda v: (v, 0, 0)),
        ],
        out_shape=[
            jax.ShapeDtypeStruct(tracer.shape, jnp.float32),
            jax.ShapeDtypeStruct((n_vars, slot, 3 * PY), jnp.bfloat16),
        ],
        scratch_shapes=[pltpu.VMEM((rows * slot, PY), jnp.bfloat16)],
        cost_estimate=pl.CostEstimate(
            flops=20 * tracer.size, transcendentals=0, bytes_accessed=4 * (2 * tracer.size + 2 * along_x.size)
        ),
    )(*args)


def pack_kernel(st_ref, surf_ref, pay_ref, feat_ref, stack_ref, *, n_surf):
    rows = st_ref.shape[2] // PY
    slot = stack_ref.shape[0] // rows
    levels = st_ref.shape[1]
    keep_surface = pl.program_id(0) < n_surf
    stack_ref[...] = jnp.zeros(stack_ref.shape, stack_ref.dtype)
    for x in range(rows):
        here = slice(x * PY, (x + 1) * PY)
        packed = st_ref[0, :, here].astype(jnp.bfloat16)
        stack_ref[x * slot : x * slot + levels, :] = packed
        feat_ref[x, 0, 0:levels, :] = packed
        surf_row = surf_ref[0, :, here]
        feat_ref[x, 0, levels : levels + 1, :] = jnp.where(keep_surface, surf_row, jnp.zeros_like(surf_row))
        if x == 0:
            pay_ref[0, 0:levels, 0:PY] = packed
        if x == rows - 1:
            pay_ref[0, 0:levels, PY : 2 * PY] = packed
    finish_payload(pay_ref, stack_ref, levels)


def first_edges(tracer, surface):
    n_vars, levels, width = tracer.shape
    n_surf = surface.shape[0]
    rows = width // PY
    slot = 16
    surf_rows = surface.reshape(n_surf, 1, width)
    return pl.pallas_call(
        functools.partial(pack_kernel, n_surf=n_surf),
        grid=(n_vars,),
        in_specs=[
            pl.BlockSpec((1, levels, width), lambda v: (v, 0, 0)),
            pl.BlockSpec((1, 1, width), lambda v: (jnp.minimum(v, n_surf - 1), 0, 0)),
        ],
        out_specs=[
            pl.BlockSpec((1, slot, 3 * PY), lambda v: (v, 0, 0)),
            pl.BlockSpec((rows, 1, slot, PY), lambda v: (0, v, 0, 0)),
        ],
        out_shape=[
            jax.ShapeDtypeStruct((n_vars, slot, 3 * PY), jnp.bfloat16),
            jax.ShapeDtypeStruct((rows, n_vars, slot, PY), jnp.bfloat16),
        ],
        scratch_shapes=[pltpu.VMEM((rows * slot, PY), jnp.bfloat16)],
        cost_estimate=pl.CostEstimate(flops=0, transcendentals=0, bytes_accessed=5 * tracer.size),
    )(tracer, surf_rows)


def exchange_halo(payload, beside_all, patches, levels):
    n_vars, slot, _ = payload.shape
    rows = PX
    chunk_rows = PY // slot
    got = lax.all_gather(payload, "patch", axis=0, tiled=False)
    north = jnp.take(got, beside_all[0], axis=0)[:, 0:levels, PY : 2 * PY]
    south = jnp.take(got, beside_all[1], axis=0)[:, 0:levels, 0:PY]

    def column(patch, which):
        cols = jnp.take(got, patch, axis=0)[..., 2 * PY : 3 * PY]
        cols = cols.reshape(n_vars, rows // chunk_rows, 2, chunk_rows, slot)[:, :, which]
        return cols.transpose(0, 3, 1, 2).reshape(n_vars, slot, rows)[:, 0:levels]

    west = column(beside_all[2], 1)
    east = column(beside_all[3], 0)
    sides = jnp.stack([west, jnp.roll(east, -1, axis=-1)], axis=-1).reshape(west.shape[:-1] + (2 * rows,))
    return jnp.concatenate([north, south, sides], axis=-1).astype(jnp.float32)


def activate(pre_act):
    return jax.nn.silu(pre_act).astype(jnp.bfloat16)


def hidden_layers(hidden, b_hidden, w_mid):
    for layer_index in range(w_mid.shape[0]):
        pre_act = (
            jnp.einsum(
                "...h,hj->...j", hidden, w_mid[layer_index], preferred_element_type=jnp.float32
            )
            + b_hidden[layer_index + 1]
        )
        hidden = activate(pre_act)
    return hidden


def on_device(
    state, courant_x, courant_y, surface, w_in, b_hidden, w_mid, w_out, owner_map, neighbours
):
    groups = lax.axis_size("grp")
    patches = lax.axis_size("patch")
    group_here = lax.axis_index("grp")
    patch_here = lax.axis_index("patch")
    level_share = LEV // groups
    surf_share = SURF // groups
    feat_share = VARS * level_share + surf_share
    quarter_rows = PX // groups
    capacity = max(2, 2 * quarter_rows // patches)
    slot_count = patches * capacity
    slot = 16
    beside_all = jnp.take(neighbours, patch_here, axis=0)
    payload, feat = first_edges(state, surface)
    by_quarter = feat.reshape(groups, quarter_rows, VARS * slot, PY)
    owners_all = owner_map.reshape(patches, groups, quarter_rows)
    owners_here = jnp.take(owners_all, patch_here, axis=0)
    matches = (owners_here[..., None] == jnp.arange(patches, dtype=jnp.int32)).astype(jnp.int32)
    slot_rank = jnp.sum((jnp.cumsum(matches, axis=1) - matches) * matches, axis=2)
    slot_index = owners_here * capacity + slot_rank
    selector = (
        slot_index[:, None, :] == jnp.arange(slot_count, dtype=jnp.int32)[None, :, None]
    ).astype(jnp.bfloat16)
    selector_here = jnp.take(selector, group_here, axis=0)
    state_part = w_in[: VARS * LEV].reshape(VARS, groups, level_share, -1).transpose(1, 0, 2, 3)
    state_part = jnp.pad(state_part, ((0, 0), (0, 0), (0, slot - level_share), (0, 0)))
    surf_part = w_in[VARS * LEV :].reshape(groups, surf_share, -1)
    w_local = state_part.at[:, :surf_share, level_share, :].set(surf_part).reshape(groups, VARS * slot, -1)
    w_split = w_out.reshape(-1, VARS, groups, level_share)
    regrouped = lax.all_to_all(by_quarter, "grp", split_axis=0, concat_axis=0, tiled=True)
    pre_act = (
        jnp.einsum("gbfc,gfh->bch", regrouped, w_local, preferred_element_type=jnp.float32)
        + b_hidden[0]
    )
    hidden = hidden_layers(activate(pre_act), b_hidden, w_mid)
    w_pad = jnp.pad(w_split, ((0, 0), (0, 0), (0, 0), (0, slot - level_share)))
    w_rows = w_pad.transpose(2, 1, 3, 0).reshape(groups * VARS * slot, -1)
    hidden_flat = hidden.reshape(quarter_rows * PY, -1)
    tendency = lax.dot_general(
        w_rows, hidden_flat, (((1,), (1,)), ((), ())), preferred_element_type=jnp.float32
    ).astype(jnp.bfloat16)
    tendency = tendency.reshape(groups, VARS, slot, quarter_rows * PY)
    heating = HEAT_WEIGHT * jnp.sum(
        tendency[:, 0, 0:level_share].astype(jnp.float32), axis=(0, 1)
    ).reshape(quarter_rows, PY)
    packed = jnp.dot(
        selector_here.astype(jnp.float32), heating, precision=lax.Precision.HIGHEST
    ).reshape(patches, capacity, PY)
    owner_heating = lax.all_to_all(
        packed, "patch", split_axis=0, concat_axis=0, tiled=True
    ).reshape(slot_count, PY)
    tendency_here = lax.all_to_all(tendency, "grp", split_axis=0, concat_axis=0, tiled=True)
    advected = state
    for section_index in range(SUBSTEPS):
        halo = exchange_halo(payload, beside_all, patches, level_share)
        last = section_index == SUBSTEPS - 1
        advected, payload = stencil(
            advected, courant_x, courant_y, halo, tendency_here if last else None
        )
    new_state = advected
    return (new_state, owner_heating)


def solution(mesh):
    placed = (
        P(None, "grp", "patch"),
        P("grp", "patch"),
        P("grp", "patch"),
        P("grp", "patch"),
        P(),
        P(),
        P(),
        P(),
        P(),
        P(),
    )
    return jax.shard_map(
        on_device,
        mesh=mesh,
        in_specs=placed,
        out_specs=(P(None, "grp", "patch"), P("grp", "patch")),
        check_vma=False,
    )
```

```python
import functools

import jax
import jax.numpy as jnp
from jax import lax
from jax.experimental import pallas as pl
from jax.experimental.pallas import tpu as pltpu
from jax.sharding import PartitionSpec as P

VARS = 9
LEV = 60
SURF = 16
SUBSTEPS = 3
PY = 128
PX = 64


KAPPA = 0.24
PHYS_DT = 0.05
HEAT_WEIGHT = 0.125


def stencil_kernel(*refs, with_tend):
    if with_tend:
        st_ref, cx_ref, cy_ref, rows_ref, tend_ref, out_ref, pay_ref, stack_ref = refs
    else:
        st_ref, cx_ref, cy_ref, rows_ref, out_ref, pay_ref, stack_ref = refs
    rows = st_ref.shape[2] // PY
    slot = stack_ref.shape[0] // rows
    levels = st_ref.shape[1]
    north = rows_ref[0, :, 0:PY]
    south = rows_ref[0, :, PY : 2 * PY]
    sides = rows_ref[0, :, 2 * PY : 3 * PY]
    lane = lax.broadcasted_iota(jnp.int32, north.shape, 1)
    stack_ref[...] = jnp.zeros(stack_ref.shape, stack_ref.dtype)
    for x in range(rows):
        here = slice(x * PY, (x + 1) * PY)
        cur = st_ref[0, :, here]
        up = north if x == 0 else st_ref[0, :, (x - 1) * PY : x * PY]
        down = south if x == rows - 1 else st_ref[0, :, (x + 1) * PY : (x + 2) * PY]
        side = pltpu.roll(sides, (PY - 2 * x) % PY, 1)
        west = jnp.where(lane == 0, side, pltpu.roll(cur, 1, 1))
        east = jnp.where(lane == PY - 1, side, pltpu.roll(cur, PY - 1, 1))
        along_x = cx_ref[:, here]
        along_y = cy_ref[:, here]
        val = (
            cur
            - 0.5 * along_x * (down - up)
            - 0.5 * along_y * (east - west)
            + KAPPA * (up + down + west + east - 4.0 * cur)
        )
        if with_tend:
            quarter = rows // tend_ref.shape[0]
            block = tend_ref[x // quarter, 0, 0:levels, (x % quarter) * PY : (x % quarter + 1) * PY]
            val = val + PHYS_DT * block.astype(jnp.float32)
        out_ref[0, :, here] = val
        packed = val.astype(jnp.bfloat16)
        stack_ref[x * slot : x * slot + levels, :] = packed
        if x == 0:
            pay_ref[0, 0:levels, 0:PY] = packed
        if x == rows - 1:
            pay_ref[0, 0:levels, PY : 2 * PY] = packed
    finish_payload(pay_ref, stack_ref, levels)


def finish_payload(pay_ref, stack_ref, levels):
    pad_rows = pay_ref.shape[1] - levels
    if pad_rows:
        pay_ref[0, levels:, 0 : 2 * PY] = jnp.zeros((pad_rows, 2 * PY), pay_ref.dtype)
    chunks = stack_ref.shape[0] // PY
    pick_row = lax.broadcasted_iota(jnp.int32, (2 * chunks, PY), 0)
    pick_lane = lax.broadcasted_iota(jnp.int32, (2 * chunks, PY), 1)
    cols = jnp.zeros((2 * chunks, PY), jnp.float32)
    for j in range(chunks):
        picker = (
            ((pick_row == 2 * j) & (pick_lane == 0)) | ((pick_row == 2 * j + 1) & (pick_lane == PY - 1))
        ).astype(jnp.bfloat16)
        cols = cols + lax.dot_general(
            picker,
            stack_ref[j * PY : (j + 1) * PY, :],
            (((1,), (1,)), ((), ())),
            preferred_element_type=jnp.float32,
        )
    pay_ref[0, :, 2 * PY : 3 * PY] = cols.astype(pay_ref.dtype)


def stencil(tracer, along_x, along_y, halo, tend):
    n_vars, levels, width = tracer.shape
    rows = width // PY
    slot = 16
    with_tend = tend is not None
    in_specs = [
        pl.BlockSpec((1, levels, width), lambda v: (v, 0, 0)),
        pl.BlockSpec((levels, width), lambda v: (0, 0)),
        pl.BlockSpec((levels, width), lambda v: (0, 0)),
        pl.BlockSpec((1, levels, 3 * PY), lambda v: (v, 0, 0)),
    ]
    args = [tracer, along_x, along_y, halo]
    if with_tend:
        in_specs.append(pl.BlockSpec((tend.shape[0], 1) + tend.shape[2:], lambda v: (0, v, 0, 0)))
        args.append(tend)
    return pl.pallas_call(
        functools.partial(stencil_kernel, with_tend=with_tend),
        grid=(n_vars,),
        in_specs=in_specs,
        out_specs=[
            pl.BlockSpec((1, levels, width), lambda v: (v, 0, 0)),
            pl.BlockSpec((1, slot, 3 * PY), lambda v: (v, 0, 0)),
        ],
        out_shape=[
            jax.ShapeDtypeStruct(tracer.shape, jnp.float32),
            jax.ShapeDtypeStruct((n_vars, slot, 3 * PY), jnp.bfloat16),
        ],
        scratch_shapes=[pltpu.VMEM((rows * slot, PY), jnp.bfloat16)],
        cost_estimate=pl.CostEstimate(
            flops=20 * tracer.size, transcendentals=0, bytes_accessed=4 * (2 * tracer.size + 2 * along_x.size)
        ),
    )(*args)


def pack_kernel(st_ref, surf_ref, pay_ref, feat_ref, stack_ref, *, n_surf):
    rows = st_ref.shape[2] // PY
    slot = stack_ref.shape[0] // rows
    levels = st_ref.shape[1]
    keep_surface = pl.program_id(0) < n_surf
    stack_ref[...] = jnp.zeros(stack_ref.shape, stack_ref.dtype)
    for x in range(rows):
        here = slice(x * PY, (x + 1) * PY)
        packed = st_ref[0, :, here].astype(jnp.bfloat16)
        stack_ref[x * slot : x * slot + levels, :] = packed
        feat_ref[x, 0, 0:levels, :] = packed
        surf_row = surf_ref[0, :, here]
        feat_ref[x, 0, levels : levels + 1, :] = jnp.where(keep_surface, surf_row, jnp.zeros_like(surf_row))
        if x == 0:
            pay_ref[0, 0:levels, 0:PY] = packed
        if x == rows - 1:
            pay_ref[0, 0:levels, PY : 2 * PY] = packed
    finish_payload(pay_ref, stack_ref, levels)


def first_edges(tracer, surface):
    n_vars, levels, width = tracer.shape
    n_surf = surface.shape[0]
    rows = width // PY
    slot = 16
    surf_rows = surface.reshape(n_surf, 1, width)
    return pl.pallas_call(
        functools.partial(pack_kernel, n_surf=n_surf),
        grid=(n_vars,),
        in_specs=[
            pl.BlockSpec((1, levels, width), lambda v: (v, 0, 0)),
            pl.BlockSpec((1, 1, width), lambda v: (jnp.minimum(v, n_surf - 1), 0, 0)),
        ],
        out_specs=[
            pl.BlockSpec((1, slot, 3 * PY), lambda v: (v, 0, 0)),
            pl.BlockSpec((rows, 1, slot, PY), lambda v: (0, v, 0, 0)),
        ],
        out_shape=[
            jax.ShapeDtypeStruct((n_vars, slot, 3 * PY), jnp.bfloat16),
            jax.ShapeDtypeStruct((rows, n_vars, slot, PY), jnp.bfloat16),
        ],
        scratch_shapes=[pltpu.VMEM((rows * slot, PY), jnp.bfloat16)],
        cost_estimate=pl.CostEstimate(flops=0, transcendentals=0, bytes_accessed=5 * tracer.size),
    )(tracer, surf_rows)


def exchange_halo(payload, beside_all, patches, levels):
    n_vars, slot, _ = payload.shape
    rows = PX
    chunk_rows = PY // slot
    got = lax.all_gather(payload, "patch", axis=0, tiled=False)
    north = jnp.take(got, beside_all[0], axis=0)[:, 0:levels, PY : 2 * PY]
    south = jnp.take(got, beside_all[1], axis=0)[:, 0:levels, 0:PY]

    def column(patch, which):
        cols = jnp.take(got, patch, axis=0)[..., 2 * PY : 3 * PY]
        cols = cols.reshape(n_vars, rows // chunk_rows, 2, chunk_rows, slot)[:, :, which]
        return cols.transpose(0, 3, 1, 2).reshape(n_vars, slot, rows)[:, 0:levels]

    west = column(beside_all[2], 1)
    east = column(beside_all[3], 0)
    sides = jnp.stack([west, jnp.roll(east, -1, axis=-1)], axis=-1).reshape(west.shape[:-1] + (2 * rows,))
    return jnp.concatenate([north, south, sides], axis=-1).astype(jnp.float32)


def activate(pre_act):
    return jax.nn.silu(pre_act).astype(jnp.bfloat16)


def hidden_layers(hidden, b_hidden, w_mid):
    for layer_index in range(w_mid.shape[0]):
        pre_act = (
            jnp.einsum(
                "...h,hj->...j", hidden, w_mid[layer_index], preferred_element_type=jnp.float32
            )
            + b_hidden[layer_index + 1]
        )
        hidden = activate(pre_act)
    return hidden


def on_device(
    state, courant_x, courant_y, surface, w_in, b_hidden, w_mid, w_out, owner_map, neighbours
):
    groups = lax.axis_size("grp")
    patches = lax.axis_size("patch")
    group_here = lax.axis_index("grp")
    patch_here = lax.axis_index("patch")
    level_share = LEV // groups
    surf_share = SURF // groups
    feat_share = VARS * level_share + surf_share
    quarter_rows = PX // groups
    capacity = max(2, 2 * quarter_rows // patches)
    slot_count = patches * capacity
    slot = 16
    beside_all = jnp.take(neighbours, patch_here, axis=0)
    owners_all = owner_map.reshape(patches, groups, quarter_rows)
    owners_here = jnp.take(owners_all, patch_here, axis=0)
    matches = (owners_here[..., None] == jnp.arange(patches, dtype=jnp.int32)).astype(jnp.int32)
    slot_rank = jnp.sum((jnp.cumsum(matches, axis=1) - matches) * matches, axis=2)
    slot_index = owners_here * capacity + slot_rank
    selector = (
        slot_index[:, None, :] == jnp.arange(slot_count, dtype=jnp.int32)[None, :, None]
    ).astype(jnp.bfloat16)
    selector_here = jnp.take(selector, group_here, axis=0)
    state_part = w_in[: VARS * LEV].reshape(VARS, groups, level_share, -1).transpose(1, 0, 2, 3)
    state_part = jnp.pad(state_part, ((0, 0), (0, 0), (0, slot - level_share), (0, 0)))
    surf_part = w_in[VARS * LEV :].reshape(groups, surf_share, -1)
    w_local = state_part.at[:, :surf_share, level_share, :].set(surf_part).reshape(groups, VARS * slot, -1)
    w_split = w_out.reshape(-1, VARS, groups, level_share)
    w_pad = jnp.pad(w_split, ((0, 0), (0, 0), (0, 0), (0, slot - level_share)))
    w_rows = w_pad.transpose(2, 1, 3, 0).reshape(groups * VARS * slot, -1)
    w_local, w_rows, state_in = lax.optimization_barrier((w_local, w_rows, state))
    payload, feat = first_edges(state_in, surface)
    by_quarter = feat.reshape(groups, quarter_rows, VARS * slot, PY)
    regrouped = lax.all_to_all(by_quarter, "grp", split_axis=0, concat_axis=0, tiled=True)
    pre_act = (
        jnp.einsum("gbfc,gfh->bch", regrouped, w_local, preferred_element_type=jnp.float32)
        + b_hidden[0]
    )
    hidden = hidden_layers(activate(pre_act), b_hidden, w_mid)
    hidden_flat = hidden.reshape(quarter_rows * PY, -1)
    tendency = lax.dot_general(
        w_rows, hidden_flat, (((1,), (1,)), ((), ())), preferred_element_type=jnp.float32
    ).astype(jnp.bfloat16)
    tendency = tendency.reshape(groups, VARS, slot, quarter_rows * PY)
    heating = HEAT_WEIGHT * jnp.sum(
        tendency[:, 0, 0:level_share].astype(jnp.float32), axis=(0, 1)
    ).reshape(quarter_rows, PY)
    packed = jnp.dot(
        selector_here.astype(jnp.float32), heating, precision=lax.Precision.HIGHEST
    ).reshape(patches, capacity, PY)
    owner_heating = lax.all_to_all(
        packed, "patch", split_axis=0, concat_axis=0, tiled=True
    ).reshape(slot_count, PY)
    tendency_here = lax.all_to_all(tendency, "grp", split_axis=0, concat_axis=0, tiled=True)
    advected = state
    for section_index in range(SUBSTEPS):
        halo = exchange_halo(payload, beside_all, patches, level_share)
        last = section_index == SUBSTEPS - 1
        advected, payload = stencil(
            advected, courant_x, courant_y, halo, tendency_here if last else None
        )
    new_state = advected
    return (new_state, owner_heating)


def solution(mesh):
    placed = (
        P(None, "grp", "patch"),
        P("grp", "patch"),
        P("grp", "patch"),
        P("grp", "patch"),
        P(),
        P(),
        P(),
        P(),
        P(),
        P(),
    )
    return jax.shard_map(
        on_device,
        mesh=mesh,
        in_specs=placed,
        out_specs=(P(None, "grp", "patch"), P("grp", "patch")),
        check_vma=False,
    )
```

```python
import functools

import jax
import jax.numpy as jnp
from jax import lax
from jax.experimental import pallas as pl
from jax.experimental.pallas import tpu as pltpu
from jax.sharding import PartitionSpec as P

VARS = 9
LEV = 60
SURF = 16
SUBSTEPS = 3
PY = 128
PX = 64


KAPPA = 0.24
PHYS_DT = 0.05
HEAT_WEIGHT = 0.125


def stencil_kernel(*refs, with_tend):
    if with_tend:
        st_ref, cx_ref, cy_ref, rows_ref, tend_ref, out_ref, pay_ref, stack_ref = refs
    else:
        st_ref, cx_ref, cy_ref, rows_ref, out_ref, pay_ref, stack_ref = refs
    rows = st_ref.shape[2] // PY
    slot = stack_ref.shape[0] // rows
    levels = st_ref.shape[1]
    north = rows_ref[0, :, 0:PY]
    south = rows_ref[0, :, PY : 2 * PY]
    sides = rows_ref[0, :, 2 * PY : 3 * PY]
    lane = lax.broadcasted_iota(jnp.int32, north.shape, 1)
    stack_ref[...] = jnp.zeros(stack_ref.shape, stack_ref.dtype)
    for x in range(rows):
        here = slice(x * PY, (x + 1) * PY)
        cur = st_ref[0, :, here]
        up = north if x == 0 else st_ref[0, :, (x - 1) * PY : x * PY]
        down = south if x == rows - 1 else st_ref[0, :, (x + 1) * PY : (x + 2) * PY]
        side = pltpu.roll(sides, (PY - 2 * x) % PY, 1)
        west = jnp.where(lane == 0, side, pltpu.roll(cur, 1, 1))
        east = jnp.where(lane == PY - 1, side, pltpu.roll(cur, PY - 1, 1))
        along_x = cx_ref[:, here]
        along_y = cy_ref[:, here]
        val = (
            cur
            - 0.5 * along_x * (down - up)
            - 0.5 * along_y * (east - west)
            + KAPPA * (up + down + west + east - 4.0 * cur)
        )
        if with_tend:
            quarter = rows // tend_ref.shape[0]
            block = tend_ref[x // quarter, 0, 0:levels, (x % quarter) * PY : (x % quarter + 1) * PY]
            val = val + PHYS_DT * block.astype(jnp.float32)
        out_ref[0, :, here] = val
        packed = val.astype(jnp.bfloat16)
        stack_ref[x * slot : x * slot + levels, :] = packed
        if x == 0:
            pay_ref[0, 0:levels, 0:PY] = packed
        if x == rows - 1:
            pay_ref[0, 0:levels, PY : 2 * PY] = packed
    finish_payload(pay_ref, stack_ref, levels)


def finish_payload(pay_ref, stack_ref, levels):
    pad_rows = pay_ref.shape[1] - levels
    if pad_rows:
        pay_ref[0, levels:, 0 : 2 * PY] = jnp.zeros((pad_rows, 2 * PY), pay_ref.dtype)
    chunks = stack_ref.shape[0] // PY
    pick_row = lax.broadcasted_iota(jnp.int32, (2 * chunks, PY), 0)
    pick_lane = lax.broadcasted_iota(jnp.int32, (2 * chunks, PY), 1)
    cols = jnp.zeros((2 * chunks, PY), jnp.float32)
    for j in range(chunks):
        picker = (
            ((pick_row == 2 * j) & (pick_lane == 0)) | ((pick_row == 2 * j + 1) & (pick_lane == PY - 1))
        ).astype(jnp.bfloat16)
        cols = cols + lax.dot_general(
            picker,
            stack_ref[j * PY : (j + 1) * PY, :],
            (((1,), (1,)), ((), ())),
            preferred_element_type=jnp.float32,
        )
    pay_ref[0, :, 2 * PY : 3 * PY] = cols.astype(pay_ref.dtype)


def stencil(tracer, along_x, along_y, halo, tend):
    n_vars, levels, width = tracer.shape
    rows = width // PY
    slot = 16
    with_tend = tend is not None
    in_specs = [
        pl.BlockSpec((1, levels, width), lambda v: (v, 0, 0)),
        pl.BlockSpec((levels, width), lambda v: (0, 0)),
        pl.BlockSpec((levels, width), lambda v: (0, 0)),
        pl.BlockSpec((1, levels, 3 * PY), lambda v: (v, 0, 0)),
    ]
    args = [tracer, along_x, along_y, halo]
    if with_tend:
        in_specs.append(pl.BlockSpec((tend.shape[0], 1) + tend.shape[2:], lambda v: (0, v, 0, 0)))
        args.append(tend)
    return pl.pallas_call(
        functools.partial(stencil_kernel, with_tend=with_tend),
        grid=(n_vars,),
        in_specs=in_specs,
        out_specs=[
            pl.BlockSpec((1, levels, width), lambda v: (v, 0, 0)),
            pl.BlockSpec((1, slot, 3 * PY), lambda v: (v, 0, 0)),
        ],
        out_shape=[
            jax.ShapeDtypeStruct(tracer.shape, jnp.float32),
            jax.ShapeDtypeStruct((n_vars, slot, 3 * PY), jnp.bfloat16),
        ],
        scratch_shapes=[pltpu.VMEM((rows * slot, PY), jnp.bfloat16)],
        cost_estimate=pl.CostEstimate(
            flops=20 * tracer.size, transcendentals=0, bytes_accessed=4 * (2 * tracer.size + 2 * along_x.size)
        ),
    )(*args)


def pack_kernel(st_ref, surf_ref, pay_ref, feat_ref, stack_ref, *, n_surf):
    rows = st_ref.shape[2] // PY
    slot = stack_ref.shape[0] // rows
    levels = st_ref.shape[1]
    keep_surface = pl.program_id(0) < n_surf
    stack_ref[...] = jnp.zeros(stack_ref.shape, stack_ref.dtype)
    for x in range(rows):
        here = slice(x * PY, (x + 1) * PY)
        packed = st_ref[0, :, here].astype(jnp.bfloat16)
        stack_ref[x * slot : x * slot + levels, :] = packed
        feat_ref[x, 0, 0:levels, :] = packed
        surf_row = surf_ref[0, :, here]
        feat_ref[x, 0, levels : levels + 1, :] = jnp.where(keep_surface, surf_row, jnp.zeros_like(surf_row))
        if x == 0:
            pay_ref[0, 0:levels, 0:PY] = packed
        if x == rows - 1:
            pay_ref[0, 0:levels, PY : 2 * PY] = packed
    finish_payload(pay_ref, stack_ref, levels)


def first_edges(tracer, surface):
    n_vars, levels, width = tracer.shape
    n_surf = surface.shape[0]
    rows = width // PY
    slot = 16
    surf_rows = surface.reshape(n_surf, 1, width)
    return pl.pallas_call(
        functools.partial(pack_kernel, n_surf=n_surf),
        grid=(n_vars,),
        in_specs=[
            pl.BlockSpec((1, levels, width), lambda v: (v, 0, 0)),
            pl.BlockSpec((1, 1, width), lambda v: (jnp.minimum(v, n_surf - 1), 0, 0)),
        ],
        out_specs=[
            pl.BlockSpec((1, slot, 3 * PY), lambda v: (v, 0, 0)),
            pl.BlockSpec((rows, 1, slot, PY), lambda v: (0, v, 0, 0)),
        ],
        out_shape=[
            jax.ShapeDtypeStruct((n_vars, slot, 3 * PY), jnp.bfloat16),
            jax.ShapeDtypeStruct((rows, n_vars, slot, PY), jnp.bfloat16),
        ],
        scratch_shapes=[pltpu.VMEM((rows * slot, PY), jnp.bfloat16)],
        cost_estimate=pl.CostEstimate(flops=0, transcendentals=0, bytes_accessed=5 * tracer.size),
    )(tracer, surf_rows)


def exchange_halo(payload, beside_all, patches, levels):
    n_vars, slot, _ = payload.shape
    rows = PX
    chunk_rows = PY // slot
    got = lax.all_gather(payload, "patch", axis=0, tiled=False)
    north = jnp.take(got, beside_all[0], axis=0)[:, 0:levels, PY : 2 * PY]
    south = jnp.take(got, beside_all[1], axis=0)[:, 0:levels, 0:PY]

    def column(patch, which):
        cols = jnp.take(got, patch, axis=0)[..., 2 * PY : 3 * PY]
        cols = cols.reshape(n_vars, rows // chunk_rows, 2, chunk_rows, slot)[:, :, which]
        return cols.transpose(0, 3, 1, 2).reshape(n_vars, slot, rows)[:, 0:levels]

    west = column(beside_all[2], 1)
    east = column(beside_all[3], 0)
    sides = jnp.stack([west, jnp.roll(east, -1, axis=-1)], axis=-1).reshape(west.shape[:-1] + (2 * rows,))
    return jnp.concatenate([north, south, sides], axis=-1).astype(jnp.float32)


def activate(pre_act):
    return jax.nn.silu(pre_act).astype(jnp.bfloat16)


def hidden_layers(hidden, b_hidden, w_mid):
    for layer_index in range(w_mid.shape[0]):
        pre_act = (
            jnp.einsum(
                "...h,hj->...j", hidden, w_mid[layer_index], preferred_element_type=jnp.float32
            )
            + b_hidden[layer_index + 1]
        )
        hidden = activate(pre_act)
    return hidden


def on_device(
    state, courant_x, courant_y, surface, w_in, b_hidden, w_mid, w_out, owner_map, neighbours
):
    groups = lax.axis_size("grp")
    patches = lax.axis_size("patch")
    group_here = lax.axis_index("grp")
    patch_here = lax.axis_index("patch")
    level_share = LEV // groups
    surf_share = SURF // groups
    feat_share = VARS * level_share + surf_share
    quarter_rows = PX // groups
    capacity = max(2, 2 * quarter_rows // patches)
    slot_count = patches * capacity
    slot = 16
    beside_all = jnp.take(neighbours, patch_here, axis=0)
    owners_all = owner_map.reshape(patches, groups, quarter_rows)
    owners_here = jnp.take(owners_all, patch_here, axis=0)
    matches = (owners_here[..., None] == jnp.arange(patches, dtype=jnp.int32)).astype(jnp.int32)
    slot_rank = jnp.sum((jnp.cumsum(matches, axis=1) - matches) * matches, axis=2)
    slot_index = owners_here * capacity + slot_rank
    selector = (
        slot_index[:, None, :] == jnp.arange(slot_count, dtype=jnp.int32)[None, :, None]
    ).astype(jnp.bfloat16)
    selector_here = jnp.take(selector, group_here, axis=0)
    state_part = w_in[: VARS * LEV].reshape(VARS, groups, level_share, -1).transpose(1, 0, 2, 3)
    state_part = jnp.pad(state_part, ((0, 0), (0, 0), (0, slot - level_share), (0, 0)))
    surf_part = w_in[VARS * LEV :].reshape(groups, surf_share, -1)
    w_local = state_part.at[:, :surf_share, level_share, :].set(surf_part).reshape(groups, VARS * slot, -1)
    w_split = w_out.reshape(-1, VARS, groups, level_share)
    w_pad = jnp.pad(w_split, ((0, 0), (0, 0), (0, 0), (0, slot - level_share)))
    w_rows = w_pad.transpose(2, 1, 3, 0).reshape(groups * VARS * slot, -1)
    w_local, w_rows, selector_here, beside_all, state_in = lax.optimization_barrier(
        (w_local, w_rows, selector_here, beside_all, state)
    )
    payload, feat = first_edges(state_in, surface)
    by_quarter = feat.reshape(groups, quarter_rows, VARS * slot, PY)
    regrouped = lax.all_to_all(by_quarter, "grp", split_axis=0, concat_axis=0, tiled=True)
    pre_act = (
        jnp.einsum("gbfc,gfh->bch", regrouped, w_local, preferred_element_type=jnp.float32)
        + b_hidden[0]
    )
    hidden = hidden_layers(activate(pre_act), b_hidden, w_mid)
    hidden_flat = hidden.reshape(quarter_rows * PY, -1)
    tendency = lax.dot_general(
        w_rows, hidden_flat, (((1,), (1,)), ((), ())), preferred_element_type=jnp.float32
    ).astype(jnp.bfloat16)
    tendency = tendency.reshape(groups, VARS, slot, quarter_rows * PY)
    heating = HEAT_WEIGHT * jnp.sum(
        tendency[:, 0, 0:level_share].astype(jnp.float32), axis=(0, 1)
    ).reshape(quarter_rows, PY)
    packed = jnp.dot(
        selector_here.astype(jnp.float32), heating, precision=lax.Precision.HIGHEST
    ).reshape(patches, capacity, PY)
    owner_heating = lax.all_to_all(
        packed, "patch", split_axis=0, concat_axis=0, tiled=True
    ).reshape(slot_count, PY)
    tendency_here = lax.all_to_all(tendency, "grp", split_axis=0, concat_axis=0, tiled=True)
    advected = state
    for section_index in range(SUBSTEPS):
        halo = exchange_halo(payload, beside_all, patches, level_share)
        last = section_index == SUBSTEPS - 1
        advected, payload = stencil(
            advected, courant_x, courant_y, halo, tendency_here if last else None
        )
    new_state = advected
    return (new_state, owner_heating)


def solution(mesh):
    placed = (
        P(None, "grp", "patch"),
        P("grp", "patch"),
        P("grp", "patch"),
        P("grp", "patch"),
        P(),
        P(),
        P(),
        P(),
        P(),
        P(),
    )
    return jax.shard_map(
        on_device,
        mesh=mesh,
        in_specs=placed,
        out_specs=(P(None, "grp", "patch"), P("grp", "patch")),
        check_vma=False,
    )
```

```python
import functools

import jax
import jax.numpy as jnp
from jax import lax
from jax.experimental import pallas as pl
from jax.experimental.pallas import tpu as pltpu
from jax.sharding import PartitionSpec as P

VARS = 9
LEV = 60
SURF = 16
SUBSTEPS = 3
PY = 128
PX = 64


KAPPA = 0.24
PHYS_DT = 0.05
HEAT_WEIGHT = 0.125


def stencil_kernel(*refs, with_tend):
    if with_tend:
        st_ref, cx_ref, cy_ref, rows_ref, tend_ref, out_ref, pay_ref, stack_ref = refs
    else:
        st_ref, cx_ref, cy_ref, rows_ref, out_ref, pay_ref, stack_ref = refs
    rows = st_ref.shape[2] // PY
    slot = stack_ref.shape[0] // rows
    levels = st_ref.shape[1]
    north = rows_ref[0, :, 0:PY]
    south = rows_ref[0, :, PY : 2 * PY]
    sides = rows_ref[0, :, 2 * PY : 3 * PY]
    lane = lax.broadcasted_iota(jnp.int32, north.shape, 1)
    stack_ref[...] = jnp.zeros(stack_ref.shape, stack_ref.dtype)
    for x in range(rows):
        here = slice(x * PY, (x + 1) * PY)
        cur = st_ref[0, :, here]
        up = north if x == 0 else st_ref[0, :, (x - 1) * PY : x * PY]
        down = south if x == rows - 1 else st_ref[0, :, (x + 1) * PY : (x + 2) * PY]
        side = pltpu.roll(sides, (PY - 2 * x) % PY, 1)
        west = jnp.where(lane == 0, side, pltpu.roll(cur, 1, 1))
        east = jnp.where(lane == PY - 1, side, pltpu.roll(cur, PY - 1, 1))
        along_x = cx_ref[:, here]
        along_y = cy_ref[:, here]
        val = (
            cur
            - 0.5 * along_x * (down - up)
            - 0.5 * along_y * (east - west)
            + KAPPA * (up + down + west + east - 4.0 * cur)
        )
        if with_tend:
            quarter = rows // tend_ref.shape[0]
            block = tend_ref[x // quarter, 0, 0:levels, (x % quarter) * PY : (x % quarter + 1) * PY]
            val = val + PHYS_DT * block.astype(jnp.float32)
        out_ref[0, :, here] = val
        packed = val.astype(jnp.bfloat16)
        stack_ref[x * slot : x * slot + levels, :] = packed
        if x == 0:
            pay_ref[0, 0:levels, 0:PY] = packed
        if x == rows - 1:
            pay_ref[0, 0:levels, PY : 2 * PY] = packed
    finish_payload(pay_ref, stack_ref, levels)


def finish_payload(pay_ref, stack_ref, levels):
    pad_rows = pay_ref.shape[1] - levels
    if pad_rows:
        pay_ref[0, levels:, 0 : 2 * PY] = jnp.zeros((pad_rows, 2 * PY), pay_ref.dtype)
    chunks = stack_ref.shape[0] // PY
    pick_row = lax.broadcasted_iota(jnp.int32, (2 * chunks, PY), 0)
    pick_lane = lax.broadcasted_iota(jnp.int32, (2 * chunks, PY), 1)
    cols = jnp.zeros((2 * chunks, PY), jnp.float32)
    for j in range(chunks):
        picker = (
            ((pick_row == 2 * j) & (pick_lane == 0)) | ((pick_row == 2 * j + 1) & (pick_lane == PY - 1))
        ).astype(jnp.bfloat16)
        cols = cols + lax.dot_general(
            picker,
            stack_ref[j * PY : (j + 1) * PY, :],
            (((1,), (1,)), ((), ())),
            preferred_element_type=jnp.float32,
        )
    pay_ref[0, :, 2 * PY : 3 * PY] = cols.astype(pay_ref.dtype)


def stencil(tracer, along_x, along_y, halo, tend):
    n_vars, levels, width = tracer.shape
    rows = width // PY
    slot = 16
    with_tend = tend is not None
    in_specs = [
        pl.BlockSpec((1, levels, width), lambda v: (v, 0, 0)),
        pl.BlockSpec((levels, width), lambda v: (0, 0)),
        pl.BlockSpec((levels, width), lambda v: (0, 0)),
        pl.BlockSpec((1, levels, 3 * PY), lambda v: (v, 0, 0)),
    ]
    args = [tracer, along_x, along_y, halo]
    if with_tend:
        in_specs.append(pl.BlockSpec((tend.shape[0], 1) + tend.shape[2:], lambda v: (0, v, 0, 0)))
        args.append(tend)
    return pl.pallas_call(
        functools.partial(stencil_kernel, with_tend=with_tend),
        grid=(n_vars,),
        in_specs=in_specs,
        out_specs=[
            pl.BlockSpec((1, levels, width), lambda v: (v, 0, 0)),
            pl.BlockSpec((1, slot, 3 * PY), lambda v: (v, 0, 0)),
        ],
        out_shape=[
            jax.ShapeDtypeStruct(tracer.shape, jnp.float32),
            jax.ShapeDtypeStruct((n_vars, slot, 3 * PY), jnp.bfloat16),
        ],
        scratch_shapes=[pltpu.VMEM((rows * slot, PY), jnp.bfloat16)],
        cost_estimate=pl.CostEstimate(
            flops=20 * tracer.size, transcendentals=0, bytes_accessed=4 * (2 * tracer.size + 2 * along_x.size)
        ),
    )(*args)


def pack_kernel(st_ref, surf_ref, pay_ref, feat_ref, stack_ref, *, n_surf):
    rows = st_ref.shape[2] // PY
    slot = stack_ref.shape[0] // rows
    levels = st_ref.shape[1]
    keep_surface = pl.program_id(0) < n_surf
    stack_ref[...] = jnp.zeros(stack_ref.shape, stack_ref.dtype)
    for x in range(rows):
        here = slice(x * PY, (x + 1) * PY)
        packed = st_ref[0, :, here].astype(jnp.bfloat16)
        stack_ref[x * slot : x * slot + levels, :] = packed
        feat_ref[x, 0, 0:levels, :] = packed
        surf_row = surf_ref[0, :, here]
        feat_ref[x, 0, levels : levels + 1, :] = jnp.where(keep_surface, surf_row, jnp.zeros_like(surf_row))
        if x == 0:
            pay_ref[0, 0:levels, 0:PY] = packed
        if x == rows - 1:
            pay_ref[0, 0:levels, PY : 2 * PY] = packed
    finish_payload(pay_ref, stack_ref, levels)


def first_edges(tracer, surface):
    n_vars, levels, width = tracer.shape
    n_surf = surface.shape[0]
    rows = width // PY
    slot = 16
    surf_rows = surface.reshape(n_surf, 1, width)
    return pl.pallas_call(
        functools.partial(pack_kernel, n_surf=n_surf),
        grid=(n_vars,),
        in_specs=[
            pl.BlockSpec((1, levels, width), lambda v: (v, 0, 0)),
            pl.BlockSpec((1, 1, width), lambda v: (jnp.minimum(v, n_surf - 1), 0, 0)),
        ],
        out_specs=[
            pl.BlockSpec((1, slot, 3 * PY), lambda v: (v, 0, 0)),
            pl.BlockSpec((rows, 1, slot, PY), lambda v: (0, v, 0, 0)),
        ],
        out_shape=[
            jax.ShapeDtypeStruct((n_vars, slot, 3 * PY), jnp.bfloat16),
            jax.ShapeDtypeStruct((rows, n_vars, slot, PY), jnp.bfloat16),
        ],
        scratch_shapes=[pltpu.VMEM((rows * slot, PY), jnp.bfloat16)],
        cost_estimate=pl.CostEstimate(flops=0, transcendentals=0, bytes_accessed=5 * tracer.size),
    )(tracer, surf_rows)


def exchange_halo(payload, beside_all, patches, levels):
    n_vars, slot, _ = payload.shape
    rows = PX
    chunk_rows = PY // slot
    got = lax.all_gather(payload, "patch", axis=0, tiled=False)
    north = jnp.take(got, beside_all[0], axis=0)[:, 0:levels, PY : 2 * PY]
    south = jnp.take(got, beside_all[1], axis=0)[:, 0:levels, 0:PY]

    def column(patch, which):
        cols = jnp.take(got, patch, axis=0)[..., 2 * PY : 3 * PY]
        cols = cols.reshape(n_vars, rows // chunk_rows, 2, chunk_rows, slot)[:, :, which]
        return cols.transpose(0, 3, 1, 2).reshape(n_vars, slot, rows)[:, 0:levels]

    west = column(beside_all[2], 1)
    east = column(beside_all[3], 0)
    sides = jnp.stack([west, jnp.roll(east, -1, axis=-1)], axis=-1).reshape(west.shape[:-1] + (2 * rows,))
    return jnp.concatenate([north, south, sides], axis=-1).astype(jnp.float32)


def activate(pre_act):
    return jax.nn.silu(pre_act).astype(jnp.bfloat16)


def hidden_layers(hidden, b_hidden, w_mid):
    for layer_index in range(w_mid.shape[0]):
        pre_act = (
            jnp.einsum(
                "...h,hj->...j", hidden, w_mid[layer_index], preferred_element_type=jnp.float32
            )
            + b_hidden[layer_index + 1]
        )
        hidden = activate(pre_act)
    return hidden


def on_device(
    state, courant_x, courant_y, surface, w_in, b_hidden, w_mid, w_out, owner_map, neighbours
):
    groups = lax.axis_size("grp")
    patches = lax.axis_size("patch")
    group_here = lax.axis_index("grp")
    patch_here = lax.axis_index("patch")
    level_share = LEV // groups
    surf_share = SURF // groups
    feat_share = VARS * level_share + surf_share
    quarter_rows = PX // groups
    capacity = max(2, 2 * quarter_rows // patches)
    slot_count = patches * capacity
    slot = 16
    beside_all = jnp.take(neighbours, patch_here, axis=0)
    owners_all = owner_map.reshape(patches, groups, quarter_rows)
    owners_here = jnp.take(jnp.take(owners_all, patch_here, axis=0), group_here, axis=0)
    matches = (owners_here[:, None] == jnp.arange(patches, dtype=jnp.int32)).astype(jnp.int32)
    slot_rank = jnp.sum((jnp.cumsum(matches, axis=0) - matches) * matches, axis=1)
    slot_index = owners_here * capacity + slot_rank
    selector_here = (
        slot_index[None, :] == jnp.arange(slot_count, dtype=jnp.int32)[:, None]
    ).astype(jnp.bfloat16)
    state_part = w_in[: VARS * LEV].reshape(VARS, groups, level_share, -1).transpose(1, 0, 2, 3)
    surf_part = w_in[VARS * LEV :].reshape(groups, surf_share, 1, -1)
    surf_part = jnp.pad(surf_part, ((0, 0), (0, VARS - surf_share), (0, 0), (0, 0)))
    pad_part = jnp.zeros(state_part.shape[:2] + (slot - level_share - 1, state_part.shape[3]), w_in.dtype)
    w_local = jnp.concatenate([state_part, surf_part, pad_part], axis=2).reshape(groups, VARS * slot, -1)
    w_split = w_out.reshape(-1, VARS, groups, level_share)
    w_pad = jnp.pad(w_split, ((0, 0), (0, 0), (0, 0), (0, slot - level_share)))
    w_rows = w_pad.transpose(2, 1, 3, 0).reshape(groups * VARS * slot, -1)
    w_local, w_rows, selector_here, beside_all, state_in = lax.optimization_barrier(
        (w_local, w_rows, selector_here, beside_all, state)
    )
    payload, feat = first_edges(state_in, surface)
    by_quarter = feat.reshape(groups, quarter_rows, VARS * slot, PY)
    regrouped = lax.all_to_all(by_quarter, "grp", split_axis=0, concat_axis=0, tiled=True)
    pre_act = (
        jnp.einsum("gbfc,gfh->bch", regrouped, w_local, preferred_element_type=jnp.float32)
        + b_hidden[0]
    )
    hidden = hidden_layers(activate(pre_act), b_hidden, w_mid)
    hidden_flat = hidden.reshape(quarter_rows * PY, -1)
    tendency = lax.dot_general(
        w_rows, hidden_flat, (((1,), (1,)), ((), ())), preferred_element_type=jnp.float32
    ).astype(jnp.bfloat16)
    tendency = tendency.reshape(groups, VARS, slot, quarter_rows * PY)
    tendency_here = lax.all_to_all(tendency, "grp", split_axis=0, concat_axis=0, tiled=True)
    heating = HEAT_WEIGHT * jnp.sum(
        tendency[:, 0, 0:level_share].astype(jnp.float32), axis=(0, 1)
    ).reshape(quarter_rows, PY)
    packed = jnp.dot(
        selector_here.astype(jnp.float32), heating, precision=lax.Precision.HIGHEST
    ).reshape(patches, capacity, PY)
    owner_heating = lax.all_to_all(
        packed, "patch", split_axis=0, concat_axis=0, tiled=True
    ).reshape(slot_count, PY)
    advected = state
    for section_index in range(SUBSTEPS):
        halo = exchange_halo(payload, beside_all, patches, level_share)
        last = section_index == SUBSTEPS - 1
        advected, payload = stencil(
            advected, courant_x, courant_y, halo, tendency_here if last else None
        )
    new_state = advected
    return (new_state, owner_heating)


def solution(mesh):
    placed = (
        P(None, "grp", "patch"),
        P("grp", "patch"),
        P("grp", "patch"),
        P("grp", "patch"),
        P(),
        P(),
        P(),
        P(),
        P(),
        P(),
    )
    return jax.shard_map(
        on_device,
        mesh=mesh,
        in_specs=placed,
        out_specs=(P(None, "grp", "patch"), P("grp", "patch")),
        check_vma=False,
    )
```

```python
import functools

import jax
import jax.numpy as jnp
from jax import lax
from jax.experimental import pallas as pl
from jax.experimental.pallas import tpu as pltpu
from jax.sharding import PartitionSpec as P

VARS = 9
LEV = 60
SURF = 16
SUBSTEPS = 3
PY = 128
PX = 64


KAPPA = 0.24
PHYS_DT = 0.05
HEAT_WEIGHT = 0.125


def stencil_kernel(*refs, with_tend):
    if with_tend:
        st_ref, cx_ref, cy_ref, rows_ref, tend_ref, out_ref, pay_ref, stack_ref = refs
    else:
        st_ref, cx_ref, cy_ref, rows_ref, out_ref, pay_ref, stack_ref = refs
    rows = st_ref.shape[2] // PY
    slot = stack_ref.shape[0] // rows
    levels = st_ref.shape[1]
    north = rows_ref[0, :, 0:PY]
    south = rows_ref[0, :, PY : 2 * PY]
    sides = rows_ref[0, :, 2 * PY : 3 * PY]
    lane = lax.broadcasted_iota(jnp.int32, north.shape, 1)
    stack_ref[...] = jnp.zeros(stack_ref.shape, stack_ref.dtype)
    for x in range(rows):
        here = slice(x * PY, (x + 1) * PY)
        cur = st_ref[0, :, here]
        up = north if x == 0 else st_ref[0, :, (x - 1) * PY : x * PY]
        down = south if x == rows - 1 else st_ref[0, :, (x + 1) * PY : (x + 2) * PY]
        side = pltpu.roll(sides, (PY - 2 * x) % PY, 1)
        west = jnp.where(lane == 0, side, pltpu.roll(cur, 1, 1))
        east = jnp.where(lane == PY - 1, side, pltpu.roll(cur, PY - 1, 1))
        along_x = cx_ref[:, here]
        along_y = cy_ref[:, here]
        val = (
            cur
            - 0.5 * along_x * (down - up)
            - 0.5 * along_y * (east - west)
            + KAPPA * (up + down + west + east - 4.0 * cur)
        )
        if with_tend:
            quarter = rows // tend_ref.shape[0]
            block = tend_ref[x // quarter, 0, 0:levels, (x % quarter) * PY : (x % quarter + 1) * PY]
            val = val + PHYS_DT * block.astype(jnp.float32)
        out_ref[0, :, here] = val
        packed = val.astype(jnp.bfloat16)
        stack_ref[x * slot : x * slot + levels, :] = packed
        if x == 0:
            pay_ref[0, 0:levels, 0:PY] = packed
        if x == rows - 1:
            pay_ref[0, 0:levels, PY : 2 * PY] = packed
    finish_payload(pay_ref, stack_ref, levels)


def finish_payload(pay_ref, stack_ref, levels):
    pad_rows = pay_ref.shape[1] - levels
    if pad_rows:
        pay_ref[0, levels:, 0 : 2 * PY] = jnp.zeros((pad_rows, 2 * PY), pay_ref.dtype)
    chunks = stack_ref.shape[0] // PY
    pick_row = lax.broadcasted_iota(jnp.int32, (2 * chunks, PY), 0)
    pick_lane = lax.broadcasted_iota(jnp.int32, (2 * chunks, PY), 1)
    cols = jnp.zeros((2 * chunks, PY), jnp.float32)
    for j in range(chunks):
        picker = (
            ((pick_row == 2 * j) & (pick_lane == 0)) | ((pick_row == 2 * j + 1) & (pick_lane == PY - 1))
        ).astype(jnp.bfloat16)
        cols = cols + lax.dot_general(
            picker,
            stack_ref[j * PY : (j + 1) * PY, :],
            (((1,), (1,)), ((), ())),
            preferred_element_type=jnp.float32,
        )
    pay_ref[0, :, 2 * PY : 3 * PY] = cols.astype(pay_ref.dtype)


def stencil(tracer, along_x, along_y, halo, tend):
    n_vars, levels, width = tracer.shape
    rows = width // PY
    slot = 16
    with_tend = tend is not None
    in_specs = [
        pl.BlockSpec((1, levels, width), lambda v: (v, 0, 0)),
        pl.BlockSpec((levels, width), lambda v: (0, 0)),
        pl.BlockSpec((levels, width), lambda v: (0, 0)),
        pl.BlockSpec((1, levels, 3 * PY), lambda v: (v, 0, 0)),
    ]
    args = [tracer, along_x, along_y, halo]
    if with_tend:
        in_specs.append(pl.BlockSpec((tend.shape[0], 1) + tend.shape[2:], lambda v: (0, v, 0, 0)))
        args.append(tend)
    return pl.pallas_call(
        functools.partial(stencil_kernel, with_tend=with_tend),
        grid=(n_vars,),
        in_specs=in_specs,
        out_specs=[
            pl.BlockSpec((1, levels, width), lambda v: (v, 0, 0)),
            pl.BlockSpec((1, slot, 3 * PY), lambda v: (v, 0, 0)),
        ],
        out_shape=[
            jax.ShapeDtypeStruct(tracer.shape, jnp.float32),
            jax.ShapeDtypeStruct((n_vars, slot, 3 * PY), jnp.bfloat16),
        ],
        scratch_shapes=[pltpu.VMEM((rows * slot, PY), jnp.bfloat16)],
        cost_estimate=pl.CostEstimate(
            flops=20 * tracer.size, transcendentals=0, bytes_accessed=4 * (2 * tracer.size + 2 * along_x.size)
        ),
    )(*args)


def pack_kernel(st_ref, surf_ref, pay_ref, feat_ref, stack_ref, *, n_surf):
    rows = st_ref.shape[2] // PY
    slot = stack_ref.shape[0] // rows
    levels = st_ref.shape[1]
    keep_surface = pl.program_id(0) < n_surf
    stack_ref[...] = jnp.zeros(stack_ref.shape, stack_ref.dtype)
    for x in range(rows):
        here = slice(x * PY, (x + 1) * PY)
        packed = st_ref[0, :, here].astype(jnp.bfloat16)
        stack_ref[x * slot : x * slot + levels, :] = packed
        feat_ref[x, 0, 0:levels, :] = packed
        surf_row = surf_ref[0, :, here]
        feat_ref[x, 0, levels : levels + 1, :] = jnp.where(keep_surface, surf_row, jnp.zeros_like(surf_row))
        if x == 0:
            pay_ref[0, 0:levels, 0:PY] = packed
        if x == rows - 1:
            pay_ref[0, 0:levels, PY : 2 * PY] = packed
    finish_payload(pay_ref, stack_ref, levels)


def first_edges(tracer, surface):
    n_vars, levels, width = tracer.shape
    n_surf = surface.shape[0]
    rows = width // PY
    slot = 16
    surf_rows = surface.reshape(n_surf, 1, width)
    return pl.pallas_call(
        functools.partial(pack_kernel, n_surf=n_surf),
        grid=(n_vars,),
        in_specs=[
            pl.BlockSpec((1, levels, width), lambda v: (v, 0, 0)),
            pl.BlockSpec((1, 1, width), lambda v: (jnp.minimum(v, n_surf - 1), 0, 0)),
        ],
        out_specs=[
            pl.BlockSpec((1, slot, 3 * PY), lambda v: (v, 0, 0)),
            pl.BlockSpec((rows, 1, slot, PY), lambda v: (0, v, 0, 0)),
        ],
        out_shape=[
            jax.ShapeDtypeStruct((n_vars, slot, 3 * PY), jnp.bfloat16),
            jax.ShapeDtypeStruct((rows, n_vars, slot, PY), jnp.bfloat16),
        ],
        scratch_shapes=[pltpu.VMEM((rows * slot, PY), jnp.bfloat16)],
        cost_estimate=pl.CostEstimate(flops=0, transcendentals=0, bytes_accessed=5 * tracer.size),
    )(tracer, surf_rows)


def exchange_halo(payload, beside_all, patches, levels, n_vars):
    slot = payload.shape[1]
    rows = PX
    chunk_rows = PY // slot
    got = lax.all_gather(payload, "patch", axis=0, tiled=False)
    north = jnp.take(got, beside_all[0], axis=0)[0:n_vars, 0:levels, PY : 2 * PY]
    south = jnp.take(got, beside_all[1], axis=0)[0:n_vars, 0:levels, 0:PY]

    def column(patch, which):
        cols = jnp.take(got, patch, axis=0)[0:n_vars, :, 2 * PY : 3 * PY]
        cols = cols.reshape(n_vars, rows // chunk_rows, 2, chunk_rows, slot)[:, :, which]
        return cols.transpose(0, 3, 1, 2).reshape(n_vars, slot, rows)[:, 0:levels]

    west = column(beside_all[2], 1)
    east = column(beside_all[3], 0)
    sides = jnp.stack([west, jnp.roll(east, -1, axis=-1)], axis=-1).reshape(west.shape[:-1] + (2 * rows,))
    halo = jnp.concatenate([north, south, sides], axis=-1).astype(jnp.float32)
    return halo, got[:, n_vars:]


def split_pieces(values, block_shape):
    flat = values.reshape(-1)
    high = flat.astype(jnp.bfloat16)
    rest = flat - high.astype(jnp.float32)
    middle = rest.astype(jnp.bfloat16)
    low = (rest - middle.astype(jnp.float32)).astype(jnp.bfloat16)
    pieces = jnp.concatenate([high, middle, low])
    block = block_shape[0] * block_shape[1]
    count = -(-pieces.size // block)
    pieces = jnp.pad(pieces, (0, count * block - pieces.size))
    return pieces.reshape((count,) + block_shape)


def join_pieces(blocks, size):
    flat = blocks.reshape(blocks.shape[0], -1)[:, : 3 * size].astype(jnp.float32)
    flat = flat.reshape(blocks.shape[0], 3, size)
    return (flat[:, 0] + flat[:, 1]) + flat[:, 2]


def activate(pre_act):
    return jax.nn.silu(pre_act).astype(jnp.bfloat16)


def hidden_layers(hidden, b_hidden, w_mid):
    for layer_index in range(w_mid.shape[0]):
        pre_act = (
            jnp.einsum(
                "...h,hj->...j", hidden, w_mid[layer_index], preferred_element_type=jnp.float32
            )
            + b_hidden[layer_index + 1]
        )
        hidden = activate(pre_act)
    return hidden


def on_device(
    state, courant_x, courant_y, surface, w_in, b_hidden, w_mid, w_out, owner_map, neighbours
):
    groups = lax.axis_size("grp")
    patches = lax.axis_size("patch")
    group_here = lax.axis_index("grp")
    patch_here = lax.axis_index("patch")
    level_share = LEV // groups
    surf_share = SURF // groups
    feat_share = VARS * level_share + surf_share
    quarter_rows = PX // groups
    capacity = max(2, 2 * quarter_rows // patches)
    slot_count = patches * capacity
    slot = 16
    beside_all = jnp.take(neighbours, patch_here, axis=0)
    owners_all = owner_map.reshape(patches, groups, quarter_rows)
    owners_here = jnp.take(jnp.take(owners_all, patch_here, axis=0), group_here, axis=0)
    matches = (owners_here[:, None] == jnp.arange(patches, dtype=jnp.int32)).astype(jnp.int32)
    slot_rank = jnp.sum((jnp.cumsum(matches, axis=0) - matches) * matches, axis=1)
    slot_index = owners_here * capacity + slot_rank
    selector_here = (
        slot_index[None, :] == jnp.arange(slot_count, dtype=jnp.int32)[:, None]
    ).astype(jnp.bfloat16)
    state_part = w_in[: VARS * LEV].reshape(VARS, groups, level_share, -1).transpose(1, 0, 2, 3)
    surf_part = w_in[VARS * LEV :].reshape(groups, surf_share, 1, -1)
    surf_part = jnp.pad(surf_part, ((0, 0), (0, VARS - surf_share), (0, 0), (0, 0)))
    pad_part = jnp.zeros(state_part.shape[:2] + (slot - level_share - 1, state_part.shape[3]), w_in.dtype)
    w_local = jnp.concatenate([state_part, surf_part, pad_part], axis=2).reshape(groups, VARS * slot, -1)
    w_split = w_out.reshape(-1, VARS, groups, level_share)
    w_pad = jnp.pad(w_split, ((0, 0), (0, 0), (0, 0), (0, slot - level_share)))
    w_rows = w_pad.transpose(2, 1, 3, 0).reshape(groups * VARS * slot, -1)
    w_local, w_rows, selector_here, beside_all, state_in = lax.optimization_barrier(
        (w_local, w_rows, selector_here, beside_all, state)
    )
    payload, feat = first_edges(state_in, surface)
    by_quarter = feat.reshape(groups, quarter_rows, VARS * slot, PY)
    regrouped = lax.all_to_all(by_quarter, "grp", split_axis=0, concat_axis=0, tiled=True)
    pre_act = (
        jnp.einsum("gbfc,gfh->bch", regrouped, w_local, preferred_element_type=jnp.float32)
        + b_hidden[0]
    )
    hidden = hidden_layers(activate(pre_act), b_hidden, w_mid)
    hidden_flat = hidden.reshape(quarter_rows * PY, -1)
    tendency = lax.dot_general(
        w_rows, hidden_flat, (((1,), (1,)), ((), ())), preferred_element_type=jnp.float32
    ).astype(jnp.bfloat16)
    tendency = tendency.reshape(groups, VARS, slot, quarter_rows * PY)
    tendency_here = lax.all_to_all(tendency, "grp", split_axis=0, concat_axis=0, tiled=True)
    heating = HEAT_WEIGHT * jnp.sum(
        tendency[:, 0, 0:level_share].astype(jnp.float32), axis=(0, 1)
    ).reshape(quarter_rows, PY)
    packed = jnp.dot(
        selector_here.astype(jnp.float32), heating, precision=lax.Precision.HIGHEST
    ).reshape(patches, capacity, PY)
    heat_blocks = split_pieces(packed, (slot, 3 * PY))
    advected = state
    for section_index in range(SUBSTEPS):
        last = section_index == SUBSTEPS - 1
        if last:
            payload = jnp.concatenate([payload, heat_blocks], axis=0)
        halo, extra = exchange_halo(payload, beside_all, patches, level_share, VARS)
        if last:
            heat_all = join_pieces(extra, packed.size).reshape((patches,) + packed.shape)
            owner_heating = jnp.take(heat_all, patch_here, axis=1).reshape(slot_count, PY)
        advected, payload = stencil(
            advected, courant_x, courant_y, halo, tendency_here if last else None
        )
    new_state = advected
    return (new_state, owner_heating)


def solution(mesh):
    placed = (
        P(None, "grp", "patch"),
        P("grp", "patch"),
        P("grp", "patch"),
        P("grp", "patch"),
        P(),
        P(),
        P(),
        P(),
        P(),
        P(),
    )
    return jax.shard_map(
        on_device,
        mesh=mesh,
        in_specs=placed,
        out_specs=(P(None, "grp", "patch"), P("grp", "patch")),
        check_vma=False,
    )
```

```python
import functools

import jax
import jax.numpy as jnp
from jax import lax
from jax.experimental import pallas as pl
from jax.experimental.pallas import tpu as pltpu

from jax.sharding import PartitionSpec as P

VARS = 9
LEV = 60
SURF = 16
SUBSTEPS = 3
PY = 128
PX = 64


KAPPA = 0.24
PHYS_DT = 0.05
HEAT_WEIGHT = 0.125


def stencil_kernel(*refs, with_tend):
    if with_tend:
        st_ref, cx_ref, cy_ref, rows_ref, tend_ref, out_ref, pay_ref, stack_ref = refs
    else:
        st_ref, cx_ref, cy_ref, rows_ref, out_ref, pay_ref, stack_ref = refs
    rows = st_ref.shape[2] // PY
    slot = stack_ref.shape[0] // rows
    levels = st_ref.shape[1]
    north = rows_ref[0, :, 0:PY]
    south = rows_ref[0, :, PY : 2 * PY]
    sides = rows_ref[0, :, 2 * PY : 3 * PY]
    lane = lax.broadcasted_iota(jnp.int32, north.shape, 1)
    stack_ref[...] = jnp.zeros(stack_ref.shape, stack_ref.dtype)
    for x in range(rows):
        here = slice(x * PY, (x + 1) * PY)
        cur = st_ref[0, :, here]
        up = north if x == 0 else st_ref[0, :, (x - 1) * PY : x * PY]
        down = south if x == rows - 1 else st_ref[0, :, (x + 1) * PY : (x + 2) * PY]
        side = pltpu.roll(sides, (PY - 2 * x) % PY, 1)
        west = jnp.where(lane == 0, side, pltpu.roll(cur, 1, 1))
        east = jnp.where(lane == PY - 1, side, pltpu.roll(cur, PY - 1, 1))
        along_x = cx_ref[:, here]
        along_y = cy_ref[:, here]
        val = (
            cur
            - 0.5 * along_x * (down - up)
            - 0.5 * along_y * (east - west)
            + KAPPA * (up + down + west + east - 4.0 * cur)
        )
        if with_tend:
            quarter = rows // tend_ref.shape[0]
            block = tend_ref[x // quarter, 0, 0:levels, (x % quarter) * PY : (x % quarter + 1) * PY]
            val = val + PHYS_DT * block.astype(jnp.float32)
        out_ref[0, :, here] = val
        packed = val.astype(jnp.bfloat16)
        stack_ref[x * slot : x * slot + levels, :] = packed
        if x == 0:
            pay_ref[0, 0:levels, 0:PY] = packed
        if x == rows - 1:
            pay_ref[0, 0:levels, PY : 2 * PY] = packed
    finish_payload(pay_ref, stack_ref, levels)


def finish_payload(pay_ref, stack_ref, levels):
    pad_rows = pay_ref.shape[1] - levels
    if pad_rows:
        pay_ref[0, levels:, 0 : 2 * PY] = jnp.zeros((pad_rows, 2 * PY), pay_ref.dtype)
    chunks = stack_ref.shape[0] // PY
    pick_row = lax.broadcasted_iota(jnp.int32, (2 * chunks, PY), 0)
    pick_lane = lax.broadcasted_iota(jnp.int32, (2 * chunks, PY), 1)
    cols = jnp.zeros((2 * chunks, PY), jnp.float32)
    for j in range(chunks):
        picker = (
            ((pick_row == 2 * j) & (pick_lane == 0)) | ((pick_row == 2 * j + 1) & (pick_lane == PY - 1))
        ).astype(jnp.bfloat16)
        cols = cols + lax.dot_general(
            picker,
            stack_ref[j * PY : (j + 1) * PY, :],
            (((1,), (1,)), ((), ())),
            preferred_element_type=jnp.float32,
        )
    pay_ref[0, :, 2 * PY : 3 * PY] = cols.astype(pay_ref.dtype)


def stencil(tracer, along_x, along_y, halo, tend):
    n_vars, levels, width = tracer.shape
    rows = width // PY
    slot = 16
    with_tend = tend is not None
    in_specs = [
        pl.BlockSpec((1, levels, width), lambda v: (v, 0, 0)),
        pl.BlockSpec((levels, width), lambda v: (0, 0)),
        pl.BlockSpec((levels, width), lambda v: (0, 0)),
        pl.BlockSpec((1, levels, 3 * PY), lambda v: (v, 0, 0)),
    ]
    args = [tracer, along_x, along_y, halo]
    if with_tend:
        in_specs.append(pl.BlockSpec((tend.shape[0], 1) + tend.shape[2:], lambda v: (0, v, 0, 0)))
        args.append(tend)
    return pl.pallas_call(
        functools.partial(stencil_kernel, with_tend=with_tend),
        grid=(n_vars,),
        in_specs=in_specs,
        out_specs=[
            pl.BlockSpec((1, levels, width), lambda v: (v, 0, 0)),
            pl.BlockSpec((1, slot, 3 * PY), lambda v: (v, 0, 0)),
        ],
        out_shape=[
            jax.ShapeDtypeStruct(tracer.shape, jnp.float32),
            jax.ShapeDtypeStruct((n_vars, slot, 3 * PY), jnp.bfloat16),
        ],
        scratch_shapes=[pltpu.VMEM((rows * slot, PY), jnp.bfloat16)],
        cost_estimate=pl.CostEstimate(
            flops=20 * tracer.size, transcendentals=0, bytes_accessed=4 * (2 * tracer.size + 2 * along_x.size)
        ),
    )(*args)


def pack_kernel(st_ref, surf_ref, pay_ref, feat_ref, stack_ref, *, n_surf):
    rows = st_ref.shape[2] // PY
    slot = stack_ref.shape[0] // rows
    levels = st_ref.shape[1]
    keep_surface = pl.program_id(0) < n_surf
    stack_ref[...] = jnp.zeros(stack_ref.shape, stack_ref.dtype)
    for x in range(rows):
        here = slice(x * PY, (x + 1) * PY)
        packed = st_ref[0, :, here].astype(jnp.bfloat16)
        stack_ref[x * slot : x * slot + levels, :] = packed
        feat_ref[x, 0, 0:levels, :] = packed
        surf_row = surf_ref[0, :, here]
        feat_ref[x, 0, levels : levels + 1, :] = jnp.where(keep_surface, surf_row, jnp.zeros_like(surf_row))
        if x == 0:
            pay_ref[0, 0:levels, 0:PY] = packed
        if x == rows - 1:
            pay_ref[0, 0:levels, PY : 2 * PY] = packed
    finish_payload(pay_ref, stack_ref, levels)


def first_edges(tracer, surface):
    n_vars, levels, width = tracer.shape
    n_surf = surface.shape[0]
    rows = width // PY
    slot = 16
    surf_rows = surface.reshape(n_surf, 1, width)
    return pl.pallas_call(
        functools.partial(pack_kernel, n_surf=n_surf),
        grid=(n_vars,),
        in_specs=[
            pl.BlockSpec((1, levels, width), lambda v: (v, 0, 0)),
            pl.BlockSpec((1, 1, width), lambda v: (jnp.minimum(v, n_surf - 1), 0, 0)),
        ],
        out_specs=[
            pl.BlockSpec((1, slot, 3 * PY), lambda v: (v, 0, 0)),
            pl.BlockSpec((rows, 1, slot, PY), lambda v: (0, v, 0, 0)),
        ],
        out_shape=[
            jax.ShapeDtypeStruct((n_vars, slot, 3 * PY), jnp.bfloat16),
            jax.ShapeDtypeStruct((rows, n_vars, slot, PY), jnp.bfloat16),
        ],
        scratch_shapes=[pltpu.VMEM((rows * slot, PY), jnp.bfloat16)],
        cost_estimate=pl.CostEstimate(flops=0, transcendentals=0, bytes_accessed=5 * tracer.size),
    )(tracer, surf_rows)


def exchange_halo(payload, beside_all, levels):
    n_vars, slot, _ = payload.shape
    rows = PX
    chunk_rows = PY // slot
    got = lax.all_gather(payload, "patch", axis=0, tiled=False)
    north = jnp.take(got, beside_all[0], axis=0)[:, 0:levels, PY : 2 * PY]
    south = jnp.take(got, beside_all[1], axis=0)[:, 0:levels, 0:PY]

    def column(patch, which):
        cols = jnp.take(got, patch, axis=0)[..., 2 * PY : 3 * PY]
        cols = cols.reshape(n_vars, rows // chunk_rows, 2, chunk_rows, slot)[:, :, which]
        return cols.transpose(0, 3, 1, 2).reshape(n_vars, slot, rows)[:, 0:levels]

    west = column(beside_all[2], 1)
    east = column(beside_all[3], 0)
    sides = jnp.stack([west, jnp.roll(east, -1, axis=-1)], axis=-1).reshape(west.shape[:-1] + (2 * rows,))
    return jnp.concatenate([north, south, sides], axis=-1).astype(jnp.float32)


def activate(pre_act):
    return jax.nn.silu(pre_act).astype(jnp.bfloat16)


def hidden_layers(hidden, b_hidden, w_mid):
    for layer_index in range(w_mid.shape[0]):
        pre_act = (
            jnp.einsum(
                "...h,hj->...j", hidden, w_mid[layer_index], preferred_element_type=jnp.float32
            )
            + b_hidden[layer_index + 1]
        )
        hidden = activate(pre_act)
    return hidden


def on_device(
    state, courant_x, courant_y, surface, w_in, b_hidden, w_mid, w_out, owner_map, neighbours
):
    groups = lax.axis_size("grp")
    patches = lax.axis_size("patch")
    group_here = lax.axis_index("grp")
    patch_here = lax.axis_index("patch")
    level_share = LEV // groups
    surf_share = SURF // groups
    quarter_rows = PX // groups
    capacity = max(2, 2 * quarter_rows // patches)
    slot_count = patches * capacity
    slot = 16
    beside_all = jnp.take(neighbours, patch_here, axis=0)
    owners_all = owner_map.reshape(patches, groups, quarter_rows)
    owners_here = jnp.take(jnp.take(owners_all, patch_here, axis=0), group_here, axis=0)
    matches = (owners_here[:, None] == jnp.arange(patches, dtype=jnp.int32)).astype(jnp.int32)
    slot_rank = jnp.sum((jnp.cumsum(matches, axis=0) - matches) * matches, axis=1)
    slot_index = owners_here * capacity + slot_rank
    selector_here = (
        slot_index[None, :] == jnp.arange(slot_count, dtype=jnp.int32)[:, None]
    ).astype(jnp.bfloat16)
    state_part = w_in[: VARS * LEV].reshape(VARS, groups, level_share, -1).transpose(1, 0, 2, 3)
    surf_part = w_in[VARS * LEV :].reshape(groups, surf_share, 1, -1)
    surf_part = jnp.pad(surf_part, ((0, 0), (0, VARS - surf_share), (0, 0), (0, 0)))
    pad_part = jnp.zeros(state_part.shape[:2] + (slot - level_share - 1, state_part.shape[3]), w_in.dtype)
    w_local = jnp.concatenate([state_part, surf_part, pad_part], axis=2).reshape(groups, VARS * slot, -1)
    w_split = w_out.reshape(-1, VARS, groups, level_share)
    w_pad = jnp.pad(w_split, ((0, 0), (0, 0), (0, 0), (0, slot - level_share)))
    w_rows = w_pad.transpose(2, 1, 3, 0).reshape(groups * VARS * slot, -1)
    w_local, w_rows, selector_here, beside_all, state_in = lax.optimization_barrier(
        (w_local, w_rows, selector_here, beside_all, state)
    )
    payload, feat = first_edges(state_in, surface)
    by_quarter = feat.reshape(groups, quarter_rows, VARS * slot, PY)
    regrouped = lax.all_to_all(by_quarter, "grp", split_axis=0, concat_axis=0, tiled=True)
    pre_act = (
        jnp.einsum("gbfc,gfh->bch", regrouped, w_local, preferred_element_type=jnp.float32)
        + b_hidden[0]
    )
    hidden = hidden_layers(activate(pre_act), b_hidden, w_mid)
    hidden_flat = hidden.reshape(quarter_rows * PY, -1)
    tendency = lax.dot_general(
        w_rows, hidden_flat, (((1,), (1,)), ((), ())), preferred_element_type=jnp.float32
    ).astype(jnp.bfloat16)
    tendency = tendency.reshape(groups, VARS, slot, quarter_rows * PY)
    tendency_here = lax.all_to_all(tendency, "grp", split_axis=0, concat_axis=0, tiled=True)
    heating = HEAT_WEIGHT * jnp.sum(
        tendency[:, 0, 0:level_share].astype(jnp.float32), axis=(0, 1)
    ).reshape(quarter_rows, PY)
    packed = jnp.dot(
        selector_here.astype(jnp.float32), heating, precision=lax.Precision.HIGHEST
    ).reshape(patches, capacity, PY)
    owner_heating = lax.all_to_all(
        packed, "patch", split_axis=0, concat_axis=0, tiled=True
    ).reshape(slot_count, PY)
    advected = state
    for section_index in range(SUBSTEPS):
        halo = exchange_halo(payload, beside_all, level_share)
        last = section_index == SUBSTEPS - 1
        advected, payload = stencil(
            advected, courant_x, courant_y, halo, tendency_here if last else None
        )
    new_state = advected
    return (new_state, owner_heating)


def solution(mesh):
    placed = (
        P(None, "grp", "patch"),
        P("grp", "patch"),
        P("grp", "patch"),
        P("grp", "patch"),
        P(),
        P(),
        P(),
        P(),
        P(),
        P(),
    )

    return jax.shard_map(
        on_device,
        mesh=mesh,
        in_specs=placed,
        out_specs=(P(None, "grp", "patch"), P("grp", "patch")),
        check_vma=False,
    )
```

```python
import functools

import jax
import jax.numpy as jnp
from jax import lax
from jax.experimental import pallas as pl
from jax.experimental.pallas import tpu as pltpu
from jax.sharding import PartitionSpec as P

VARS = 9
LEV = 60
SURF = 16
SUBSTEPS = 3
PY = 128
PX = 64


KAPPA = 0.24
PHYS_DT = 0.05
HEAT_WEIGHT = 0.125


def stencil_kernel(*refs, with_tend):
    if with_tend:
        st_ref, cx_ref, cy_ref, rows_ref, tend_ref, out_ref, pay_ref, stack_ref = refs
    else:
        st_ref, cx_ref, cy_ref, rows_ref, out_ref, pay_ref, stack_ref = refs
    rows = st_ref.shape[2] // PY
    slot = stack_ref.shape[0] // rows
    levels = st_ref.shape[1]
    north = rows_ref[0, :, 0:PY].astype(jnp.float32)
    south = rows_ref[0, :, PY : 2 * PY].astype(jnp.float32)
    sides = rows_ref[0, :, 2 * PY : 3 * PY].astype(jnp.float32)
    lane = lax.broadcasted_iota(jnp.int32, north.shape, 1)
    stack_ref[...] = jnp.zeros(stack_ref.shape, stack_ref.dtype)
    for x in range(rows):
        here = slice(x * PY, (x + 1) * PY)
        cur = st_ref[0, :, here]
        up = north if x == 0 else st_ref[0, :, (x - 1) * PY : x * PY]
        down = south if x == rows - 1 else st_ref[0, :, (x + 1) * PY : (x + 2) * PY]
        side = pltpu.roll(sides, (PY - 2 * x) % PY, 1)
        west = jnp.where(lane == 0, side, pltpu.roll(cur, 1, 1))
        east = jnp.where(lane == PY - 1, side, pltpu.roll(cur, PY - 1, 1))
        along_x = cx_ref[:, here]
        along_y = cy_ref[:, here]
        val = (
            cur
            - 0.5 * along_x * (down - up)
            - 0.5 * along_y * (east - west)
            + KAPPA * (up + down + west + east - 4.0 * cur)
        )
        if with_tend:
            quarter = rows // tend_ref.shape[0]
            block = tend_ref[x // quarter, 0, 0:levels, (x % quarter) * PY : (x % quarter + 1) * PY]
            val = val + PHYS_DT * block.astype(jnp.float32)
        out_ref[0, :, here] = val
        packed = val.astype(jnp.bfloat16)
        stack_ref[x * slot : x * slot + levels, :] = packed
        if x == 0:
            pay_ref[0, 0:levels, 0:PY] = packed
        if x == rows - 1:
            pay_ref[0, 0:levels, PY : 2 * PY] = packed
    finish_payload(pay_ref, stack_ref, levels)


def finish_payload(pay_ref, stack_ref, levels):
    pad_rows = pay_ref.shape[1] - levels
    if pad_rows:
        pay_ref[0, levels:, 0 : 2 * PY] = jnp.zeros((pad_rows, 2 * PY), pay_ref.dtype)
    chunks = stack_ref.shape[0] // PY
    pick_row = lax.broadcasted_iota(jnp.int32, (2 * chunks, PY), 0)
    pick_lane = lax.broadcasted_iota(jnp.int32, (2 * chunks, PY), 1)
    cols = jnp.zeros((2 * chunks, PY), jnp.float32)
    for j in range(chunks):
        picker = (
            ((pick_row == 2 * j) & (pick_lane == 0)) | ((pick_row == 2 * j + 1) & (pick_lane == PY - 1))
        ).astype(jnp.bfloat16)
        cols = cols + lax.dot_general(
            picker,
            stack_ref[j * PY : (j + 1) * PY, :],
            (((1,), (1,)), ((), ())),
            preferred_element_type=jnp.float32,
        )
    pay_ref[0, :, 2 * PY : 3 * PY] = cols.astype(pay_ref.dtype)


def stencil(tracer, along_x, along_y, halo, tend):
    n_vars, levels, width = tracer.shape
    rows = width // PY
    slot = 16
    with_tend = tend is not None
    in_specs = [
        pl.BlockSpec((1, levels, width), lambda v: (v, 0, 0)),
        pl.BlockSpec((levels, width), lambda v: (0, 0)),
        pl.BlockSpec((levels, width), lambda v: (0, 0)),
        pl.BlockSpec((1, levels, 3 * PY), lambda v: (v, 0, 0)),
    ]
    args = [tracer, along_x, along_y, halo]
    if with_tend:
        in_specs.append(pl.BlockSpec((tend.shape[0], 1) + tend.shape[2:], lambda v: (0, v, 0, 0)))
        args.append(tend)
    return pl.pallas_call(
        functools.partial(stencil_kernel, with_tend=with_tend),
        grid=(n_vars,),
        in_specs=in_specs,
        out_specs=[
            pl.BlockSpec((1, levels, width), lambda v: (v, 0, 0)),
            pl.BlockSpec((1, slot, 3 * PY), lambda v: (v, 0, 0)),
        ],
        out_shape=[
            jax.ShapeDtypeStruct(tracer.shape, jnp.float32),
            jax.ShapeDtypeStruct((n_vars, slot, 3 * PY), jnp.bfloat16),
        ],
        scratch_shapes=[pltpu.VMEM((rows * slot, PY), jnp.bfloat16)],
        cost_estimate=pl.CostEstimate(
            flops=20 * tracer.size, transcendentals=0, bytes_accessed=4 * (2 * tracer.size + 2 * along_x.size)
        ),
    )(*args)


def pack_kernel(st_ref, surf_ref, pay_ref, feat_ref, stack_ref, *, n_surf):
    rows = st_ref.shape[2] // PY
    slot = stack_ref.shape[0] // rows
    levels = st_ref.shape[1]
    keep_surface = pl.program_id(0) < n_surf
    stack_ref[...] = jnp.zeros(stack_ref.shape, stack_ref.dtype)
    for x in range(rows):
        here = slice(x * PY, (x + 1) * PY)
        packed = st_ref[0, :, here].astype(jnp.bfloat16)
        stack_ref[x * slot : x * slot + levels, :] = packed
        feat_ref[x, 0, 0:levels, :] = packed
        surf_row = surf_ref[0, :, here]
        feat_ref[x, 0, levels : levels + 1, :] = jnp.where(keep_surface, surf_row, jnp.zeros_like(surf_row))
        if x == 0:
            pay_ref[0, 0:levels, 0:PY] = packed
        if x == rows - 1:
            pay_ref[0, 0:levels, PY : 2 * PY] = packed
    finish_payload(pay_ref, stack_ref, levels)


def first_edges(tracer, surface):
    n_vars, levels, width = tracer.shape
    n_surf = surface.shape[0]
    rows = width // PY
    slot = 16
    surf_rows = surface.reshape(n_surf, 1, width)
    return pl.pallas_call(
        functools.partial(pack_kernel, n_surf=n_surf),
        grid=(n_vars,),
        in_specs=[
            pl.BlockSpec((1, levels, width), lambda v: (v, 0, 0)),
            pl.BlockSpec((1, 1, width), lambda v: (jnp.minimum(v, n_surf - 1), 0, 0)),
        ],
        out_specs=[
            pl.BlockSpec((1, slot, 3 * PY), lambda v: (v, 0, 0)),
            pl.BlockSpec((rows, 1, slot, PY), lambda v: (0, v, 0, 0)),
        ],
        out_shape=[
            jax.ShapeDtypeStruct((n_vars, slot, 3 * PY), jnp.bfloat16),
            jax.ShapeDtypeStruct((rows, n_vars, slot, PY), jnp.bfloat16),
        ],
        scratch_shapes=[pltpu.VMEM((rows * slot, PY), jnp.bfloat16)],
        cost_estimate=pl.CostEstimate(flops=0, transcendentals=0, bytes_accessed=5 * tracer.size),
    )(tracer, surf_rows)


def exchange_halo(payload, beside_all, patches, levels):
    n_vars, slot, _ = payload.shape
    rows = PX
    chunk_rows = PY // slot
    got = lax.all_gather(payload, "patch", axis=0, tiled=False)
    north = jnp.take(got, beside_all[0], axis=0)[:, 0:levels, PY : 2 * PY]
    south = jnp.take(got, beside_all[1], axis=0)[:, 0:levels, 0:PY]

    def column(patch, which):
        cols = jnp.take(got, patch, axis=0)[..., 2 * PY : 3 * PY]
        cols = cols.reshape(n_vars, rows // chunk_rows, 2, chunk_rows, slot)[:, :, which]
        return cols.transpose(0, 3, 1, 2).reshape(n_vars, slot, rows)[:, 0:levels]

    west = column(beside_all[2], 1)
    east = column(beside_all[3], 0)
    sides = jnp.stack([west, jnp.roll(east, -1, axis=-1)], axis=-1).reshape(west.shape[:-1] + (2 * rows,))
    return jnp.concatenate([north, south, sides], axis=-1)


def activate(pre_act):
    return jax.nn.silu(pre_act).astype(jnp.bfloat16)


def hidden_layers(hidden, b_hidden, w_mid):
    for layer_index in range(w_mid.shape[0]):
        pre_act = (
            jnp.einsum(
                "...h,hj->...j", hidden, w_mid[layer_index], preferred_element_type=jnp.float32
            )
            + b_hidden[layer_index + 1]
        )
        hidden = activate(pre_act)
    return hidden


def on_device(
    state, courant_x, courant_y, surface, w_in, b_hidden, w_mid, w_out, owner_map, neighbours
):
    groups = lax.axis_size("grp")
    patches = lax.axis_size("patch")
    group_here = lax.axis_index("grp")
    patch_here = lax.axis_index("patch")
    level_share = LEV // groups
    surf_share = SURF // groups
    feat_share = VARS * level_share + surf_share
    quarter_rows = PX // groups
    capacity = max(2, 2 * quarter_rows // patches)
    slot_count = patches * capacity
    slot = 16
    beside_all = jnp.take(neighbours, patch_here, axis=0)
    owners_all = owner_map.reshape(patches, groups, quarter_rows)
    owners_here = jnp.take(jnp.take(owners_all, patch_here, axis=0), group_here, axis=0)
    matches = (owners_here[:, None] == jnp.arange(patches, dtype=jnp.int32)).astype(jnp.int32)
    slot_rank = jnp.sum((jnp.cumsum(matches, axis=0) - matches) * matches, axis=1)
    slot_index = owners_here * capacity + slot_rank
    selector_here = (
        slot_index[None, :] == jnp.arange(slot_count, dtype=jnp.int32)[:, None]
    ).astype(jnp.bfloat16)
    state_part = w_in[: VARS * LEV].reshape(VARS, groups, level_share, -1).transpose(1, 0, 2, 3)
    surf_part = w_in[VARS * LEV :].reshape(groups, surf_share, 1, -1)
    surf_part = jnp.pad(surf_part, ((0, 0), (0, VARS - surf_share), (0, 0), (0, 0)))
    pad_part = jnp.zeros(state_part.shape[:2] + (slot - level_share - 1, state_part.shape[3]), w_in.dtype)
    w_local = jnp.concatenate([state_part, surf_part, pad_part], axis=2).reshape(groups, VARS * slot, -1)
    w_split = w_out.reshape(-1, VARS, groups, level_share)
    w_pad = jnp.pad(w_split, ((0, 0), (0, 0), (0, 0), (0, slot - level_share)))
    w_rows = w_pad.transpose(2, 1, 3, 0).reshape(groups * VARS * slot, -1)
    w_local, w_rows, selector_here, beside_all, state_in = lax.optimization_barrier(
        (w_local, w_rows, selector_here, beside_all, state)
    )
    payload, feat = first_edges(state_in, surface)
    by_quarter = feat.reshape(groups, quarter_rows, VARS * slot, PY)
    regrouped = lax.all_to_all(by_quarter, "grp", split_axis=0, concat_axis=0, tiled=True)
    pre_act = (
        jnp.einsum("gbfc,gfh->bch", regrouped, w_local, preferred_element_type=jnp.float32)
        + b_hidden[0]
    )
    hidden = hidden_layers(activate(pre_act), b_hidden, w_mid)
    hidden_flat = hidden.reshape(quarter_rows * PY, -1)
    tendency = lax.dot_general(
        w_rows, hidden_flat, (((1,), (1,)), ((), ())), preferred_element_type=jnp.float32
    ).astype(jnp.bfloat16)
    tendency = tendency.reshape(groups, VARS, slot, quarter_rows * PY)
    tendency_here = lax.all_to_all(tendency, "grp", split_axis=0, concat_axis=0, tiled=True)
    heating = HEAT_WEIGHT * jnp.sum(
        tendency[:, 0, 0:level_share].astype(jnp.float32), axis=(0, 1)
    ).reshape(quarter_rows, PY)
    packed = jnp.dot(
        selector_here.astype(jnp.float32), heating, precision=lax.Precision.HIGHEST
    ).reshape(patches, capacity, PY)
    owner_heating = lax.all_to_all(
        packed, "patch", split_axis=0, concat_axis=0, tiled=True
    ).reshape(slot_count, PY)
    advected = state
    for section_index in range(SUBSTEPS):
        halo = exchange_halo(payload, beside_all, patches, level_share)
        last = section_index == SUBSTEPS - 1
        advected, payload = stencil(
            advected, courant_x, courant_y, halo, tendency_here if last else None
        )
    new_state = advected
    return (new_state, owner_heating)


def solution(mesh):
    placed = (
        P(None, "grp", "patch"),
        P("grp", "patch"),
        P("grp", "patch"),
        P("grp", "patch"),
        P(),
        P(),
        P(),
        P(),
        P(),
        P(),
    )
    return jax.shard_map(
        on_device,
        mesh=mesh,
        in_specs=placed,
        out_specs=(P(None, "grp", "patch"), P("grp", "patch")),
        check_vma=False,
    )
```

```python
import functools

import jax
import jax.numpy as jnp
from jax import lax
from jax.experimental import pallas as pl
from jax.experimental.pallas import tpu as pltpu
from jax.sharding import PartitionSpec as P

VARS = 9
LEV = 60
SURF = 16
SUBSTEPS = 3
PY = 128
PX = 64


KAPPA = 0.24
PHYS_DT = 0.05
HEAT_WEIGHT = 0.125


def stencil_kernel(*refs, with_tend):
    if with_tend:
        st_ref, cx_ref, cy_ref, rows_ref, tend_ref, out_ref, pay_ref, stack_ref = refs
    else:
        st_ref, cx_ref, cy_ref, rows_ref, out_ref, pay_ref, stack_ref = refs
    rows = st_ref.shape[2] // PY
    slot = stack_ref.shape[0] // rows
    levels = st_ref.shape[1]
    north = rows_ref[0, :, 0:PY].astype(jnp.float32)
    south = rows_ref[0, :, PY : 2 * PY].astype(jnp.float32)
    sides = rows_ref[0, :, 2 * PY : 3 * PY].astype(jnp.float32)
    lane = lax.broadcasted_iota(jnp.int32, north.shape, 1)
    stack_ref[...] = jnp.zeros(stack_ref.shape, stack_ref.dtype)
    for x in range(rows):
        here = slice(x * PY, (x + 1) * PY)
        cur = st_ref[0, :, here]
        up = north if x == 0 else st_ref[0, :, (x - 1) * PY : x * PY]
        down = south if x == rows - 1 else st_ref[0, :, (x + 1) * PY : (x + 2) * PY]
        side = pltpu.roll(sides, (PY - 2 * x) % PY, 1)
        west = jnp.where(lane == 0, side, pltpu.roll(cur, 1, 1))
        east = jnp.where(lane == PY - 1, side, pltpu.roll(cur, PY - 1, 1))
        along_x = cx_ref[:, here]
        along_y = cy_ref[:, here]
        val = (
            cur
            - 0.5 * along_x * (down - up)
            - 0.5 * along_y * (east - west)
            + KAPPA * (up + down + west + east - 4.0 * cur)
        )
        if with_tend:
            quarter = rows // tend_ref.shape[0]
            block = tend_ref[x // quarter, 0, 0:levels, (x % quarter) * PY : (x % quarter + 1) * PY]
            val = val + PHYS_DT * block.astype(jnp.float32)
        out_ref[0, :, here] = val
        packed = val.astype(jnp.bfloat16)
        stack_ref[x * slot : x * slot + levels, :] = packed
        if x == 0:
            pay_ref[0, 0:levels, 0:PY] = packed
        if x == rows - 1:
            pay_ref[0, 0:levels, PY : 2 * PY] = packed
    finish_payload(pay_ref, stack_ref, levels)


def finish_payload(pay_ref, stack_ref, levels):
    pad_rows = pay_ref.shape[1] - levels
    if pad_rows:
        pay_ref[0, levels:, 0 : 2 * PY] = jnp.zeros((pad_rows, 2 * PY), pay_ref.dtype)
    chunks = stack_ref.shape[0] // PY
    pick_row = lax.broadcasted_iota(jnp.int32, (2 * chunks, PY), 0)
    pick_lane = lax.broadcasted_iota(jnp.int32, (2 * chunks, PY), 1)
    cols = jnp.zeros((2 * chunks, PY), jnp.float32)
    for j in range(chunks):
        picker = (
            ((pick_row == 2 * j) & (pick_lane == 0)) | ((pick_row == 2 * j + 1) & (pick_lane == PY - 1))
        ).astype(jnp.bfloat16)
        cols = cols + lax.dot_general(
            picker,
            stack_ref[j * PY : (j + 1) * PY, :],
            (((1,), (1,)), ((), ())),
            preferred_element_type=jnp.float32,
        )
    pay_ref[0, :, 2 * PY : 3 * PY] = cols.astype(pay_ref.dtype)


def stencil(tracer, along_x, along_y, halo, tend):
    n_vars, levels, width = tracer.shape
    rows = width // PY
    slot = 16
    with_tend = tend is not None
    in_specs = [
        pl.BlockSpec((1, levels, width), lambda v: (v, 0, 0)),
        pl.BlockSpec((levels, width), lambda v: (0, 0)),
        pl.BlockSpec((levels, width), lambda v: (0, 0)),
        pl.BlockSpec((1, levels, 3 * PY), lambda v: (v, 0, 0)),
    ]
    args = [tracer, along_x, along_y, halo]
    if with_tend:
        in_specs.append(pl.BlockSpec((tend.shape[0], 1) + tend.shape[2:], lambda v: (0, v, 0, 0)))
        args.append(tend)
    return pl.pallas_call(
        functools.partial(stencil_kernel, with_tend=with_tend),
        grid=(n_vars,),
        in_specs=in_specs,
        out_specs=[
            pl.BlockSpec((1, levels, width), lambda v: (v, 0, 0)),
            pl.BlockSpec((1, slot, 3 * PY), lambda v: (v, 0, 0)),
        ],
        out_shape=[
            jax.ShapeDtypeStruct(tracer.shape, jnp.float32),
            jax.ShapeDtypeStruct((n_vars, slot, 3 * PY), jnp.bfloat16),
        ],
        scratch_shapes=[pltpu.VMEM((rows * slot, PY), jnp.bfloat16)],
        cost_estimate=pl.CostEstimate(
            flops=20 * tracer.size, transcendentals=0, bytes_accessed=4 * (2 * tracer.size + 2 * along_x.size)
        ),
    )(*args)


def pack_kernel(st_ref, surf_ref, pay_ref, feat_ref, stack_ref, *, n_surf):
    rows = st_ref.shape[2] // PY
    slot = stack_ref.shape[0] // rows
    levels = st_ref.shape[1]
    stack_ref[...] = jnp.zeros(stack_ref.shape, stack_ref.dtype)
    for x in range(rows):
        here = slice(x * PY, (x + 1) * PY)
        packed = st_ref[0, :, here].astype(jnp.bfloat16)
        stack_ref[x * slot : x * slot + levels, :] = packed
        feat_ref[x, 0, 0:levels, :] = packed
        surf_all = surf_ref[:, here].astype(jnp.float32)
        pick = lax.broadcasted_iota(jnp.int32, surf_all.shape, 0) == pl.program_id(0)
        surf_row = jnp.sum(jnp.where(pick, surf_all, 0.0), axis=0, keepdims=True)
        feat_ref[x, 0, levels : levels + 1, :] = surf_row.astype(feat_ref.dtype)
        if x == 0:
            pay_ref[0, 0:levels, 0:PY] = packed
        if x == rows - 1:
            pay_ref[0, 0:levels, PY : 2 * PY] = packed
    finish_payload(pay_ref, stack_ref, levels)


def first_edges(tracer, surface):
    n_vars, levels, width = tracer.shape
    n_surf = surface.shape[0]
    rows = width // PY
    slot = 16
    return pl.pallas_call(
        functools.partial(pack_kernel, n_surf=n_surf),
        grid=(n_vars,),
        in_specs=[
            pl.BlockSpec((1, levels, width), lambda v: (v, 0, 0)),
            pl.BlockSpec((n_surf, width), lambda v: (0, 0)),
        ],
        out_specs=[
            pl.BlockSpec((1, slot, 3 * PY), lambda v: (v, 0, 0)),
            pl.BlockSpec((rows, 1, slot, PY), lambda v: (0, v, 0, 0)),
        ],
        out_shape=[
            jax.ShapeDtypeStruct((n_vars, slot, 3 * PY), jnp.bfloat16),
            jax.ShapeDtypeStruct((rows, n_vars, slot, PY), jnp.bfloat16),
        ],
        scratch_shapes=[pltpu.VMEM((rows * slot, PY), jnp.bfloat16)],
        cost_estimate=pl.CostEstimate(flops=0, transcendentals=0, bytes_accessed=5 * tracer.size),
    )(tracer, surface)


def exchange_halo(payload, beside_all, patches, levels):
    n_vars, slot, _ = payload.shape
    rows = PX
    chunk_rows = PY // slot
    got = lax.all_gather(payload, "patch", axis=0, tiled=False)
    north = jnp.take(got, beside_all[0], axis=0)[:, 0:levels, PY : 2 * PY]
    south = jnp.take(got, beside_all[1], axis=0)[:, 0:levels, 0:PY]

    def column(patch, which):
        cols = jnp.take(got, patch, axis=0)[..., 2 * PY : 3 * PY]
        cols = cols.reshape(n_vars, rows // chunk_rows, 2, chunk_rows, slot)[:, :, which]
        return cols.transpose(0, 3, 1, 2).reshape(n_vars, slot, rows)[:, 0:levels]

    west = column(beside_all[2], 1)
    east = column(beside_all[3], 0)
    sides = jnp.stack([west, jnp.roll(east, -1, axis=-1)], axis=-1).reshape(west.shape[:-1] + (2 * rows,))
    return jnp.concatenate([north, south, sides], axis=-1)


def activate(pre_act):
    return jax.nn.silu(pre_act).astype(jnp.bfloat16)


def hidden_layers(hidden, b_hidden, w_mid):
    for layer_index in range(w_mid.shape[0]):
        pre_act = (
            jnp.einsum(
                "...h,hj->...j", hidden, w_mid[layer_index], preferred_element_type=jnp.float32
            )
            + b_hidden[layer_index + 1]
        )
        hidden = activate(pre_act)
    return hidden


def on_device(
    state, courant_x, courant_y, surface, w_in, b_hidden, w_mid, w_out, owner_map, neighbours
):
    groups = lax.axis_size("grp")
    patches = lax.axis_size("patch")
    group_here = lax.axis_index("grp")
    patch_here = lax.axis_index("patch")
    level_share = LEV // groups
    surf_share = SURF // groups
    feat_share = VARS * level_share + surf_share
    quarter_rows = PX // groups
    capacity = max(2, 2 * quarter_rows // patches)
    slot_count = patches * capacity
    slot = 16
    beside_all = jnp.take(neighbours, patch_here, axis=0)
    owners_all = owner_map.reshape(patches, groups, quarter_rows)
    owners_here = jnp.take(jnp.take(owners_all, patch_here, axis=0), group_here, axis=0)
    matches = (owners_here[:, None] == jnp.arange(patches, dtype=jnp.int32)).astype(jnp.int32)
    slot_rank = jnp.sum((jnp.cumsum(matches, axis=0) - matches) * matches, axis=1)
    slot_index = owners_here * capacity + slot_rank
    selector_here = (
        slot_index[None, :] == jnp.arange(slot_count, dtype=jnp.int32)[:, None]
    ).astype(jnp.bfloat16)
    state_part = w_in[: VARS * LEV].reshape(VARS, groups, level_share, -1).transpose(1, 0, 2, 3)
    surf_part = w_in[VARS * LEV :].reshape(groups, surf_share, 1, -1)
    surf_part = jnp.pad(surf_part, ((0, 0), (0, VARS - surf_share), (0, 0), (0, 0)))
    pad_part = jnp.zeros(state_part.shape[:2] + (slot - level_share - 1, state_part.shape[3]), w_in.dtype)
    w_local = jnp.concatenate([state_part, surf_part, pad_part], axis=2).reshape(groups, VARS * slot, -1)
    w_split = w_out.reshape(-1, VARS, groups, level_share)
    w_pad = jnp.pad(w_split, ((0, 0), (0, 0), (0, 0), (0, slot - level_share)))
    w_rows = w_pad.transpose(2, 1, 3, 0).reshape(groups * VARS * slot, -1)
    w_local, w_rows, selector_here, beside_all, state_in = lax.optimization_barrier(
        (w_local, w_rows, selector_here, beside_all, state)
    )
    payload, feat = first_edges(state_in, surface)
    by_quarter = feat.reshape(groups, quarter_rows, VARS * slot, PY)
    regrouped = lax.all_to_all(by_quarter, "grp", split_axis=0, concat_axis=0, tiled=True)
    pre_act = (
        jnp.einsum("gbfc,gfh->bch", regrouped, w_local, preferred_element_type=jnp.float32)
        + b_hidden[0]
    )
    hidden = hidden_layers(activate(pre_act), b_hidden, w_mid)
    hidden_flat = hidden.reshape(quarter_rows * PY, -1)
    tendency = lax.dot_general(
        w_rows, hidden_flat, (((1,), (1,)), ((), ())), preferred_element_type=jnp.float32
    ).astype(jnp.bfloat16)
    tendency = tendency.reshape(groups, VARS, slot, quarter_rows * PY)
    tendency_here = lax.all_to_all(tendency, "grp", split_axis=0, concat_axis=0, tiled=True)
    heating = HEAT_WEIGHT * jnp.sum(
        tendency[:, 0, 0:level_share].astype(jnp.float32), axis=(0, 1)
    ).reshape(quarter_rows, PY)
    packed = jnp.dot(
        selector_here.astype(jnp.float32), heating, precision=lax.Precision.HIGHEST
    ).reshape(patches, capacity, PY)
    owner_heating = lax.all_to_all(
        packed, "patch", split_axis=0, concat_axis=0, tiled=True
    ).reshape(slot_count, PY)
    advected = state
    for section_index in range(SUBSTEPS):
        halo = exchange_halo(payload, beside_all, patches, level_share)
        last = section_index == SUBSTEPS - 1
        advected, payload = stencil(
            advected, courant_x, courant_y, halo, tendency_here if last else None
        )
    new_state = advected
    return (new_state, owner_heating)


def solution(mesh):
    placed = (
        P(None, "grp", "patch"),
        P("grp", "patch"),
        P("grp", "patch"),
        P("grp", "patch"),
        P(),
        P(),
        P(),
        P(),
        P(),
        P(),
    )
    return jax.shard_map(
        on_device,
        mesh=mesh,
        in_specs=placed,
        out_specs=(P(None, "grp", "patch"), P("grp", "patch")),
        check_vma=False,
    )
```

```python
import functools

import jax
import numpy as np
import jax.numpy as jnp
from jax import lax
from jax.experimental import pallas as pl
from jax.experimental.pallas import tpu as pltpu
from jax.sharding import PartitionSpec as P

VARS = 9
LEV = 60
SURF = 16
SUBSTEPS = 3
PY = 128
PX = 64


KAPPA = 0.24
PHYS_DT = 0.05
HEAT_WEIGHT = 0.125


def stencil_kernel(*refs, with_tend):
    if with_tend:
        st_ref, cx_ref, cy_ref, rows_ref, tend_ref, out_ref, pay_ref, stack_ref = refs
    else:
        st_ref, cx_ref, cy_ref, rows_ref, out_ref, pay_ref, stack_ref = refs
    rows = st_ref.shape[2] // PY
    slot = stack_ref.shape[0] // rows
    levels = st_ref.shape[1]
    north = rows_ref[0, :, 0:PY].astype(jnp.float32)
    south = rows_ref[0, :, PY : 2 * PY].astype(jnp.float32)
    sides = rows_ref[0, :, 2 * PY : 3 * PY].astype(jnp.float32)
    lane = lax.broadcasted_iota(jnp.int32, north.shape, 1)
    stack_ref[...] = jnp.zeros(stack_ref.shape, stack_ref.dtype)
    for x in range(rows):
        here = slice(x * PY, (x + 1) * PY)
        cur = st_ref[0, :, here]
        up = north if x == 0 else st_ref[0, :, (x - 1) * PY : x * PY]
        down = south if x == rows - 1 else st_ref[0, :, (x + 1) * PY : (x + 2) * PY]
        side = pltpu.roll(sides, (PY - 2 * x) % PY, 1)
        west = jnp.where(lane == 0, side, pltpu.roll(cur, 1, 1))
        east = jnp.where(lane == PY - 1, side, pltpu.roll(cur, PY - 1, 1))
        along_x = cx_ref[:, here]
        along_y = cy_ref[:, here]
        val = (
            cur
            - 0.5 * along_x * (down - up)
            - 0.5 * along_y * (east - west)
            + KAPPA * (up + down + west + east - 4.0 * cur)
        )
        if with_tend:
            quarter = rows // tend_ref.shape[0]
            block = tend_ref[x // quarter, 0, 0:levels, (x % quarter) * PY : (x % quarter + 1) * PY]
            val = val + PHYS_DT * block.astype(jnp.float32)
        out_ref[0, :, here] = val
        packed = val.astype(jnp.bfloat16)
        stack_ref[x * slot : x * slot + levels, :] = packed
        if x == 0:
            pay_ref[0, 0:levels, 0:PY] = packed
        if x == rows - 1:
            pay_ref[0, 0:levels, PY : 2 * PY] = packed
    finish_payload(pay_ref, stack_ref, levels)


def finish_payload(pay_ref, stack_ref, levels):
    pad_rows = pay_ref.shape[1] - levels
    if pad_rows:
        pay_ref[0, levels:, 0 : 2 * PY] = jnp.zeros((pad_rows, 2 * PY), pay_ref.dtype)
    chunks = stack_ref.shape[0] // PY
    pick_row = lax.broadcasted_iota(jnp.int32, (2 * chunks, PY), 0)
    pick_lane = lax.broadcasted_iota(jnp.int32, (2 * chunks, PY), 1)
    cols = jnp.zeros((2 * chunks, PY), jnp.float32)
    for j in range(chunks):
        picker = (
            ((pick_row == 2 * j) & (pick_lane == 0)) | ((pick_row == 2 * j + 1) & (pick_lane == PY - 1))
        ).astype(jnp.bfloat16)
        cols = cols + lax.dot_general(
            picker,
            stack_ref[j * PY : (j + 1) * PY, :],
            (((1,), (1,)), ((), ())),
            preferred_element_type=jnp.float32,
        )
    pay_ref[0, :, 2 * PY : 3 * PY] = cols.astype(pay_ref.dtype)


def stencil(tracer, along_x, along_y, halo, tend):
    n_vars, levels, width = tracer.shape
    rows = width // PY
    slot = 16
    with_tend = tend is not None
    in_specs = [
        pl.BlockSpec((1, levels, width), lambda v: (v, 0, 0)),
        pl.BlockSpec((levels, width), lambda v: (0, 0)),
        pl.BlockSpec((levels, width), lambda v: (0, 0)),
        pl.BlockSpec((1, levels, 3 * PY), lambda v: (v, 0, 0)),
    ]
    args = [tracer, along_x, along_y, halo]
    if with_tend:
        in_specs.append(pl.BlockSpec((tend.shape[0], 1) + tend.shape[2:], lambda v: (0, v, 0, 0)))
        args.append(tend)
    return pl.pallas_call(
        functools.partial(stencil_kernel, with_tend=with_tend),
        grid=(n_vars,),
        in_specs=in_specs,
        out_specs=[
            pl.BlockSpec((1, levels, width), lambda v: (v, 0, 0)),
            pl.BlockSpec((1, slot, 3 * PY), lambda v: (v, 0, 0)),
        ],
        out_shape=[
            jax.ShapeDtypeStruct(tracer.shape, jnp.float32),
            jax.ShapeDtypeStruct((n_vars, slot, 3 * PY), jnp.bfloat16),
        ],
        scratch_shapes=[pltpu.VMEM((rows * slot, PY), jnp.bfloat16)],
        cost_estimate=pl.CostEstimate(
            flops=20 * tracer.size, transcendentals=0, bytes_accessed=4 * (2 * tracer.size + 2 * along_x.size)
        ),
    )(*args)


def pack_kernel(st_ref, surf_ref, pay_ref, feat_ref, stack_ref, *, n_surf):
    rows = st_ref.shape[2] // PY
    slot = stack_ref.shape[0] // rows
    levels = st_ref.shape[1]
    stack_ref[...] = jnp.zeros(stack_ref.shape, stack_ref.dtype)
    for x in range(rows):
        here = slice(x * PY, (x + 1) * PY)
        packed = st_ref[0, :, here].astype(jnp.bfloat16)
        stack_ref[x * slot : x * slot + levels, :] = packed
        feat_ref[x, 0, 0:levels, :] = packed
        surf_all = surf_ref[:, here].astype(jnp.float32)
        pick = lax.broadcasted_iota(jnp.int32, surf_all.shape, 0) == pl.program_id(0)
        surf_row = jnp.sum(jnp.where(pick, surf_all, 0.0), axis=0, keepdims=True)
        feat_ref[x, 0, levels : levels + 1, :] = surf_row.astype(feat_ref.dtype)
        if x == 0:
            pay_ref[0, 0:levels, 0:PY] = packed
        if x == rows - 1:
            pay_ref[0, 0:levels, PY : 2 * PY] = packed
    finish_payload(pay_ref, stack_ref, levels)


def first_edges(tracer, surface):
    n_vars, levels, width = tracer.shape
    n_surf = surface.shape[0]
    rows = width // PY
    slot = 16
    return pl.pallas_call(
        functools.partial(pack_kernel, n_surf=n_surf),
        grid=(n_vars,),
        in_specs=[
            pl.BlockSpec((1, levels, width), lambda v: (v, 0, 0)),
            pl.BlockSpec((n_surf, width), lambda v: (0, 0)),
        ],
        out_specs=[
            pl.BlockSpec((1, slot, 3 * PY), lambda v: (v, 0, 0)),
            pl.BlockSpec((rows, 1, slot, PY), lambda v: (0, v, 0, 0)),
        ],
        out_shape=[
            jax.ShapeDtypeStruct((n_vars, slot, 3 * PY), jnp.bfloat16),
            jax.ShapeDtypeStruct((rows, n_vars, slot, PY), jnp.bfloat16),
        ],
        scratch_shapes=[pltpu.VMEM((rows * slot, PY), jnp.bfloat16)],
        cost_estimate=pl.CostEstimate(flops=0, transcendentals=0, bytes_accessed=5 * tracer.size),
    )(tracer, surface)


def exchange_halo(payload, beside_all, patches, levels):
    n_vars, slot, _ = payload.shape
    rows = PX
    chunk_rows = PY // slot
    got = lax.all_gather(payload, "patch", axis=0, tiled=False)
    north = jnp.take(got, beside_all[0], axis=0)[:, 0:levels, PY : 2 * PY]
    south = jnp.take(got, beside_all[1], axis=0)[:, 0:levels, 0:PY]

    def column(patch, which):
        cols = jnp.take(got, patch, axis=0)[..., 2 * PY : 3 * PY]
        cols = cols.reshape(n_vars, rows // chunk_rows, 2, chunk_rows, slot)[:, :, which]
        return cols.transpose(0, 3, 1, 2).reshape(n_vars, slot, rows)[:, 0:levels]

    west = column(beside_all[2], 1)
    east = column(beside_all[3], 0)
    sides = jnp.stack([west, jnp.roll(east, -1, axis=-1)], axis=-1).reshape(west.shape[:-1] + (2 * rows,))
    return jnp.concatenate([north, south, sides], axis=-1)


def activate(pre_act):
    return jax.nn.silu(pre_act).astype(jnp.bfloat16)


def hidden_layers(hidden, b_hidden, w_mid):
    for layer_index in range(w_mid.shape[0]):
        pre_act = (
            jnp.einsum(
                "...h,hj->...j", hidden, w_mid[layer_index], preferred_element_type=jnp.float32
            )
            + b_hidden[layer_index + 1]
        )
        hidden = activate(pre_act)
    return hidden


def on_device(
    state, courant_x, courant_y, surface, w_in, b_hidden, w_mid, w_out, owner_map, neighbours
):
    groups = lax.axis_size("grp")
    patches = lax.axis_size("patch")
    group_here = lax.axis_index("grp")
    patch_here = lax.axis_index("patch")
    level_share = LEV // groups
    surf_share = SURF // groups
    feat_share = VARS * level_share + surf_share
    quarter_rows = PX // groups
    capacity = max(2, 2 * quarter_rows // patches)
    slot_count = patches * capacity
    slot = 16
    beside_all = jnp.take(neighbours, patch_here, axis=0)
    owners_all = owner_map.reshape(patches, groups, quarter_rows)
    owners_here = jnp.take(jnp.take(owners_all, patch_here, axis=0), group_here, axis=0)
    matches = (owners_here[:, None] == jnp.arange(patches, dtype=jnp.int32)).astype(jnp.int32)
    slot_rank = jnp.sum((jnp.cumsum(matches, axis=0) - matches) * matches, axis=1)
    slot_index = owners_here * capacity + slot_rank
    selector_here = (
        slot_index[None, :] == jnp.arange(slot_count, dtype=jnp.int32)[:, None]
    ).astype(jnp.bfloat16)
    order = np.full((groups, VARS, slot), w_in.shape[0], np.int32)
    for q in range(groups):
        for v in range(VARS):
            order[q, v, :level_share] = v * LEV + q * level_share + np.arange(level_share)
            if v < surf_share:
                order[q, v, level_share] = VARS * LEV + q * surf_share + v
    w_padded = jnp.concatenate([w_in, jnp.zeros((1, w_in.shape[1]), w_in.dtype)], axis=0)
    w_local = jnp.take(w_padded, jnp.asarray(order.reshape(-1)), axis=0).reshape(groups, VARS * slot, -1)
    w_split = w_out.reshape(-1, VARS, groups, level_share)
    w_pad = jnp.pad(w_split, ((0, 0), (0, 0), (0, 0), (0, slot - level_share)))
    w_rows = w_pad.transpose(2, 1, 3, 0).reshape(groups * VARS * slot, -1)
    w_local, w_rows, selector_here, beside_all, state_in = lax.optimization_barrier(
        (w_local, w_rows, selector_here, beside_all, state)
    )
    payload, feat = first_edges(state_in, surface)
    by_quarter = feat.reshape(groups, quarter_rows, VARS * slot, PY)
    regrouped = lax.all_to_all(by_quarter, "grp", split_axis=0, concat_axis=0, tiled=True)
    pre_act = (
        jnp.einsum("gbfc,gfh->bch", regrouped, w_local, preferred_element_type=jnp.float32)
        + b_hidden[0]
    )
    hidden = hidden_layers(activate(pre_act), b_hidden, w_mid)
    hidden_flat = hidden.reshape(quarter_rows * PY, -1)
    tendency = lax.dot_general(
        w_rows, hidden_flat, (((1,), (1,)), ((), ())), preferred_element_type=jnp.float32
    ).astype(jnp.bfloat16)
    tendency = tendency.reshape(groups, VARS, slot, quarter_rows * PY)
    tendency_here = lax.all_to_all(tendency, "grp", split_axis=0, concat_axis=0, tiled=True)
    heating = HEAT_WEIGHT * jnp.sum(
        tendency[:, 0, 0:level_share].astype(jnp.float32), axis=(0, 1)
    ).reshape(quarter_rows, PY)
    packed = jnp.dot(
        selector_here.astype(jnp.float32), heating, precision=lax.Precision.HIGHEST
    ).reshape(patches, capacity, PY)
    owner_heating = lax.all_to_all(
        packed, "patch", split_axis=0, concat_axis=0, tiled=True
    ).reshape(slot_count, PY)
    advected = state
    for section_index in range(SUBSTEPS):
        halo = exchange_halo(payload, beside_all, patches, level_share)
        last = section_index == SUBSTEPS - 1
        advected, payload = stencil(
            advected, courant_x, courant_y, halo, tendency_here if last else None
        )
    new_state = advected
    return (new_state, owner_heating)


def solution(mesh):
    placed = (
        P(None, "grp", "patch"),
        P("grp", "patch"),
        P("grp", "patch"),
        P("grp", "patch"),
        P(),
        P(),
        P(),
        P(),
        P(),
        P(),
    )
    return jax.shard_map(
        on_device,
        mesh=mesh,
        in_specs=placed,
        out_specs=(P(None, "grp", "patch"), P("grp", "patch")),
        check_vma=False,
    )
```

```python
import functools

import jax
import jax.numpy as jnp
from jax import lax
from jax.experimental import pallas as pl
from jax.experimental.pallas import tpu as pltpu
from jax.sharding import PartitionSpec as P

VARS = 9
LEV = 60
SURF = 16
SUBSTEPS = 3
PY = 128
PX = 64


KAPPA = 0.24
PHYS_DT = 0.05
HEAT_WEIGHT = 0.125


def stencil_kernel(*refs, with_tend):
    if with_tend:
        st_ref, cx_ref, cy_ref, rows_ref, sides_ref, tend_ref, out_ref, pay_ref, stack_ref = refs
    else:
        st_ref, cx_ref, cy_ref, rows_ref, sides_ref, out_ref, pay_ref, stack_ref = refs
    rows = st_ref.shape[2] // PY
    slot = stack_ref.shape[0] // rows
    levels = st_ref.shape[1]
    north = rows_ref[0, :, 0:PY].astype(jnp.float32)
    south = rows_ref[0, :, PY : 2 * PY].astype(jnp.float32)
    sides = sides_ref[0].astype(jnp.float32)
    lane = lax.broadcasted_iota(jnp.int32, north.shape, 1)
    stack_ref[...] = jnp.zeros(stack_ref.shape, stack_ref.dtype)
    for x in range(rows):
        here = slice(x * PY, (x + 1) * PY)
        cur = st_ref[0, :, here]
        up = north if x == 0 else st_ref[0, :, (x - 1) * PY : x * PY]
        down = south if x == rows - 1 else st_ref[0, :, (x + 1) * PY : (x + 2) * PY]
        side = pltpu.roll(sides, (PY - 2 * x) % PY, 1)
        west = jnp.where(lane == 0, side, pltpu.roll(cur, 1, 1))
        east = jnp.where(lane == PY - 1, side, pltpu.roll(cur, PY - 1, 1))
        along_x = cx_ref[:, here]
        along_y = cy_ref[:, here]
        val = (
            cur
            - 0.5 * along_x * (down - up)
            - 0.5 * along_y * (east - west)
            + KAPPA * (up + down + west + east - 4.0 * cur)
        )
        if with_tend:
            quarter = rows // tend_ref.shape[0]
            block = tend_ref[x // quarter, 0, 0:levels, (x % quarter) * PY : (x % quarter + 1) * PY]
            val = val + PHYS_DT * block.astype(jnp.float32)
        out_ref[0, :, here] = val
        packed = val.astype(jnp.bfloat16)
        stack_ref[x * slot : x * slot + levels, :] = packed
        if x == 0:
            pay_ref[0, 0:levels, 0:PY] = packed
        if x == rows - 1:
            pay_ref[0, 0:levels, PY : 2 * PY] = packed
    finish_payload(pay_ref, stack_ref, levels)


def finish_payload(pay_ref, stack_ref, levels):
    pad_rows = pay_ref.shape[1] - levels
    if pad_rows:
        pay_ref[0, levels:, 0 : 2 * PY] = jnp.zeros((pad_rows, 2 * PY), pay_ref.dtype)
    chunks = stack_ref.shape[0] // PY
    pick_row = lax.broadcasted_iota(jnp.int32, (2 * chunks, PY), 0)
    pick_lane = lax.broadcasted_iota(jnp.int32, (2 * chunks, PY), 1)
    cols = jnp.zeros((2 * chunks, PY), jnp.float32)
    for j in range(chunks):
        picker = (
            ((pick_row == 2 * j) & (pick_lane == 0)) | ((pick_row == 2 * j + 1) & (pick_lane == PY - 1))
        ).astype(jnp.bfloat16)
        cols = cols + lax.dot_general(
            picker,
            stack_ref[j * PY : (j + 1) * PY, :],
            (((1,), (1,)), ((), ())),
            preferred_element_type=jnp.float32,
        )
    pay_ref[0, :, 2 * PY : 3 * PY] = cols.astype(pay_ref.dtype)


def stencil(tracer, along_x, along_y, halo, tend):
    n_vars, levels, width = tracer.shape
    rows = width // PY
    slot = 16
    with_tend = tend is not None
    in_specs = [
        pl.BlockSpec((1, levels, width), lambda v: (v, 0, 0)),
        pl.BlockSpec((levels, width), lambda v: (0, 0)),
        pl.BlockSpec((levels, width), lambda v: (0, 0)),
        pl.BlockSpec((1, levels, 2 * PY), lambda v: (v, 0, 0)),
        pl.BlockSpec((1, levels, PY), lambda v: (v, 0, 0)),
    ]
    args = [tracer, along_x, along_y, halo[0], halo[1]]
    if with_tend:
        in_specs.append(pl.BlockSpec((tend.shape[0], 1) + tend.shape[2:], lambda v: (0, v, 0, 0)))
        args.append(tend)
    return pl.pallas_call(
        functools.partial(stencil_kernel, with_tend=with_tend),
        grid=(n_vars,),
        in_specs=in_specs,
        out_specs=[
            pl.BlockSpec((1, levels, width), lambda v: (v, 0, 0)),
            pl.BlockSpec((1, slot, 3 * PY), lambda v: (v, 0, 0)),
        ],
        out_shape=[
            jax.ShapeDtypeStruct(tracer.shape, jnp.float32),
            jax.ShapeDtypeStruct((n_vars, slot, 3 * PY), jnp.bfloat16),
        ],
        scratch_shapes=[pltpu.VMEM((rows * slot, PY), jnp.bfloat16)],
        cost_estimate=pl.CostEstimate(
            flops=20 * tracer.size, transcendentals=0, bytes_accessed=4 * (2 * tracer.size + 2 * along_x.size)
        ),
    )(*args)


def pack_kernel(st_ref, surf_ref, pay_ref, feat_ref, stack_ref, *, n_surf):
    rows = st_ref.shape[2] // PY
    slot = stack_ref.shape[0] // rows
    levels = st_ref.shape[1]
    stack_ref[...] = jnp.zeros(stack_ref.shape, stack_ref.dtype)
    for x in range(rows):
        here = slice(x * PY, (x + 1) * PY)
        packed = st_ref[0, :, here].astype(jnp.bfloat16)
        stack_ref[x * slot : x * slot + levels, :] = packed
        feat_ref[x, 0, 0:levels, :] = packed
        surf_all = surf_ref[:, here].astype(jnp.float32)
        pick = lax.broadcasted_iota(jnp.int32, surf_all.shape, 0) == pl.program_id(0)
        surf_row = jnp.sum(jnp.where(pick, surf_all, 0.0), axis=0, keepdims=True)
        feat_ref[x, 0, levels : levels + 1, :] = surf_row.astype(feat_ref.dtype)
        if x == 0:
            pay_ref[0, 0:levels, 0:PY] = packed
        if x == rows - 1:
            pay_ref[0, 0:levels, PY : 2 * PY] = packed
    finish_payload(pay_ref, stack_ref, levels)


def first_edges(tracer, surface):
    n_vars, levels, width = tracer.shape
    n_surf = surface.shape[0]
    rows = width // PY
    slot = 16
    return pl.pallas_call(
        functools.partial(pack_kernel, n_surf=n_surf),
        grid=(n_vars,),
        in_specs=[
            pl.BlockSpec((1, levels, width), lambda v: (v, 0, 0)),
            pl.BlockSpec((n_surf, width), lambda v: (0, 0)),
        ],
        out_specs=[
            pl.BlockSpec((1, slot, 3 * PY), lambda v: (v, 0, 0)),
            pl.BlockSpec((rows, 1, slot, PY), lambda v: (0, v, 0, 0)),
        ],
        out_shape=[
            jax.ShapeDtypeStruct((n_vars, slot, 3 * PY), jnp.bfloat16),
            jax.ShapeDtypeStruct((rows, n_vars, slot, PY), jnp.bfloat16),
        ],
        scratch_shapes=[pltpu.VMEM((rows * slot, PY), jnp.bfloat16)],
        cost_estimate=pl.CostEstimate(flops=0, transcendentals=0, bytes_accessed=5 * tracer.size),
    )(tracer, surface)


def exchange_halo(payload, beside_all, patches, levels):
    n_vars, slot, _ = payload.shape
    rows = PX
    chunk_rows = PY // slot
    got = lax.all_gather(payload, "patch", axis=0, tiled=False)
    north = jnp.take(got, beside_all[0], axis=0)[:, 0:levels, PY : 2 * PY]
    south = jnp.take(got, beside_all[1], axis=0)[:, 0:levels, 0:PY]

    def column(patch, which):
        cols = jnp.take(got, patch, axis=0)[..., 2 * PY : 3 * PY]
        cols = cols.reshape(n_vars, rows // chunk_rows, 2, chunk_rows, slot)[:, :, which]
        return cols.transpose(0, 3, 1, 2).reshape(n_vars, slot, rows)[:, 0:levels]

    west = column(beside_all[2], 1)
    east = column(beside_all[3], 0)
    sides = jnp.stack([west, jnp.roll(east, -1, axis=-1)], axis=-1).reshape(west.shape[:-1] + (2 * rows,))
    return (jnp.concatenate([north, south], axis=-1), sides)


def activate(pre_act):
    return jax.nn.silu(pre_act).astype(jnp.bfloat16)


def hidden_layers(hidden, b_hidden, w_mid):
    for layer_index in range(w_mid.shape[0]):
        pre_act = (
            jnp.einsum(
                "...h,hj->...j", hidden, w_mid[layer_index], preferred_element_type=jnp.float32
            )
            + b_hidden[layer_index + 1]
        )
        hidden = activate(pre_act)
    return hidden


def on_device(
    state, courant_x, courant_y, surface, w_in, b_hidden, w_mid, w_out, owner_map, neighbours
):
    groups = lax.axis_size("grp")
    patches = lax.axis_size("patch")
    group_here = lax.axis_index("grp")
    patch_here = lax.axis_index("patch")
    level_share = LEV // groups
    surf_share = SURF // groups
    feat_share = VARS * level_share + surf_share
    quarter_rows = PX // groups
    capacity = max(2, 2 * quarter_rows // patches)
    slot_count = patches * capacity
    slot = 16
    beside_all = jnp.take(neighbours, patch_here, axis=0)
    owners_all = owner_map.reshape(patches, groups, quarter_rows)
    owners_here = jnp.take(jnp.take(owners_all, patch_here, axis=0), group_here, axis=0)
    matches = (owners_here[:, None] == jnp.arange(patches, dtype=jnp.int32)).astype(jnp.int32)
    slot_rank = jnp.sum((jnp.cumsum(matches, axis=0) - matches) * matches, axis=1)
    slot_index = owners_here * capacity + slot_rank
    selector_here = (
        slot_index[None, :] == jnp.arange(slot_count, dtype=jnp.int32)[:, None]
    ).astype(jnp.bfloat16)
    state_part = w_in[: VARS * LEV].reshape(VARS, groups, level_share, -1).transpose(1, 0, 2, 3)
    surf_part = w_in[VARS * LEV :].reshape(groups, surf_share, 1, -1)
    surf_part = jnp.pad(surf_part, ((0, 0), (0, VARS - surf_share), (0, 0), (0, 0)))
    pad_part = jnp.zeros(state_part.shape[:2] + (slot - level_share - 1, state_part.shape[3]), w_in.dtype)
    w_local = jnp.concatenate([state_part, surf_part, pad_part], axis=2).reshape(groups, VARS * slot, -1)
    w_split = w_out.reshape(-1, VARS, groups, level_share)
    w_pad = jnp.pad(w_split, ((0, 0), (0, 0), (0, 0), (0, slot - level_share)))
    w_rows = w_pad.transpose(2, 1, 3, 0).reshape(groups * VARS * slot, -1)
    w_local, w_rows, selector_here, beside_all, state_in = lax.optimization_barrier(
        (w_local, w_rows, selector_here, beside_all, state)
    )
    payload, feat = first_edges(state_in, surface)
    by_quarter = feat.reshape(groups, quarter_rows, VARS * slot, PY)
    regrouped = lax.all_to_all(by_quarter, "grp", split_axis=0, concat_axis=0, tiled=True)
    pre_act = (
        jnp.einsum("gbfc,gfh->bch", regrouped, w_local, preferred_element_type=jnp.float32)
        + b_hidden[0]
    )
    hidden = hidden_layers(activate(pre_act), b_hidden, w_mid)
    hidden_flat = hidden.reshape(quarter_rows * PY, -1)
    tendency = lax.dot_general(
        w_rows, hidden_flat, (((1,), (1,)), ((), ())), preferred_element_type=jnp.float32
    ).astype(jnp.bfloat16)
    tendency = tendency.reshape(groups, VARS, slot, quarter_rows * PY)
    tendency_here = lax.all_to_all(tendency, "grp", split_axis=0, concat_axis=0, tiled=True)
    heating = HEAT_WEIGHT * jnp.sum(
        tendency[:, 0, 0:level_share].astype(jnp.float32), axis=(0, 1)
    ).reshape(quarter_rows, PY)
    packed = jnp.dot(
        selector_here.astype(jnp.float32), heating, precision=lax.Precision.HIGHEST
    ).reshape(patches, capacity, PY)
    owner_heating = lax.all_to_all(
        packed, "patch", split_axis=0, concat_axis=0, tiled=True
    ).reshape(slot_count, PY)
    advected = state
    for section_index in range(SUBSTEPS):
        halo = exchange_halo(payload, beside_all, patches, level_share)
        last = section_index == SUBSTEPS - 1
        advected, payload = stencil(
            advected, courant_x, courant_y, halo, tendency_here if last else None
        )
    new_state = advected
    return (new_state, owner_heating)


def solution(mesh):
    placed = (
        P(None, "grp", "patch"),
        P("grp", "patch"),
        P("grp", "patch"),
        P("grp", "patch"),
        P(),
        P(),
        P(),
        P(),
        P(),
        P(),
    )
    return jax.shard_map(
        on_device,
        mesh=mesh,
        in_specs=placed,
        out_specs=(P(None, "grp", "patch"), P("grp", "patch")),
        check_vma=False,
    )
```
